32 devices in a mesh: tile: 8 (over z, y), win: 4 (over x, core).
Axes of the slice: x: 2, y: 2, z: 4, core: 2. Of those that a mesh axis runs over, the one named last changes fastest.
Arguments:
- records: bfloat16 [16, 2048, 2048], P('win', 'tile'), may hold values from -6 to 6
- pair_first: int32 [2048], P('tile'), may hold values from 0 to 255
- pair_offset: int32 [2048], P('tile'), may hold values from 1 to 255
- owners: int32 [2048, 1], P('tile'), may hold values from 0 to 7; in each aligned block of 256 rows (0 to 255, 256 to 511, ...) at most 80 rows name the same one
Outputs:
- gathers: bfloat16 [8, 8, 80, 2048], P('tile', None, None, 'win')
The draws below stay inside these ranges and needn't reach their ends.
Inputs may be any that keep to these rules, and one draw needn't show every extreme that they name: `owners`: among the 256 pairs of one tile no owner is named more than 80 times, and in every draw some tile names some owner exactly 80 times.
All inputs are finite; a program needn't handle non-finite values.
Results may differ from the reference program's by a relative error of at most 0.0066.
Values may be sent and summed in bfloat16 or wider, within the bound.
No kernel may reach another device: no remote copies, remote signals or barrier semaphores. Data moves between devices by JAX's collectives and lax.ppermute only.
A program may use at most 128 MiB of HBM per device.

```python
import math
import jax
import jax.numpy as jnp
import numpy as np
from jax import lax

NF = 2048
BAND = 64
CH_DEV = 256
P_DEV = 256
CH = 2048
SEGS = 16
PAIRS = 2048
CAP = 80
N_TILE = 8


def plant(array, own_key, low, largest):
    extent = array.shape
    spot = [jax.random.randint(jax.random.fold_in(own_key, axis), (), 0, extent[axis]) for axis in range(len(extent))]
    array = array.at[tuple(spot)].set(low)
    longest = extent.index(max(extent))
    spot[longest] = (spot[longest] + 1) % extent[longest]
    return array.at[tuple(spot)].set(largest)


def steps_of(own_key, extent, cuts, smallest, largest):
    level, own = 1.0, jax.random.fold_in(own_key, 6)
    for dim, shards_of in cuts:
        heights = jnp.exp(jax.random.uniform(jax.random.fold_in(own, dim), (shards_of,), jnp.float32, smallest / len(cuts), largest / len(cuts)))
        level = level * jnp.repeat(heights, extent[dim] // shards_of).reshape([-1 if axis == dim else 1 for axis in range(len(extent))])
    return level


def shared_out(own_key, own, number, rows, number_of, top, most, slope):
    ranking = jax.random.permutation(own_key, number_of)
    heavy_load, ordinary = portions_of(number_of, rows * top, most, slope, True), portions_of(number_of, rows * top, most, slope, False)
    places = jnp.arange(number_of)

    def named(tallies, turn):
        used = int((tallies > 0).sum())
        fixed = max(1, used // 4)
        moved = fixed + (places - fixed + turn * (used - fixed)) % max(1, number_of - fixed)
        return jnp.zeros((number_of,), jnp.int32).at[ranking[jnp.where(places < fixed, places, moved)]].set(jnp.asarray(tallies, jnp.int32))

    tallies = jnp.where(number % 4 == 0, named(heavy_load, number // 4), named(ordinary, number - number // 4 - 1))
    mixed = jax.random.permutation(jax.random.fold_in(own, 3), number_of)
    source_of, taker = mixed[0:number_of // 2 * 2:2], mixed[1:number_of // 2 * 2:2]
    margin = jnp.minimum(tallies[source_of] - 1, most - tallies[taker]) // 2
    margin = jnp.where((source_of == ranking[0]) | (taker == ranking[0]) | (tallies[taker] == 0), 0, jnp.maximum(margin, 0))
    moved = jax.random.randint(jax.random.fold_in(own, 4), (number_of // 2,), 0, 1 << 20) % (margin + 1)
    tallies = tallies.at[source_of].add(-moved).at[taker].add(moved)
    members = jnp.searchsorted(jnp.cumsum(tallies), jnp.arange(rows * top), side="right").astype(jnp.int32)
    table = members.reshape(top, rows).T
    table = table[jax.random.permutation(jax.random.fold_in(own, 1), rows)]
    turn = jax.random.randint(jax.random.fold_in(own, 2), (rows, 1), 0, top)
    return jnp.take_along_axis(table, (jnp.arange(top)[None, :] + turn) % top, axis=1)


def portions_of(count, total, reach, slope, full):
    weights = [(1 << 20) // math.isqrt(rank ** slope) + 1 for rank in range(1, count + 1)]
    largest = reach if full else min(reach, max(-(-total // count), total * weights[0] // sum(weights)))
    least = 1 if total - largest >= count - 1 else 0
    given, spare = [largest] + [least] * (count - 1), total - largest - least * (count - 1)
    while spare > 0:
        candidates = [i for i in range(1, count) if given[i] < largest] or [i for i in range(1, count) if given[i] < reach]
        mass, left = sum([weights[i] for i in candidates]), spare
        for i in candidates:
            addition = min(reach - given[i], max(1, left * weights[i] // mass), spare)
            given[i] = given[i] + addition
            spare = spare - addition
    return np.array(given)


def normal_values(stream_key, shape, deviation, limit, cuts=(), kind=jnp.bfloat16):
    entries = jax.random.normal(stream_key, shape, jnp.float32) * deviation
    if len(cuts) > 0:
        entries = steps_of(stream_key, shape, cuts, -0.22, 0.18) * entries
    return jnp.clip(entries, min=-limit, max=limit).astype(kind)


def setup_inputs(seed: int = 0) -> dict:
    seeds = jax.random.split(jax.random.key(seed), 5)
    records = normal_values(seeds[0], (SEGS, NF, CH), 1.0, 6.0, ((0, 4), (1, 8)))
    pair_first = plant(jax.random.randint(seeds[1], (PAIRS,), 0, CH_DEV), jax.random.fold_in(seeds[1], 1), 0, CH_DEV - 1).astype(jnp.int32)
    pair_offset = plant(jax.random.randint(seeds[2], (PAIRS,), 1, CH_DEV), jax.random.fold_in(seeds[2], 1), 1, CH_DEV - 1).astype(jnp.int32)
    owners_keys = jax.random.split(jax.random.fold_in(seeds[3], 1), PAIRS // P_DEV)
    owners_turns = jax.random.permutation(jax.random.fold_in(seeds[3], 3), PAIRS // P_DEV)
    owners = jax.vmap(lambda own, number: shared_out(jax.random.fold_in(seeds[3], 2), own, number, P_DEV, N_TILE, 1, CAP, 2))(owners_keys, owners_turns).reshape((PAIRS, 1))
    return {"records": records, "pair_first": pair_first, "pair_offset": pair_offset, "owners": owners}


power_floor = 1e-06

def forward_matrix(length):
    row_index = lax.broadcasted_iota(jnp.int32, (length // 2, length), 0)
    col_index = lax.broadcasted_iota(jnp.int32, (length // 2, length), 1)
    phases = row_index * col_index % length
    angles = phases.astype(jnp.float32) * (2.0 * math.pi / length)
    return jnp.concatenate([jnp.cos(angles), -jnp.sin(angles)], axis=0).astype(jnp.bfloat16)

def inverse_matrix(length, first_lag, lag_count, seg_total):
    half_bins = length // 2
    lag_index = lax.broadcasted_iota(jnp.int32, (lag_count, half_bins), 0) + first_lag
    bin_index = lax.broadcasted_iota(jnp.int32, (lag_count, half_bins), 1)
    phases = lag_index * bin_index % length
    angles = phases.astype(jnp.float32) * (2.0 * math.pi / length)
    weights = jnp.where(bin_index == 0, 1.0, 2.0).astype(jnp.float32) * (1.0 / math.sqrt(half_bins * seg_total))
    return jnp.concatenate([weights * jnp.cos(angles), -weights * jnp.sin(angles)], axis=1)

def whiten(spectra, band_width):
    half_bins = spectra.shape[-2] // 2
    real_rows = spectra[..., :half_bins, :]
    imaginary = spectra[..., half_bins:, :]
    energy = real_rows * real_rows + imaginary * imaginary
    grouped = energy.shape[:-2] + (half_bins // band_width, band_width, energy.shape[-1])
    band_power = lax.optimization_barrier(jnp.mean(energy.reshape(grouped), axis=-2, keepdims=True))
    inverse_rms = jnp.broadcast_to(lax.rsqrt(band_power + power_floor), grouped).reshape(energy.shape)
    return (spectra * jnp.concatenate([inverse_rms, inverse_rms], axis=-2)).astype(jnp.bfloat16)

def cross_terms(first_part, second_part):
    half_bins = first_part.shape[-2] // 2
    first_real = first_part[..., :half_bins, :].astype(jnp.float32)
    first_imag = first_part[..., half_bins:, :].astype(jnp.float32)
    second_real = second_part[..., :half_bins, :].astype(jnp.float32)
    second_imag = second_part[..., half_bins:, :].astype(jnp.float32)
    real_sum = first_real * second_real + first_imag * second_imag
    imag_sum = first_imag * second_real - first_real * second_imag
    return jnp.concatenate([real_sum, imag_sum], axis=-2)

def bucket_select(owner_ids, owner_count, capacity):
    onehot = (owner_ids[:, None] == jnp.arange(owner_count, dtype=jnp.int32)[None, :]).astype(jnp.int32)
    slot_rank = lax.optimization_barrier(jnp.sum((jnp.cumsum(onehot, axis=0, dtype=jnp.int32) - 1) * onehot, axis=1))
    slot_id = owner_ids * capacity + slot_rank
    return (slot_id[None, :] == jnp.arange(owner_count * capacity, dtype=jnp.int32)[:, None]).astype(jnp.bfloat16)

def reference(records, pair_first, pair_offset, owners):
    forward = forward_matrix(NF)

    def per_segment(segment):
        return whiten(jnp.dot(forward, segment, preferred_element_type=jnp.float32), BAND)
    whitened = lax.map(per_segment, records)
    pair_tile = jnp.arange(PAIRS, dtype=jnp.int32) // P_DEV
    first_channel = pair_tile * CH_DEV + pair_first
    second_channel = (first_channel + pair_offset) % CH

    def accumulate(stacked, segment):
        first_part = jnp.take(segment, first_channel, axis=1)
        second_part = jnp.take(segment, second_channel, axis=1)
        return (stacked + cross_terms(first_part, second_part), None)
    cross = lax.scan(accumulate, jnp.zeros((NF, PAIRS), jnp.float32), whitened)[0]
    inverse = inverse_matrix(NF, 0, NF, SEGS)
    correlation = jnp.dot(inverse, cross, precision=lax.Precision.HIGHEST).astype(jnp.bfloat16)
    lag_tiles = jnp.transpose(correlation.reshape(NF, N_TILE, P_DEV), (1, 0, 2))
    owner_tiles = owners[:, 0].reshape(N_TILE, P_DEV)

    def per_tile(tile_item):
        tile_lags, tile_owners = tile_item
        chooser = bucket_select(tile_owners, N_TILE, CAP)
        picked = lax.dot_general(chooser, tile_lags, (((1,), (1,)), ((), ())), preferred_element_type=jnp.float32)
        return picked.astype(jnp.bfloat16).reshape(N_TILE, CAP, NF)
    stacked = lax.map(per_tile, (lag_tiles, owner_tiles))
    return jnp.transpose(stacked, (1, 0, 2, 3))
```

```python
import math

import jax
import jax.numpy as jnp
from jax import lax
from jax.sharding import PartitionSpec as P

BAND = 64


power_floor = 1e-06


def passed_along(block, axis, distance):
    devices = range(lax.axis_size(axis))
    route = [((i - distance) % len(devices), i) for i in devices]
    return lax.ppermute(block, axis, route)


def phase_table(rows, col_count, length):
    split = 64 if col_count % 64 == 0 else 1
    coarse = jnp.arange(col_count // split, dtype=jnp.int32) * split
    fine = jnp.arange(split, dtype=jnp.int32)
    scale = 2.0 * math.pi / length
    coarse_angle = ((rows[:, None] * coarse[None, :]) % length).astype(jnp.float32) * scale
    fine_angle = ((rows[:, None] * fine[None, :]) % length).astype(jnp.float32) * scale
    c_hi, s_hi = jnp.cos(coarse_angle)[:, :, None], jnp.sin(coarse_angle)[:, :, None]
    c_lo, s_lo = jnp.cos(fine_angle)[:, None, :], jnp.sin(fine_angle)[:, None, :]
    shape = (rows.shape[0], col_count)
    cosine = (c_hi * c_lo - s_hi * s_lo).reshape(shape)
    sine = (s_hi * c_lo + c_hi * s_lo).reshape(shape)
    return cosine, sine


def forward_matrix(length):
    cosine, sine = phase_table(jnp.arange(length // 2, dtype=jnp.int32), length, length)
    return jnp.concatenate([cosine, -sine], axis=0).astype(jnp.bfloat16)


def inverse_matrix(length, first_lag, lag_count, seg_total):
    half_bins = length // 2
    lags = jnp.arange(lag_count, dtype=jnp.int32) + first_lag
    cosine, sine = phase_table(lags, half_bins, length)
    bin_index = jnp.arange(half_bins)[None, :]
    weights = jnp.where(bin_index == 0, 1.0, 2.0).astype(jnp.float32) * (
        1.0 / math.sqrt(half_bins * seg_total)
    )
    return jnp.concatenate([weights * cosine, -weights * sine], axis=1)


def whiten(spectra, band_width):
    half_bins = spectra.shape[-2] // 2
    real_rows = spectra[..., :half_bins, :]
    imaginary = spectra[..., half_bins:, :]
    energy = real_rows * real_rows + imaginary * imaginary
    grouped = energy.shape[:-2] + (half_bins // band_width, band_width, energy.shape[-1])
    band_power = jnp.mean(energy.reshape(grouped), axis=-2, keepdims=True)
    inverse_rms = jnp.broadcast_to(lax.rsqrt(band_power + power_floor), grouped).reshape(
        energy.shape
    )
    return (spectra * jnp.concatenate([inverse_rms, inverse_rms], axis=-2)).astype(jnp.bfloat16)


def cross_terms(first_part, second_part):
    half_bins = first_part.shape[-2] // 2
    first_real = first_part[..., :half_bins, :].astype(jnp.float32)
    first_imag = first_part[..., half_bins:, :].astype(jnp.float32)
    second_real = second_part[..., :half_bins, :].astype(jnp.float32)
    second_imag = second_part[..., half_bins:, :].astype(jnp.float32)
    real_sum = first_real * second_real + first_imag * second_imag
    imag_sum = first_imag * second_real - first_real * second_imag
    return jnp.concatenate([real_sum, imag_sum], axis=-2)


def bucket_select(owner_ids, owner_count, capacity):
    onehot = (owner_ids[:, None] == jnp.arange(owner_count, dtype=jnp.int32)[None, :]).astype(
        jnp.int32
    )
    slot_rank = jnp.sum((jnp.cumsum(onehot, axis=0, dtype=jnp.int32) - 1) * onehot, axis=1)
    slot_id = owner_ids * capacity + slot_rank
    return (
        slot_id[None, :] == jnp.arange(owner_count * capacity, dtype=jnp.int32)[:, None]
    ).astype(jnp.bfloat16)


def per_device(records, pair_first, pair_offset, owners):
    tile_count = lax.axis_size("tile")
    win_count = lax.axis_size("win")
    length = records.shape[1] * tile_count
    seg_total = records.shape[0] * win_count
    forward = forward_matrix(length)
    spectra = jnp.einsum(
        "fn,snc->sfc",
        forward,
        lax.all_to_all(records, "tile", split_axis=2, concat_axis=1, tiled=True),
        preferred_element_type=jnp.float32,
    )
    whitened = whiten(spectra, BAND)
    following = passed_along(whitened, "tile", -1)
    joined = jnp.concatenate([whitened, following], axis=2)
    channel_ids = jnp.arange(joined.shape[2], dtype=jnp.int32)[:, None]
    pick_first = (channel_ids == pair_first[None, :]).astype(jnp.bfloat16)
    pick_second = (channel_ids == (pair_first + pair_offset)[None, :]).astype(jnp.bfloat16)
    first_part = jnp.einsum("sfc,cp->sfp", joined, pick_first, preferred_element_type=jnp.float32)
    second_part = jnp.einsum("sfc,cp->sfp", joined, pick_second, preferred_element_type=jnp.float32)
    cross = jnp.sum(cross_terms(first_part, second_part), axis=0)
    lag_count = length // win_count
    stacked = lax.psum(cross, "win")
    inverse = inverse_matrix(length, lax.axis_index("win") * lag_count, lag_count, seg_total)
    correlation = jnp.dot(inverse, stacked, precision=lax.Precision.HIGHEST)
    capacity = 5 * pair_first.shape[0] // (2 * tile_count)
    chooser = bucket_select(owners[:, 0], tile_count, capacity)
    picked = lax.dot_general(
        chooser,
        correlation.astype(jnp.bfloat16),
        (((1,), (1,)), ((), ())),
        preferred_element_type=jnp.float32,
    )
    buckets = picked.astype(jnp.bfloat16).reshape(tile_count, capacity, lag_count)
    received = lax.all_to_all(buckets, "tile", split_axis=0, concat_axis=0, tiled=True)
    return received[None]


def solution(mesh):
    placed = (P("win", "tile", None), P("tile"), P("tile"), P("tile", None))
    return jax.shard_map(
        per_device,
        mesh=mesh,
        in_specs=placed,
        out_specs=P("tile", None, None, "win"),
        check_vma=False,
    )
```

```python
import math

import jax
import jax.numpy as jnp
from jax import lax
from jax.sharding import PartitionSpec as P

BAND = 64


power_floor = 1e-06


def phase_table(rows, col_count, length):
    split = 64 if col_count % 64 == 0 else 1
    coarse = jnp.arange(col_count // split, dtype=jnp.int32) * split
    fine = jnp.arange(split, dtype=jnp.int32)
    scale = 2.0 * math.pi / length
    coarse_angle = ((rows[:, None] * coarse[None, :]) % length).astype(jnp.float32) * scale
    fine_angle = ((rows[:, None] * fine[None, :]) % length).astype(jnp.float32) * scale
    c_hi, s_hi = jnp.cos(coarse_angle)[:, :, None], jnp.sin(coarse_angle)[:, :, None]
    c_lo, s_lo = jnp.cos(fine_angle)[:, None, :], jnp.sin(fine_angle)[:, None, :]
    shape = (rows.shape[0], col_count)
    cosine = (c_hi * c_lo - s_hi * s_lo).reshape(shape)
    sine = (s_hi * c_lo + c_hi * s_lo).reshape(shape)
    return cosine, sine


def forward_matrix(length):
    cosine, sine = phase_table(jnp.arange(length // 2, dtype=jnp.int32), length, length)
    return jnp.concatenate([cosine, -sine], axis=0).astype(jnp.bfloat16)


def inverse_matrix(length, first_lag, lag_count, seg_total):
    half_bins = length // 2
    lags = jnp.arange(lag_count, dtype=jnp.int32) + first_lag
    cosine, sine = phase_table(lags, half_bins, length)
    bin_index = jnp.arange(half_bins)[None, :]
    weights = jnp.where(bin_index == 0, 1.0, 2.0).astype(jnp.float32) * (
        1.0 / math.sqrt(half_bins * seg_total)
    )
    return jnp.concatenate([weights * cosine, -weights * sine], axis=1)


def whiten(spectra, band_width):
    half_bins = spectra.shape[-2] // 2
    real_rows = spectra[..., :half_bins, :]
    imaginary = spectra[..., half_bins:, :]
    energy = real_rows * real_rows + imaginary * imaginary
    grouped = energy.shape[:-2] + (half_bins // band_width, band_width, energy.shape[-1])
    band_power = jnp.mean(energy.reshape(grouped), axis=-2, keepdims=True)
    inverse_rms = jnp.broadcast_to(lax.rsqrt(band_power + power_floor), grouped).reshape(
        energy.shape
    )
    return (spectra * jnp.concatenate([inverse_rms, inverse_rms], axis=-2)).astype(jnp.bfloat16)


def cross_terms(first_part, second_part):
    half_bins = first_part.shape[-2] // 2
    first_real = first_part[..., :half_bins, :].astype(jnp.float32)
    first_imag = first_part[..., half_bins:, :].astype(jnp.float32)
    second_real = second_part[..., :half_bins, :].astype(jnp.float32)
    second_imag = second_part[..., half_bins:, :].astype(jnp.float32)
    real_sum = first_real * second_real + first_imag * second_imag
    imag_sum = first_imag * second_real - first_real * second_imag
    return jnp.concatenate([real_sum, imag_sum], axis=-2)


def bucket_select(owner_ids, owner_count, capacity):
    onehot = (owner_ids[:, None] == jnp.arange(owner_count, dtype=jnp.int32)[None, :]).astype(
        jnp.int32
    )
    slot_rank = jnp.sum((jnp.cumsum(onehot, axis=0, dtype=jnp.int32) - 1) * onehot, axis=1)
    slot_id = owner_ids * capacity + slot_rank
    return (
        slot_id[None, :] == jnp.arange(owner_count * capacity, dtype=jnp.int32)[:, None]
    ).astype(jnp.bfloat16)


def tile_ring(mesh):
    count = mesh.shape["tile"]
    try:
        column = mesh.devices.reshape(count, -1)[:, 0]
        spots = [tuple(int(c) for c in d.coords) for d in column]
    except (AttributeError, TypeError):
        return list(range(count))
    near = [
        [j for j in range(count) if sum(abs(a - b) for a, b in zip(spots[i], spots[j])) == 1]
        for i in range(count)
    ]
    path, seen, budget = [0], {0}, [20000]

    def extend():
        budget[0] -= 1
        if budget[0] < 0:
            return False
        if len(path) == count:
            return count < 3 or 0 in near[path[-1]]
        options = [j for j in near[path[-1]] if j not in seen]
        options.sort(key=lambda j: sum(1 for k in near[j] if k not in seen))
        for j in options:
            path.append(j)
            seen.add(j)
            if extend():
                return True
            path.pop()
            seen.discard(j)
        return False

    return path if extend() else list(range(count))


def make_per_device(ring):
    count = len(ring)
    block_of = [0] * count
    for place, device in enumerate(ring):
        block_of[device] = place
    to_prev = [(ring[r], ring[(r - 1) % count]) for r in range(count)]
    to_next = [(ring[r], ring[(r + 1) % count]) for r in range(count)]

    def per_device(records, pair_first, pair_offset, owners):
        tile_count = lax.axis_size("tile")
        win_count = lax.axis_size("win")
        length = records.shape[1] * tile_count
        seg_total = records.shape[0] * win_count
        block = records.shape[2] // tile_count
        half = block // 2
        my_block = jnp.asarray(block_of, dtype=jnp.int32)[lax.axis_index("tile")]
        shifted = jnp.roll(records, -half, axis=2).reshape(
            records.shape[0], records.shape[1], tile_count, block
        )
        outgoing = jnp.concatenate([shifted[:, :, b] for b in block_of], axis=2)
        forward = forward_matrix(length)
        spectra = jnp.einsum(
            "fn,snc->sfc",
            forward,
            lax.all_to_all(outgoing, "tile", split_axis=2, concat_axis=1, tiled=True),
            preferred_element_type=jnp.float32,
        )
        whitened = whiten(spectra, BAND)
        from_prev = lax.ppermute(whitened[:, :, half:], "tile", to_next)
        from_next = lax.ppermute(whitened[:, :, :half], "tile", to_prev)
        joined = jnp.concatenate([from_prev, whitened, from_next], axis=2)
        all_first = lax.all_gather(pair_first, "tile")
        all_offset = lax.all_gather(pair_offset, "tile")
        all_owners = lax.all_gather(owners[:, 0], "tile")
        my_first = lax.dynamic_index_in_dim(all_first, my_block, 0, keepdims=False)
        my_offset = lax.dynamic_index_in_dim(all_offset, my_block, 0, keepdims=False)
        my_owners = lax.dynamic_index_in_dim(all_owners, my_block, 0, keepdims=False)
        channel_ids = jnp.arange(joined.shape[2], dtype=jnp.int32)[:, None]
        pick_first = (channel_ids == my_first[None, :]).astype(jnp.bfloat16)
        pick_second = (channel_ids == (my_first + my_offset)[None, :]).astype(jnp.bfloat16)
        first_part = jnp.einsum("sfc,cp->sfp", joined, pick_first, preferred_element_type=jnp.float32)
        second_part = jnp.einsum("sfc,cp->sfp", joined, pick_second, preferred_element_type=jnp.float32)
        cross = jnp.sum(cross_terms(first_part, second_part), axis=0)
        lag_count = length // win_count
        stacked = lax.psum(cross, "win")
        inverse = inverse_matrix(length, lax.axis_index("win") * lag_count, lag_count, seg_total)
        correlation = jnp.dot(inverse, stacked, precision=lax.Precision.HIGHEST)
        capacity = 5 * pair_first.shape[0] // (2 * tile_count)
        chooser = bucket_select(my_owners, tile_count, capacity)
        picked = lax.dot_general(
            chooser,
            correlation.astype(jnp.bfloat16),
            (((1,), (1,)), ((), ())),
            preferred_element_type=jnp.float32,
        )
        buckets = picked.astype(jnp.bfloat16).reshape(tile_count, capacity, lag_count)
        received = lax.all_to_all(buckets, "tile", split_axis=0, concat_axis=0, tiled=True)
        ordered = jnp.stack([received[d] for d in ring], axis=0)
        return ordered[None]

    return per_device


def solution(mesh):
    placed = (P("win", "tile", None), P("tile"), P("tile"), P("tile", None))
    return jax.shard_map(
        make_per_device(tile_ring(mesh)),
        mesh=mesh,
        in_specs=placed,
        out_specs=P("tile", None, None, "win"),
        check_vma=False,
    )
```

```python
import math

import jax
import jax.numpy as jnp
from jax import lax
from jax.sharding import PartitionSpec as P

BAND = 64


power_floor = 1e-06


def phase_table(rows, col_count, length):
    split = 64 if col_count % 64 == 0 else 1
    coarse = jnp.arange(col_count // split, dtype=jnp.int32) * split
    fine = jnp.arange(split, dtype=jnp.int32)
    scale = 2.0 * math.pi / length
    coarse_angle = ((rows[:, None] * coarse[None, :]) % length).astype(jnp.float32) * scale
    fine_angle = ((rows[:, None] * fine[None, :]) % length).astype(jnp.float32) * scale
    c_hi, s_hi = jnp.cos(coarse_angle)[:, :, None], jnp.sin(coarse_angle)[:, :, None]
    c_lo, s_lo = jnp.cos(fine_angle)[:, None, :], jnp.sin(fine_angle)[:, None, :]
    shape = (rows.shape[0], col_count)
    cosine = (c_hi * c_lo - s_hi * s_lo).reshape(shape)
    sine = (s_hi * c_lo + c_hi * s_lo).reshape(shape)
    return cosine, sine


def forward_matrix(length):
    cosine, sine = phase_table(jnp.arange(length // 2, dtype=jnp.int32), length, length)
    return jnp.concatenate([cosine, -sine], axis=0).astype(jnp.bfloat16)


def inverse_matrix(length, first_lag, lag_count, seg_total):
    half_bins = length // 2
    lags = jnp.arange(lag_count, dtype=jnp.int32) + first_lag
    cosine, sine = phase_table(lags, half_bins, length)
    bin_index = jnp.arange(half_bins)[None, :]
    weights = jnp.where(bin_index == 0, 1.0, 2.0).astype(jnp.float32) * (
        1.0 / math.sqrt(half_bins * seg_total)
    )
    return jnp.concatenate([weights * cosine, -weights * sine], axis=1)


def whiten(spectra, band_width):
    half_bins = spectra.shape[-2] // 2
    real_rows = spectra[..., :half_bins, :]
    imaginary = spectra[..., half_bins:, :]
    energy = real_rows * real_rows + imaginary * imaginary
    grouped = energy.shape[:-2] + (half_bins // band_width, band_width, energy.shape[-1])
    band_power = jnp.mean(energy.reshape(grouped), axis=-2, keepdims=True)
    inverse_rms = jnp.broadcast_to(lax.rsqrt(band_power + power_floor), grouped).reshape(
        energy.shape
    )
    return (spectra * jnp.concatenate([inverse_rms, inverse_rms], axis=-2)).astype(jnp.bfloat16)


def cross_terms(first_part, second_part):
    half_bins = first_part.shape[-2] // 2
    first_real = first_part[..., :half_bins, :].astype(jnp.float32)
    first_imag = first_part[..., half_bins:, :].astype(jnp.float32)
    second_real = second_part[..., :half_bins, :].astype(jnp.float32)
    second_imag = second_part[..., half_bins:, :].astype(jnp.float32)
    real_sum = first_real * second_real + first_imag * second_imag
    imag_sum = first_imag * second_real - first_real * second_imag
    return jnp.concatenate([real_sum, imag_sum], axis=-2)


def bucket_select(owner_ids, owner_count, capacity):
    onehot = (owner_ids[:, None] == jnp.arange(owner_count, dtype=jnp.int32)[None, :]).astype(
        jnp.int32
    )
    slot_rank = jnp.sum((jnp.cumsum(onehot, axis=0, dtype=jnp.int32) - 1) * onehot, axis=1)
    slot_id = owner_ids * capacity + slot_rank
    return (
        slot_id[None, :] == jnp.arange(owner_count * capacity, dtype=jnp.int32)[:, None]
    ).astype(jnp.bfloat16)


def tile_ring(mesh):
    count = mesh.shape["tile"]
    try:
        column = mesh.devices.reshape(count, -1)[:, 0]
        spots = [tuple(int(c) for c in d.coords) for d in column]
    except (AttributeError, TypeError):
        return list(range(count))
    near = [
        [j for j in range(count) if sum(abs(a - b) for a, b in zip(spots[i], spots[j])) == 1]
        for i in range(count)
    ]
    path, seen, budget = [0], {0}, [20000]

    def extend():
        budget[0] -= 1
        if budget[0] < 0:
            return False
        if len(path) == count:
            return count < 3 or 0 in near[path[-1]]
        options = [j for j in near[path[-1]] if j not in seen]
        options.sort(key=lambda j: sum(1 for k in near[j] if k not in seen))
        for j in options:
            path.append(j)
            seen.add(j)
            if extend():
                return True
            path.pop()
            seen.discard(j)
        return False

    return path if extend() else list(range(count))


def make_per_device(ring):
    count = len(ring)
    block_of = [0] * count
    for place, device in enumerate(ring):
        block_of[device] = place
    to_prev = [(ring[r], ring[(r - 1) % count]) for r in range(count)]
    to_next = [(ring[r], ring[(r + 1) % count]) for r in range(count)]
    to_owner = [(b, ring[b]) for b in range(count)]

    def per_device(records, pair_first, pair_offset, owners):
        pair_data = jnp.stack([pair_first, pair_offset, owners[:, 0]], axis=0)
        tile_count = lax.axis_size("tile")
        win_count = lax.axis_size("win")
        length = records.shape[1] * tile_count
        seg_total = records.shape[0] * win_count
        block = records.shape[2] // tile_count
        half = block // 2
        pieces = []
        for b in block_of:
            low = b * block + half
            if low + block <= records.shape[2]:
                pieces.append(records[:, :, low:low + block])
            else:
                pieces.append(
                    jnp.concatenate(
                        [records[:, :, low:], records[:, :, : low + block - records.shape[2]]], axis=2
                    )
                )
        outgoing = jnp.stack(pieces, axis=0)
        received = lax.all_to_all(outgoing, "tile", split_axis=0, concat_axis=0, tiled=True)
        forward = forward_matrix(length).reshape(length, tile_count, records.shape[1])
        spectra = jnp.einsum("fjm,jsmc->sfc", forward, received, preferred_element_type=jnp.float32)
        whitened = whiten(spectra, BAND)
        from_prev = lax.ppermute(whitened[:, :, half:], "tile", to_next)
        from_next = lax.ppermute(whitened[:, :, :half], "tile", to_prev)
        joined = jnp.concatenate([from_prev, whitened, from_next], axis=2)
        my_first, my_offset, my_owners = lax.ppermute(pair_data, "tile", to_owner)
        channel_ids = jnp.arange(joined.shape[2], dtype=jnp.int32)[:, None]
        pick_first = (channel_ids == my_first[None, :]).astype(jnp.bfloat16)
        pick_second = (channel_ids == (my_first + my_offset)[None, :]).astype(jnp.bfloat16)
        first_part = jnp.einsum("sfc,cp->sfp", joined, pick_first, preferred_element_type=jnp.float32)
        second_part = jnp.einsum("sfc,cp->sfp", joined, pick_second, preferred_element_type=jnp.float32)
        cross = jnp.sum(cross_terms(first_part, second_part), axis=0)
        lag_count = length // win_count
        stacked = lax.psum(cross, "win")
        inverse = inverse_matrix(length, lax.axis_index("win") * lag_count, lag_count, seg_total)
        correlation = jnp.dot(inverse, stacked, precision=lax.Precision.HIGHEST)
        capacity = 5 * pair_first.shape[0] // (2 * tile_count)
        chooser = bucket_select(my_owners, tile_count, capacity)
        picked = lax.dot_general(
            chooser,
            correlation.astype(jnp.bfloat16),
            (((1,), (1,)), ((), ())),
            preferred_element_type=jnp.float32,
        )
        buckets = picked.astype(jnp.bfloat16).reshape(tile_count, capacity, lag_count)
        received = lax.all_to_all(buckets, "tile", split_axis=0, concat_axis=0, tiled=True)
        ordered = jnp.stack([received[d] for d in ring], axis=0)
        return ordered[None]

    return per_device


def solution(mesh):
    placed = (P("win", "tile", None), P("tile"), P("tile"), P("tile", None))
    return jax.shard_map(
        make_per_device(tile_ring(mesh)),
        mesh=mesh,
        in_specs=placed,
        out_specs=P("tile", None, None, "win"),
        check_vma=False,
    )
```

```python
import math

import jax
import jax.numpy as jnp
from jax import lax
from jax.sharding import PartitionSpec as P

BAND = 64


power_floor = 1e-06


def phase_table(rows, col_count, length):
    split = 64 if col_count % 64 == 0 else 1
    coarse = jnp.arange(col_count // split, dtype=jnp.int32) * split
    fine = jnp.arange(split, dtype=jnp.int32)
    scale = 2.0 * math.pi / length
    coarse_angle = ((rows[:, None] * coarse[None, :]) % length).astype(jnp.float32) * scale
    fine_angle = ((rows[:, None] * fine[None, :]) % length).astype(jnp.float32) * scale
    c_hi, s_hi = jnp.cos(coarse_angle)[:, :, None], jnp.sin(coarse_angle)[:, :, None]
    c_lo, s_lo = jnp.cos(fine_angle)[:, None, :], jnp.sin(fine_angle)[:, None, :]
    shape = (rows.shape[0], col_count)
    cosine = (c_hi * c_lo - s_hi * s_lo).reshape(shape)
    sine = (s_hi * c_lo + c_hi * s_lo).reshape(shape)
    return cosine, sine


def forward_matrix(length):
    cosine, sine = phase_table(jnp.arange(length // 2, dtype=jnp.int32), length, length)
    return jnp.concatenate([cosine, -sine], axis=0).astype(jnp.bfloat16)


def inverse_matrix(length, first_lag, lag_count, seg_total):
    half_bins = length // 2
    lags = jnp.arange(lag_count, dtype=jnp.int32) + first_lag
    cosine, sine = phase_table(lags, half_bins, length)
    bin_index = jnp.arange(half_bins)[None, :]
    weights = jnp.where(bin_index == 0, 1.0, 2.0).astype(jnp.float32) * (
        1.0 / math.sqrt(half_bins * seg_total)
    )
    return jnp.concatenate([weights * cosine, -weights * sine], axis=1)


def whiten(spectra, band_width):
    half_bins = spectra.shape[-2] // 2
    real_rows = spectra[..., :half_bins, :]
    imaginary = spectra[..., half_bins:, :]
    energy = real_rows * real_rows + imaginary * imaginary
    grouped = energy.shape[:-2] + (half_bins // band_width, band_width, energy.shape[-1])
    band_power = jnp.mean(energy.reshape(grouped), axis=-2, keepdims=True)
    inverse_rms = jnp.broadcast_to(lax.rsqrt(band_power + power_floor), grouped).reshape(
        energy.shape
    )
    return (spectra * jnp.concatenate([inverse_rms, inverse_rms], axis=-2)).astype(jnp.bfloat16)


def cross_terms(first_part, second_part):
    half_bins = first_part.shape[-2] // 2
    first_real = first_part[..., :half_bins, :].astype(jnp.float32)
    first_imag = first_part[..., half_bins:, :].astype(jnp.float32)
    second_real = second_part[..., :half_bins, :].astype(jnp.float32)
    second_imag = second_part[..., half_bins:, :].astype(jnp.float32)
    real_sum = first_real * second_real + first_imag * second_imag
    imag_sum = first_imag * second_real - first_real * second_imag
    return jnp.concatenate([real_sum, imag_sum], axis=-2)


def bucket_select(owner_ids, owner_count, capacity):
    onehot = (owner_ids[:, None] == jnp.arange(owner_count, dtype=jnp.int32)[None, :]).astype(
        jnp.int32
    )
    slot_rank = jnp.sum((jnp.cumsum(onehot, axis=0, dtype=jnp.int32) - 1) * onehot, axis=1)
    slot_id = owner_ids * capacity + slot_rank
    return (
        slot_id[None, :] == jnp.arange(owner_count * capacity, dtype=jnp.int32)[:, None]
    ).astype(jnp.bfloat16)


def tile_ring(mesh):
    count = mesh.shape["tile"]
    try:
        column = mesh.devices.reshape(count, -1)[:, 0]
        spots = [tuple(int(c) for c in d.coords) for d in column]
    except (AttributeError, TypeError):
        return list(range(count))
    near = [
        [j for j in range(count) if sum(abs(a - b) for a, b in zip(spots[i], spots[j])) == 1]
        for i in range(count)
    ]
    path, seen, budget = [0], {0}, [20000]

    def extend():
        budget[0] -= 1
        if budget[0] < 0:
            return False
        if len(path) == count:
            return count < 3 or 0 in near[path[-1]]
        options = [j for j in near[path[-1]] if j not in seen]
        options.sort(key=lambda j: sum(1 for k in near[j] if k not in seen))
        for j in options:
            path.append(j)
            seen.add(j)
            if extend():
                return True
            path.pop()
            seen.discard(j)
        return False

    return path if extend() else list(range(count))


def make_per_device(ring):
    count = len(ring)
    block_of = [0] * count
    for place, device in enumerate(ring):
        block_of[device] = place
    to_prev = [(ring[r], ring[(r - 1) % count]) for r in range(count)]
    to_next = [(ring[r], ring[(r + 1) % count]) for r in range(count)]
    to_owner = [(b, ring[b]) for b in range(count)]

    def per_device(records, pair_first, pair_offset, owners):
        pair_data = jnp.stack([pair_first, pair_offset, owners[:, 0]], axis=0)
        tile_count = lax.axis_size("tile")
        win_count = lax.axis_size("win")
        length = records.shape[1] * tile_count
        seg_total = records.shape[0] * win_count
        block = records.shape[2] // tile_count
        half = block // 2
        forward = forward_matrix(length).reshape(length, tile_count, records.shape[1])
        my_first, my_offset, my_owners = lax.ppermute(pair_data, "tile", to_owner)
        channel_ids = jnp.arange(2 * block, dtype=jnp.int32)[:, None]
        pick_first = (channel_ids == my_first[None, :]).astype(jnp.bfloat16)
        pick_second = (channel_ids == (my_first + my_offset)[None, :]).astype(jnp.bfloat16)
        cross = None
        for segment in range(records.shape[0]):
            pieces = []
            for b in block_of:
                low = b * block + half
                if low + block <= records.shape[2]:
                    pieces.append(records[segment, :, low:low + block])
                else:
                    pieces.append(
                        jnp.concatenate(
                            [records[segment, :, low:], records[segment, :, : low + block - records.shape[2]]],
                            axis=1,
                        )
                    )
            outgoing = jnp.stack(pieces, axis=0)
            received = lax.all_to_all(outgoing, "tile", split_axis=0, concat_axis=0, tiled=True)
            spectra = jnp.einsum("fjm,jmc->fc", forward, received, preferred_element_type=jnp.float32)
            whitened = whiten(spectra, BAND)
            from_prev = lax.ppermute(whitened[:, half:], "tile", to_next)
            from_next = lax.ppermute(whitened[:, :half], "tile", to_prev)
            joined = jnp.concatenate([from_prev, whitened, from_next], axis=1)
            first_part = jnp.dot(joined, pick_first, preferred_element_type=jnp.float32)
            second_part = jnp.dot(joined, pick_second, preferred_element_type=jnp.float32)
            term = cross_terms(first_part, second_part)
            cross = term if cross is None else cross + term
        lag_count = length // win_count
        stacked = lax.psum(cross, "win")
        inverse = inverse_matrix(length, lax.axis_index("win") * lag_count, lag_count, seg_total)
        correlation = jnp.dot(inverse, stacked, precision=lax.Precision.HIGHEST)
        capacity = 5 * pair_first.shape[0] // (2 * tile_count)
        chooser = bucket_select(my_owners, tile_count, capacity)
        picked = lax.dot_general(
            chooser,
            correlation.astype(jnp.bfloat16),
            (((1,), (1,)), ((), ())),
            preferred_element_type=jnp.float32,
        )
        buckets = picked.astype(jnp.bfloat16).reshape(tile_count, capacity, lag_count)
        received = lax.all_to_all(buckets, "tile", split_axis=0, concat_axis=0, tiled=True)
        ordered = jnp.stack([received[d] for d in ring], axis=0)
        return ordered[None]

    return per_device


def solution(mesh):
    placed = (P("win", "tile", None), P("tile"), P("tile"), P("tile", None))
    return jax.shard_map(
        make_per_device(tile_ring(mesh)),
        mesh=mesh,
        in_specs=placed,
        out_specs=P("tile", None, None, "win"),
        check_vma=False,
    )
```

```python
import math

import jax
import jax.numpy as jnp
from jax import lax
from jax.sharding import PartitionSpec as P

BAND = 64


power_floor = 1e-06


def phase_table(rows, col_count, length):
    split = 64 if col_count % 64 == 0 else 1
    coarse = jnp.arange(col_count // split, dtype=jnp.int32) * split
    fine = jnp.arange(split, dtype=jnp.int32)
    scale = 2.0 * math.pi / length
    coarse_angle = ((rows[:, None] * coarse[None, :]) % length).astype(jnp.float32) * scale
    fine_angle = ((rows[:, None] * fine[None, :]) % length).astype(jnp.float32) * scale
    c_hi, s_hi = jnp.cos(coarse_angle)[:, :, None], jnp.sin(coarse_angle)[:, :, None]
    c_lo, s_lo = jnp.cos(fine_angle)[:, None, :], jnp.sin(fine_angle)[:, None, :]
    shape = (rows.shape[0], col_count)
    cosine = (c_hi * c_lo - s_hi * s_lo).reshape(shape)
    sine = (s_hi * c_lo + c_hi * s_lo).reshape(shape)
    return cosine, sine


def forward_matrix(length):
    cosine, sine = phase_table(jnp.arange(length // 2, dtype=jnp.int32), length, length)
    return jnp.concatenate([cosine, -sine], axis=0).astype(jnp.bfloat16)


def inverse_matrix(length, first_lag, lag_count, seg_total):
    half_bins = length // 2
    lags = jnp.arange(lag_count, dtype=jnp.int32) + first_lag
    cosine, sine = phase_table(lags, half_bins, length)
    bin_index = jnp.arange(half_bins)[None, :]
    weights = jnp.where(bin_index == 0, 1.0, 2.0).astype(jnp.float32) * (
        1.0 / math.sqrt(half_bins * seg_total)
    )
    return jnp.concatenate([weights * cosine, -weights * sine], axis=1)


def whiten(spectra, band_width):
    half_bins = spectra.shape[-2] // 2
    real_rows = spectra[..., :half_bins, :]
    imaginary = spectra[..., half_bins:, :]
    energy = real_rows * real_rows + imaginary * imaginary
    grouped = energy.shape[:-2] + (half_bins // band_width, band_width, energy.shape[-1])
    band_power = jnp.mean(energy.reshape(grouped), axis=-2, keepdims=True)
    inverse_rms = jnp.broadcast_to(lax.rsqrt(band_power + power_floor), grouped).reshape(
        energy.shape
    )
    return (spectra * jnp.concatenate([inverse_rms, inverse_rms], axis=-2)).astype(jnp.bfloat16)


def cross_terms(first_part, second_part):
    half_bins = first_part.shape[-2] // 2
    first_real = first_part[..., :half_bins, :].astype(jnp.float32)
    first_imag = first_part[..., half_bins:, :].astype(jnp.float32)
    second_real = second_part[..., :half_bins, :].astype(jnp.float32)
    second_imag = second_part[..., half_bins:, :].astype(jnp.float32)
    real_sum = first_real * second_real + first_imag * second_imag
    imag_sum = first_imag * second_real - first_real * second_imag
    return jnp.concatenate([real_sum, imag_sum], axis=-2)


def bucket_select(owner_ids, owner_count, capacity):
    onehot = (owner_ids[:, None] == jnp.arange(owner_count, dtype=jnp.int32)[None, :]).astype(
        jnp.int32
    )
    slot_rank = jnp.sum((jnp.cumsum(onehot, axis=0, dtype=jnp.int32) - 1) * onehot, axis=1)
    slot_id = owner_ids * capacity + slot_rank
    return (
        slot_id[None, :] == jnp.arange(owner_count * capacity, dtype=jnp.int32)[:, None]
    ).astype(jnp.bfloat16)


def tile_ring(mesh):
    count = mesh.shape["tile"]
    try:
        column = mesh.devices.reshape(count, -1)[:, 0]
        spots = [tuple(int(c) for c in d.coords) for d in column]
    except (AttributeError, TypeError):
        return list(range(count))
    near = [
        [j for j in range(count) if sum(abs(a - b) for a, b in zip(spots[i], spots[j])) == 1]
        for i in range(count)
    ]
    path, seen, budget = [0], {0}, [20000]

    def extend():
        budget[0] -= 1
        if budget[0] < 0:
            return False
        if len(path) == count:
            return count < 3 or 0 in near[path[-1]]
        options = [j for j in near[path[-1]] if j not in seen]
        options.sort(key=lambda j: sum(1 for k in near[j] if k not in seen))
        for j in options:
            path.append(j)
            seen.add(j)
            if extend():
                return True
            path.pop()
            seen.discard(j)
        return False

    return path if extend() else list(range(count))


def make_per_device(ring):
    count = len(ring)
    block_of = [0] * count
    for place, device in enumerate(ring):
        block_of[device] = place
    to_prev = [(ring[r], ring[(r - 1) % count]) for r in range(count)]
    to_next = [(ring[r], ring[(r + 1) % count]) for r in range(count)]
    to_owner = [(b, ring[b]) for b in range(count)]

    def per_device(records, pair_first, pair_offset, owners):
        pair_data = jnp.stack([pair_first, pair_offset, owners[:, 0]], axis=0)
        tile_count = lax.axis_size("tile")
        win_count = lax.axis_size("win")
        length = records.shape[1] * tile_count
        seg_total = records.shape[0] * win_count
        block = records.shape[2] // tile_count
        half = block // 2
        forward = forward_matrix(length).reshape(length, tile_count, records.shape[1])
        my_first, my_offset, my_owners = lax.ppermute(pair_data, "tile", to_owner)
        channel_ids = jnp.arange(2 * block, dtype=jnp.int32)[:, None]
        pick_first = (channel_ids == my_first[None, :]).astype(jnp.bfloat16)
        pick_second = (channel_ids == (my_first + my_offset)[None, :]).astype(jnp.bfloat16)
        cross = None
        for segment in range(records.shape[0]):
            pieces = []
            for b in block_of:
                low = b * block + half
                if low + block <= records.shape[2]:
                    pieces.append(records[segment, :, low:low + block])
                else:
                    pieces.append(
                        jnp.concatenate(
                            [records[segment, :, low:], records[segment, :, : low + block - records.shape[2]]],
                            axis=1,
                        )
                    )
            outgoing = jnp.stack(pieces, axis=0)
            received = lax.all_to_all(outgoing, "tile", split_axis=0, concat_axis=0, tiled=True)
            spectra = jnp.einsum("fjm,jmc->fc", forward, received, preferred_element_type=jnp.float32)
            whitened = whiten(spectra, BAND)
            from_prev = lax.ppermute(whitened[:, half:], "tile", to_next)
            from_next = lax.ppermute(whitened[:, :half], "tile", to_prev)
            joined = jnp.concatenate([from_prev, whitened, from_next], axis=1)
            first_part = jnp.dot(joined, pick_first, preferred_element_type=jnp.float32)
            second_part = jnp.dot(joined, pick_second, preferred_element_type=jnp.float32)
            term = cross_terms(first_part, second_part)
            cross = term if cross is None else cross + term
        lag_count = length // win_count
        stacked = lax.psum_scatter(cross, "win", scatter_dimension=1, tiled=True)
        inverse = inverse_matrix(length, 0, length, seg_total)
        own_pairs = jnp.dot(inverse, stacked, precision=lax.Precision.HIGHEST).astype(jnp.bfloat16)
        correlation = lax.all_to_all(own_pairs, "win", split_axis=0, concat_axis=1, tiled=True)
        capacity = 5 * pair_first.shape[0] // (2 * tile_count)
        chooser = bucket_select(my_owners, tile_count, capacity)
        picked = lax.dot_general(
            chooser,
            correlation,
            (((1,), (1,)), ((), ())),
            preferred_element_type=jnp.float32,
        )
        buckets = picked.astype(jnp.bfloat16).reshape(tile_count, capacity, lag_count)
        received = lax.all_to_all(buckets, "tile", split_axis=0, concat_axis=0, tiled=True)
        ordered = jnp.stack([received[d] for d in ring], axis=0)
        return ordered[None]

    return per_device


def solution(mesh):
    placed = (P("win", "tile", None), P("tile"), P("tile"), P("tile", None))
    return jax.shard_map(
        make_per_device(tile_ring(mesh)),
        mesh=mesh,
        in_specs=placed,
        out_specs=P("tile", None, None, "win"),
        check_vma=False,
    )
```

```python
import math

import jax
import jax.numpy as jnp
from jax import lax
from jax.sharding import PartitionSpec as P

BAND = 64


power_floor = 1e-06


def phase_table(rows, col_count, length):
    split = 64 if col_count % 64 == 0 else 1
    coarse = jnp.arange(col_count // split, dtype=jnp.int32) * split
    fine = jnp.arange(split, dtype=jnp.int32)
    scale = 2.0 * math.pi / length
    coarse_angle = ((rows[:, None] * coarse[None, :]) % length).astype(jnp.float32) * scale
    fine_angle = ((rows[:, None] * fine[None, :]) % length).astype(jnp.float32) * scale
    c_hi, s_hi = jnp.cos(coarse_angle)[:, :, None], jnp.sin(coarse_angle)[:, :, None]
    c_lo, s_lo = jnp.cos(fine_angle)[:, None, :], jnp.sin(fine_angle)[:, None, :]
    shape = (rows.shape[0], col_count)
    cosine = (c_hi * c_lo - s_hi * s_lo).reshape(shape)
    sine = (s_hi * c_lo + c_hi * s_lo).reshape(shape)
    return cosine, sine


def forward_matrix(length):
    cosine, sine = phase_table(jnp.arange(length // 2, dtype=jnp.int32), length, length)
    return jnp.concatenate([cosine, -sine], axis=0).astype(jnp.bfloat16)


def inverse_matrix(length, first_lag, lag_count, seg_total):
    half_bins = length // 2
    lags = jnp.arange(lag_count, dtype=jnp.int32) + first_lag
    cosine, sine = phase_table(lags, half_bins, length)
    bin_index = jnp.arange(half_bins)[None, :]
    weights = jnp.where(bin_index == 0, 1.0, 2.0).astype(jnp.float32) * (
        1.0 / math.sqrt(half_bins * seg_total)
    )
    return jnp.concatenate([weights * cosine, -weights * sine], axis=1)


def whiten(spectra, band_width):
    half_bins = spectra.shape[-2] // 2
    real_rows = spectra[..., :half_bins, :]
    imaginary = spectra[..., half_bins:, :]
    energy = real_rows * real_rows + imaginary * imaginary
    grouped = energy.shape[:-2] + (half_bins // band_width, band_width, energy.shape[-1])
    band_power = jnp.mean(energy.reshape(grouped), axis=-2, keepdims=True)
    inverse_rms = jnp.broadcast_to(lax.rsqrt(band_power + power_floor), grouped).reshape(
        energy.shape
    )
    return (spectra * jnp.concatenate([inverse_rms, inverse_rms], axis=-2)).astype(jnp.bfloat16)


def cross_terms(first_part, second_part):
    half_bins = first_part.shape[-2] // 2
    first_real = first_part[..., :half_bins, :].astype(jnp.float32)
    first_imag = first_part[..., half_bins:, :].astype(jnp.float32)
    second_real = second_part[..., :half_bins, :].astype(jnp.float32)
    second_imag = second_part[..., half_bins:, :].astype(jnp.float32)
    real_sum = first_real * second_real + first_imag * second_imag
    imag_sum = first_imag * second_real - first_real * second_imag
    return jnp.concatenate([real_sum, imag_sum], axis=-2)


def bucket_select(owner_ids, owner_count, capacity):
    onehot = (owner_ids[:, None] == jnp.arange(owner_count, dtype=jnp.int32)[None, :]).astype(
        jnp.int32
    )
    slot_rank = jnp.sum((jnp.cumsum(onehot, axis=0, dtype=jnp.int32) - 1) * onehot, axis=1)
    slot_id = owner_ids * capacity + slot_rank
    return (
        slot_id[None, :] == jnp.arange(owner_count * capacity, dtype=jnp.int32)[:, None]
    ).astype(jnp.bfloat16)


def tile_ring(mesh):
    count = mesh.shape["tile"]
    try:
        column = mesh.devices.reshape(count, -1)[:, 0]
        spots = [tuple(int(c) for c in d.coords) for d in column]
    except (AttributeError, TypeError):
        return list(range(count))
    near = [
        [j for j in range(count) if sum(abs(a - b) for a, b in zip(spots[i], spots[j])) == 1]
        for i in range(count)
    ]
    path, seen, budget = [0], {0}, [20000]

    def extend():
        budget[0] -= 1
        if budget[0] < 0:
            return False
        if len(path) == count:
            return count < 3 or 0 in near[path[-1]]
        options = [j for j in near[path[-1]] if j not in seen]
        options.sort(key=lambda j: sum(1 for k in near[j] if k not in seen))
        for j in options:
            path.append(j)
            seen.add(j)
            if extend():
                return True
            path.pop()
            seen.discard(j)
        return False

    return path if extend() else list(range(count))


def make_per_device(ring):
    count = len(ring)
    block_of = [0] * count
    for place, device in enumerate(ring):
        block_of[device] = place
    to_prev = [(ring[r], ring[(r - 1) % count]) for r in range(count)]
    to_next = [(ring[r], ring[(r + 1) % count]) for r in range(count)]
    to_owner = [(b, ring[b]) for b in range(count)]

    def per_device(records, pair_first, pair_offset, owners):
        pair_data = jnp.stack([pair_first, pair_offset, owners[:, 0]], axis=0)
        tile_count = lax.axis_size("tile")
        win_count = lax.axis_size("win")
        length = records.shape[1] * tile_count
        seg_total = records.shape[0] * win_count
        block = records.shape[2] // tile_count
        half = block // 2
        forward = forward_matrix(length).reshape(length, tile_count, records.shape[1])
        my_first, my_offset, my_owners = lax.ppermute(pair_data, "tile", to_owner)
        channel_ids = jnp.arange(2 * block, dtype=jnp.int32)[:, None]
        pick_first = (channel_ids == my_first[None, :]).astype(jnp.bfloat16)
        pick_second = (channel_ids == (my_first + my_offset)[None, :]).astype(jnp.bfloat16)
        cross = None
        arrived = []
        for segment in range(records.shape[0]):
            pieces = []
            for b in block_of:
                low = b * block + half
                if low + block <= records.shape[2]:
                    pieces.append(records[segment, :, low:low + block])
                else:
                    pieces.append(
                        jnp.concatenate(
                            [records[segment, :, low:], records[segment, :, : low + block - records.shape[2]]],
                            axis=1,
                        )
                    )
            outgoing = jnp.stack(pieces, axis=0)
            if segment >= 2:
                outgoing, _ = lax.optimization_barrier((outgoing, arrived[segment - 2]))
            received = lax.all_to_all(outgoing, "tile", split_axis=0, concat_axis=0, tiled=True)
            spectra = jnp.einsum("fjm,jmc->fc", forward, received, preferred_element_type=jnp.float32)
            whitened = whiten(spectra, BAND)
            from_prev = lax.ppermute(whitened[:, half:], "tile", to_next)
            from_next = lax.ppermute(whitened[:, :half], "tile", to_prev)
            arrived.append((from_prev, from_next))
            joined = jnp.concatenate([from_prev, whitened, from_next], axis=1)
            first_part = jnp.dot(joined, pick_first, preferred_element_type=jnp.float32)
            second_part = jnp.dot(joined, pick_second, preferred_element_type=jnp.float32)
            term = cross_terms(first_part, second_part)
            cross = term if cross is None else cross + term
        lag_count = length // win_count
        stacked = lax.psum_scatter(cross, "win", scatter_dimension=1, tiled=True)
        inverse = inverse_matrix(length, 0, length, seg_total)
        own_pairs = jnp.dot(inverse, stacked, precision=lax.Precision.HIGH).astype(jnp.bfloat16)
        correlation = lax.all_to_all(own_pairs, "win", split_axis=0, concat_axis=1, tiled=True)
        capacity = 5 * pair_first.shape[0] // (2 * tile_count)
        chooser = bucket_select(my_owners, tile_count, capacity)
        picked = lax.dot_general(
            chooser,
            correlation,
            (((1,), (1,)), ((), ())),
            preferred_element_type=jnp.float32,
        )
        buckets = picked.astype(jnp.bfloat16).reshape(tile_count, capacity, lag_count)
        received = lax.all_to_all(buckets, "tile", split_axis=0, concat_axis=0, tiled=True)
        ordered = jnp.stack([received[d] for d in ring], axis=0)
        return ordered[None]

    return per_device


def solution(mesh):
    placed = (P("win", "tile", None), P("tile"), P("tile"), P("tile", None))
    return jax.shard_map(
        make_per_device(tile_ring(mesh)),
        mesh=mesh,
        in_specs=placed,
        out_specs=P("tile", None, None, "win"),
        check_vma=False,
    )
```

```python
import math

import jax
import jax.numpy as jnp
from jax import lax
from jax.experimental import pallas as pl
from jax.experimental.pallas import tpu as pltpu
from jax.sharding import PartitionSpec as P

BAND = 64


power_floor = 1e-06


def phase_table(rows, col_count, length):
    split = 64 if col_count % 64 == 0 else 1
    coarse = jnp.arange(col_count // split, dtype=jnp.int32) * split
    fine = jnp.arange(split, dtype=jnp.int32)
    scale = 2.0 * math.pi / length
    coarse_angle = ((rows[:, None] * coarse[None, :]) % length).astype(jnp.float32) * scale
    fine_angle = ((rows[:, None] * fine[None, :]) % length).astype(jnp.float32) * scale
    c_hi, s_hi = jnp.cos(coarse_angle)[:, :, None], jnp.sin(coarse_angle)[:, :, None]
    c_lo, s_lo = jnp.cos(fine_angle)[:, None, :], jnp.sin(fine_angle)[:, None, :]
    shape = (rows.shape[0], col_count)
    cosine = (c_hi * c_lo - s_hi * s_lo).reshape(shape)
    sine = (s_hi * c_lo + c_hi * s_lo).reshape(shape)
    return cosine, sine


def forward_matrix(length):
    cosine, sine = phase_table(jnp.arange(length // 2, dtype=jnp.int32), length, length)
    return jnp.concatenate([cosine, -sine], axis=0).astype(jnp.bfloat16)


def inverse_matrix(length, first_lag, lag_count, seg_total):
    half_bins = length // 2
    lags = jnp.arange(lag_count, dtype=jnp.int32) + first_lag
    cosine, sine = phase_table(lags, half_bins, length)
    bin_index = jnp.arange(half_bins)[None, :]
    weights = jnp.where(bin_index == 0, 1.0, 2.0).astype(jnp.float32) * (
        1.0 / math.sqrt(half_bins * seg_total)
    )
    return jnp.concatenate([weights * cosine, -weights * sine], axis=1)


def whiten(spectra, band_width):
    half_bins = spectra.shape[-2] // 2
    real_rows = spectra[..., :half_bins, :]
    imaginary = spectra[..., half_bins:, :]
    energy = real_rows * real_rows + imaginary * imaginary
    grouped = energy.shape[:-2] + (half_bins // band_width, band_width, energy.shape[-1])
    band_power = jnp.mean(energy.reshape(grouped), axis=-2, keepdims=True)
    inverse_rms = jnp.broadcast_to(lax.rsqrt(band_power + power_floor), grouped).reshape(
        energy.shape
    )
    return (spectra * jnp.concatenate([inverse_rms, inverse_rms], axis=-2)).astype(jnp.bfloat16)


def cross_terms(first_part, second_part):
    half_bins = first_part.shape[-2] // 2
    first_real = first_part[..., :half_bins, :].astype(jnp.float32)
    first_imag = first_part[..., half_bins:, :].astype(jnp.float32)
    second_real = second_part[..., :half_bins, :].astype(jnp.float32)
    second_imag = second_part[..., half_bins:, :].astype(jnp.float32)
    real_sum = first_real * second_real + first_imag * second_imag
    imag_sum = first_imag * second_real - first_real * second_imag
    return jnp.concatenate([real_sum, imag_sum], axis=-2)


def bucket_select(owner_ids, owner_count, capacity):
    onehot = (owner_ids[:, None] == jnp.arange(owner_count, dtype=jnp.int32)[None, :]).astype(
        jnp.int32
    )
    slot_rank = jnp.sum((jnp.cumsum(onehot, axis=0, dtype=jnp.int32) - 1) * onehot, axis=1)
    slot_id = owner_ids * capacity + slot_rank
    return (
        slot_id[None, :] == jnp.arange(owner_count * capacity, dtype=jnp.int32)[:, None]
    ).astype(jnp.bfloat16)


def tile_ring(mesh):
    count = mesh.shape["tile"]
    try:
        column = mesh.devices.reshape(count, -1)[:, 0]
        spots = [tuple(int(c) for c in d.coords) for d in column]
    except (AttributeError, TypeError):
        return list(range(count))
    near = [
        [j for j in range(count) if sum(abs(a - b) for a, b in zip(spots[i], spots[j])) == 1]
        for i in range(count)
    ]
    path, seen, budget = [0], {0}, [20000]

    def extend():
        budget[0] -= 1
        if budget[0] < 0:
            return False
        if len(path) == count:
            return count < 3 or 0 in near[path[-1]]
        options = [j for j in near[path[-1]] if j not in seen]
        options.sort(key=lambda j: sum(1 for k in near[j] if k not in seen))
        for j in options:
            path.append(j)
            seen.add(j)
            if extend():
                return True
            path.pop()
            seen.discard(j)
        return False

    return path if extend() else list(range(count))


def block_moves(block_of, block, half, width):
    moves = []
    for place, b in enumerate(block_of):
        low = b * block + half
        if low + block <= width:
            moves.append((low, place, 0, block))
        else:
            moves.append((low, place, 0, width - low))
            moves.append((0, place, width - low, low + block - width))
    return moves


def lay_out_blocks(records, block_of, block, half):
    segs, rows, width = records.shape
    moves = block_moves(block_of, block, half, width)

    def kernel(src, dst, sems):
        copies = []
        for index, (col, place, at, size) in enumerate(moves):
            copy = pltpu.make_async_copy(
                src.at[:, :, pl.ds(col, size)],
                dst.at[:, place, :, pl.ds(at, size)],
                sems.at[index],
            )
            copy.start()
            copies.append(copy)
        for copy in copies:
            copy.wait()

    return pl.pallas_call(
        kernel,
        out_shape=jax.ShapeDtypeStruct((segs, len(block_of), rows, block), records.dtype),
        in_specs=[pl.BlockSpec(memory_space=pl.ANY)],
        out_specs=pl.BlockSpec(memory_space=pl.ANY),
        scratch_shapes=[pltpu.SemaphoreType.DMA((len(moves),))],
    )(records)


def make_per_device(ring):
    count = len(ring)
    block_of = [0] * count
    for place, device in enumerate(ring):
        block_of[device] = place
    to_prev = [(ring[r], ring[(r - 1) % count]) for r in range(count)]
    to_next = [(ring[r], ring[(r + 1) % count]) for r in range(count)]
    to_owner = [(b, ring[b]) for b in range(count)]

    def per_device(records, pair_first, pair_offset, owners):
        pair_data = jnp.stack([pair_first, pair_offset, owners[:, 0]], axis=0)
        tile_count = lax.axis_size("tile")
        win_count = lax.axis_size("win")
        length = records.shape[1] * tile_count
        seg_total = records.shape[0] * win_count
        block = records.shape[2] // tile_count
        half = block // 2
        forward = forward_matrix(length).reshape(length, tile_count, records.shape[1])
        my_first, my_offset, my_owners = lax.ppermute(pair_data, "tile", to_owner)
        channel_ids = jnp.arange(2 * block, dtype=jnp.int32)[:, None]
        pick_first = (channel_ids == my_first[None, :]).astype(jnp.bfloat16)
        pick_second = (channel_ids == (my_first + my_offset)[None, :]).astype(jnp.bfloat16)
        cross = None
        laid_out = lay_out_blocks(records, block_of, block, half)
        for segment in range(records.shape[0]):
            outgoing = laid_out[segment]
            received = lax.all_to_all(outgoing, "tile", split_axis=0, concat_axis=0, tiled=True)
            spectra = jnp.einsum("fjm,jmc->fc", forward, received, preferred_element_type=jnp.float32)
            whitened = whiten(spectra, BAND)
            from_prev = lax.ppermute(whitened[:, half:], "tile", to_next)
            from_next = lax.ppermute(whitened[:, :half], "tile", to_prev)
            joined = jnp.concatenate([from_prev, whitened, from_next], axis=1)
            first_part = jnp.dot(joined, pick_first, preferred_element_type=jnp.float32)
            second_part = jnp.dot(joined, pick_second, preferred_element_type=jnp.float32)
            term = cross_terms(first_part, second_part)
            cross = term if cross is None else cross + term
        lag_count = length // win_count
        stacked = lax.psum(cross, "win")
        inverse = inverse_matrix(length, lax.axis_index("win") * lag_count, lag_count, seg_total)
        correlation = jnp.dot(inverse, stacked, precision=lax.Precision.HIGH)
        capacity = 5 * pair_first.shape[0] // (2 * tile_count)
        chooser = bucket_select(my_owners, tile_count, capacity)
        picked = lax.dot_general(
            chooser,
            correlation.astype(jnp.bfloat16),
            (((1,), (1,)), ((), ())),
            preferred_element_type=jnp.float32,
        )
        buckets = picked.astype(jnp.bfloat16).reshape(tile_count, capacity, lag_count)
        received = lax.all_to_all(buckets, "tile", split_axis=0, concat_axis=0, tiled=True)
        ordered = jnp.stack([received[d] for d in ring], axis=0)
        return ordered[None]

    return per_device


def solution(mesh):
    placed = (P("win", "tile", None), P("tile"), P("tile"), P("tile", None))
    return jax.shard_map(
        make_per_device(tile_ring(mesh)),
        mesh=mesh,
        in_specs=placed,
        out_specs=P("tile", None, None, "win"),
        check_vma=False,
    )
```

```python
import math

import jax
import jax.numpy as jnp
from jax import lax
from jax.sharding import PartitionSpec as P

BAND = 64


power_floor = 1e-06


def phase_table(rows, col_count, length):
    split = 64 if col_count % 64 == 0 else 1
    coarse = jnp.arange(col_count // split, dtype=jnp.int32) * split
    fine = jnp.arange(split, dtype=jnp.int32)
    scale = 2.0 * math.pi / length
    coarse_angle = ((rows[:, None] * coarse[None, :]) % length).astype(jnp.float32) * scale
    fine_angle = ((rows[:, None] * fine[None, :]) % length).astype(jnp.float32) * scale
    c_hi, s_hi = jnp.cos(coarse_angle)[:, :, None], jnp.sin(coarse_angle)[:, :, None]
    c_lo, s_lo = jnp.cos(fine_angle)[:, None, :], jnp.sin(fine_angle)[:, None, :]
    shape = (rows.shape[0], col_count)
    cosine = (c_hi * c_lo - s_hi * s_lo).reshape(shape)
    sine = (s_hi * c_lo + c_hi * s_lo).reshape(shape)
    return cosine, sine


def forward_matrix(length):
    cosine, sine = phase_table(jnp.arange(length // 2, dtype=jnp.int32), length, length)
    return jnp.concatenate([cosine, -sine], axis=0).astype(jnp.bfloat16)


def inverse_matrix(length, first_lag, lag_count, seg_total):
    half_bins = length // 2
    lags = jnp.arange(lag_count, dtype=jnp.int32) + first_lag
    cosine, sine = phase_table(lags, half_bins, length)
    bin_index = jnp.arange(half_bins)[None, :]
    weights = jnp.where(bin_index == 0, 1.0, 2.0).astype(jnp.float32) * (
        1.0 / math.sqrt(half_bins * seg_total)
    )
    return jnp.concatenate([weights * cosine, -weights * sine], axis=1)


def whiten(spectra, band_width):
    half_bins = spectra.shape[-2] // 2
    real_rows = spectra[..., :half_bins, :]
    imaginary = spectra[..., half_bins:, :]
    energy = real_rows * real_rows + imaginary * imaginary
    grouped = energy.shape[:-2] + (half_bins // band_width, band_width, energy.shape[-1])
    band_power = jnp.mean(energy.reshape(grouped), axis=-2, keepdims=True)
    inverse_rms = jnp.broadcast_to(lax.rsqrt(band_power + power_floor), grouped).reshape(
        energy.shape
    )
    return (spectra * jnp.concatenate([inverse_rms, inverse_rms], axis=-2)).astype(jnp.bfloat16)


def cross_terms(first_part, second_part):
    half_bins = first_part.shape[-2] // 2
    first_real = first_part[..., :half_bins, :].astype(jnp.float32)
    first_imag = first_part[..., half_bins:, :].astype(jnp.float32)
    second_real = second_part[..., :half_bins, :].astype(jnp.float32)
    second_imag = second_part[..., half_bins:, :].astype(jnp.float32)
    real_sum = first_real * second_real + first_imag * second_imag
    imag_sum = first_imag * second_real - first_real * second_imag
    return jnp.concatenate([real_sum, imag_sum], axis=-2)


def bucket_select(owner_ids, owner_count, capacity):
    onehot = (owner_ids[:, None] == jnp.arange(owner_count, dtype=jnp.int32)[None, :]).astype(
        jnp.int32
    )
    slot_rank = jnp.sum((jnp.cumsum(onehot, axis=0, dtype=jnp.int32) - 1) * onehot, axis=1)
    slot_id = owner_ids * capacity + slot_rank
    return (
        slot_id[None, :] == jnp.arange(owner_count * capacity, dtype=jnp.int32)[:, None]
    ).astype(jnp.bfloat16)


def tile_ring(mesh):
    count = mesh.shape["tile"]
    try:
        column = mesh.devices.reshape(count, -1)[:, 0]
        spots = [tuple(int(c) for c in d.coords) for d in column]
    except (AttributeError, TypeError):
        return list(range(count))
    near = [
        [j for j in range(count) if sum(abs(a - b) for a, b in zip(spots[i], spots[j])) == 1]
        for i in range(count)
    ]
    path, seen, budget = [0], {0}, [20000]

    def extend():
        budget[0] -= 1
        if budget[0] < 0:
            return False
        if len(path) == count:
            return count < 3 or 0 in near[path[-1]]
        options = [j for j in near[path[-1]] if j not in seen]
        options.sort(key=lambda j: sum(1 for k in near[j] if k not in seen))
        for j in options:
            path.append(j)
            seen.add(j)
            if extend():
                return True
            path.pop()
            seen.discard(j)
        return False

    return path if extend() else list(range(count))


def hierarchical_sum(value, win_count):
    if win_count % 2:
        return lax.psum(value, "win")
    near = [[2 * i, 2 * i + 1] for i in range(win_count // 2)]
    far = [list(range(c, win_count, 2)) for c in range(2)]
    part = lax.psum_scatter(value, "win", scatter_dimension=1, tiled=True, axis_index_groups=near)
    part = lax.psum(part, "win", axis_index_groups=far)
    return lax.all_gather(part, "win", axis=1, tiled=True, axis_index_groups=near)


def make_per_device(ring):
    count = len(ring)
    block_of = [0] * count
    for place, device in enumerate(ring):
        block_of[device] = place
    to_prev = [(ring[r], ring[(r - 1) % count]) for r in range(count)]
    to_next = [(ring[r], ring[(r + 1) % count]) for r in range(count)]
    to_owner = [(b, ring[b]) for b in range(count)]

    def per_device(records, pair_first, pair_offset, owners):
        pair_data = jnp.stack([pair_first, pair_offset, owners[:, 0]], axis=0)
        tile_count = lax.axis_size("tile")
        win_count = lax.axis_size("win")
        length = records.shape[1] * tile_count
        seg_total = records.shape[0] * win_count
        block = records.shape[2] // tile_count
        half = block // 2
        forward = forward_matrix(length).reshape(length, tile_count, records.shape[1])
        my_first, my_offset, my_owners = lax.ppermute(pair_data, "tile", to_owner)
        channel_ids = jnp.arange(2 * block, dtype=jnp.int32)[:, None]
        pick_first = (channel_ids == my_first[None, :]).astype(jnp.bfloat16)
        pick_second = (channel_ids == (my_first + my_offset)[None, :]).astype(jnp.bfloat16)
        cross = None
        for segment in range(records.shape[0]):
            pieces = []
            for b in block_of:
                low = b * block + half
                if low + block <= records.shape[2]:
                    pieces.append(records[segment, :, low:low + block])
                else:
                    pieces.append(
                        jnp.concatenate(
                            [records[segment, :, low:], records[segment, :, : low + block - records.shape[2]]],
                            axis=1,
                        )
                    )
            outgoing = jnp.stack(pieces, axis=0)
            received = lax.all_to_all(outgoing, "tile", split_axis=0, concat_axis=0, tiled=True)
            spectra = jnp.einsum("fjm,jmc->fc", forward, received, preferred_element_type=jnp.float32)
            whitened = whiten(spectra, BAND)
            from_prev = lax.ppermute(whitened[:, half:], "tile", to_next)
            from_next = lax.ppermute(whitened[:, :half], "tile", to_prev)
            joined = jnp.concatenate([from_prev, whitened, from_next], axis=1)
            first_part = jnp.dot(joined, pick_first, preferred_element_type=jnp.float32)
            second_part = jnp.dot(joined, pick_second, preferred_element_type=jnp.float32)
            term = cross_terms(first_part, second_part)
            cross = term if cross is None else cross + term
        lag_count = length // win_count
        stacked = hierarchical_sum(cross, win_count)
        inverse = inverse_matrix(length, lax.axis_index("win") * lag_count, lag_count, seg_total)
        correlation = jnp.dot(inverse, stacked, precision=lax.Precision.HIGH)
        capacity = 5 * pair_first.shape[0] // (2 * tile_count)
        chooser = bucket_select(my_owners, tile_count, capacity)
        picked = lax.dot_general(
            chooser,
            correlation.astype(jnp.bfloat16),
            (((1,), (1,)), ((), ())),
            preferred_element_type=jnp.float32,
        )
        buckets = picked.astype(jnp.bfloat16).reshape(tile_count, capacity, lag_count)
        received = lax.all_to_all(buckets, "tile", split_axis=0, concat_axis=0, tiled=True)
        ordered = jnp.stack([received[d] for d in ring], axis=0)
        return ordered[None]

    return per_device


def solution(mesh):
    placed = (P("win", "tile", None), P("tile"), P("tile"), P("tile", None))
    return jax.shard_map(
        make_per_device(tile_ring(mesh)),
        mesh=mesh,
        in_specs=placed,
        out_specs=P("tile", None, None, "win"),
        check_vma=False,
    )
```

```python
import math

import jax
import jax.numpy as jnp
from jax import lax
from jax.sharding import PartitionSpec as P

BAND = 64


power_floor = 1e-06


def phase_table(rows, col_count, length):
    split = 64 if col_count % 64 == 0 else 1
    coarse = jnp.arange(col_count // split, dtype=jnp.int32) * split
    fine = jnp.arange(split, dtype=jnp.int32)
    scale = 2.0 * math.pi / length
    coarse_angle = ((rows[:, None] * coarse[None, :]) % length).astype(jnp.float32) * scale
    fine_angle = ((rows[:, None] * fine[None, :]) % length).astype(jnp.float32) * scale
    c_hi, s_hi = jnp.cos(coarse_angle)[:, :, None], jnp.sin(coarse_angle)[:, :, None]
    c_lo, s_lo = jnp.cos(fine_angle)[:, None, :], jnp.sin(fine_angle)[:, None, :]
    shape = (rows.shape[0], col_count)
    cosine = (c_hi * c_lo - s_hi * s_lo).reshape(shape)
    sine = (s_hi * c_lo + c_hi * s_lo).reshape(shape)
    return cosine, sine


def forward_matrix(length):
    cosine, sine = phase_table(jnp.arange(length // 2, dtype=jnp.int32), length, length)
    return jnp.concatenate([cosine, -sine], axis=0).astype(jnp.bfloat16)


def inverse_matrix(length, first_lag, lag_count, seg_total):
    half_bins = length // 2
    lags = jnp.arange(lag_count, dtype=jnp.int32) + first_lag
    cosine, sine = phase_table(lags, half_bins, length)
    bin_index = jnp.arange(half_bins)[None, :]
    weights = jnp.where(bin_index == 0, 1.0, 2.0).astype(jnp.float32) * (
        1.0 / math.sqrt(half_bins * seg_total)
    )
    return jnp.concatenate([weights * cosine, -weights * sine], axis=1)


def whiten(spectra, band_width):
    half_bins = spectra.shape[-2] // 2
    real_rows = spectra[..., :half_bins, :]
    imaginary = spectra[..., half_bins:, :]
    energy = real_rows * real_rows + imaginary * imaginary
    grouped = energy.shape[:-2] + (half_bins // band_width, band_width, energy.shape[-1])
    band_power = jnp.mean(energy.reshape(grouped), axis=-2, keepdims=True)
    inverse_rms = jnp.broadcast_to(lax.rsqrt(band_power + power_floor), grouped).reshape(
        energy.shape
    )
    return (spectra * jnp.concatenate([inverse_rms, inverse_rms], axis=-2)).astype(jnp.bfloat16)


def cross_terms(first_part, second_part):
    half_bins = first_part.shape[-2] // 2
    first_real = first_part[..., :half_bins, :].astype(jnp.float32)
    first_imag = first_part[..., half_bins:, :].astype(jnp.float32)
    second_real = second_part[..., :half_bins, :].astype(jnp.float32)
    second_imag = second_part[..., half_bins:, :].astype(jnp.float32)
    real_sum = first_real * second_real + first_imag * second_imag
    imag_sum = first_imag * second_real - first_real * second_imag
    return jnp.concatenate([real_sum, imag_sum], axis=-2)


def bucket_select(owner_ids, owner_count, capacity):
    onehot = (owner_ids[:, None] == jnp.arange(owner_count, dtype=jnp.int32)[None, :]).astype(
        jnp.int32
    )
    slot_rank = jnp.sum((jnp.cumsum(onehot, axis=0, dtype=jnp.int32) - 1) * onehot, axis=1)
    slot_id = owner_ids * capacity + slot_rank
    return (
        slot_id[None, :] == jnp.arange(owner_count * capacity, dtype=jnp.int32)[:, None]
    ).astype(jnp.bfloat16)


def tile_ring(mesh):
    count = mesh.shape["tile"]
    try:
        column = mesh.devices.reshape(count, -1)[:, 0]
        spots = [tuple(int(c) for c in d.coords) for d in column]
    except (AttributeError, TypeError):
        return list(range(count))
    near = [
        [j for j in range(count) if sum(abs(a - b) for a, b in zip(spots[i], spots[j])) == 1]
        for i in range(count)
    ]
    path, seen, budget = [0], {0}, [20000]

    def extend():
        budget[0] -= 1
        if budget[0] < 0:
            return False
        if len(path) == count:
            return count < 3 or 0 in near[path[-1]]
        options = [j for j in near[path[-1]] if j not in seen]
        options.sort(key=lambda j: sum(1 for k in near[j] if k not in seen))
        for j in options:
            path.append(j)
            seen.add(j)
            if extend():
                return True
            path.pop()
            seen.discard(j)
        return False

    return path if extend() else list(range(count))


def make_per_device(ring):
    count = len(ring)
    block_of = [0] * count
    for place, device in enumerate(ring):
        block_of[device] = place
    to_prev = [(ring[r], ring[(r - 1) % count]) for r in range(count)]
    to_next = [(ring[r], ring[(r + 1) % count]) for r in range(count)]
    to_owner = [(b, ring[b]) for b in range(count)]

    def per_device(records, pair_first, pair_offset, owners):
        pair_data = jnp.stack([pair_first, pair_offset, owners[:, 0]], axis=0)
        tile_count = lax.axis_size("tile")
        win_count = lax.axis_size("win")
        length = records.shape[1] * tile_count
        seg_total = records.shape[0] * win_count
        block = records.shape[2] // tile_count
        half = block // 2
        forward = forward_matrix(length).reshape(length, tile_count, records.shape[1])
        my_first, my_offset, my_owners = lax.ppermute(pair_data, "tile", to_owner)
        channel_ids = jnp.arange(2 * block, dtype=jnp.int32)[:, None]
        pick_first = (channel_ids == my_first[None, :]).astype(jnp.bfloat16)
        pick_second = (channel_ids == (my_first + my_offset)[None, :]).astype(jnp.bfloat16)
        cross = None
        for segment in range(records.shape[0]):
            pieces = []
            for b in block_of:
                low = b * block + half
                if low + block <= records.shape[2]:
                    pieces.append(records[segment, :, low:low + block])
                else:
                    pieces.append(
                        jnp.concatenate(
                            [records[segment, :, low:], records[segment, :, : low + block - records.shape[2]]],
                            axis=1,
                        )
                    )
            outgoing = jnp.stack(pieces, axis=0)
            received = lax.all_to_all(outgoing, "tile", split_axis=0, concat_axis=0, tiled=True)
            spectra = jnp.einsum("fjm,jmc->fc", forward, received, preferred_element_type=jnp.float32)
            whitened = whiten(spectra, BAND)
            from_prev = lax.ppermute(whitened[:, half:], "tile", to_next)
            from_next = lax.ppermute(whitened[:, :half], "tile", to_prev)
            joined = jnp.concatenate([from_prev, whitened, from_next], axis=1)
            first_part = jnp.dot(joined, pick_first, preferred_element_type=jnp.float32)
            second_part = jnp.dot(joined, pick_second, preferred_element_type=jnp.float32)
            term = cross_terms(first_part, second_part)
            cross = term if cross is None else cross + term
        lag_count = length // win_count
        inverse = inverse_matrix(length, 0, length, seg_total)
        partial = jnp.dot(inverse, cross, precision=lax.Precision.HIGH)
        correlation = lax.psum_scatter(partial, "win", scatter_dimension=0, tiled=True)
        capacity = 5 * pair_first.shape[0] // (2 * tile_count)
        chooser = bucket_select(my_owners, tile_count, capacity)
        picked = lax.dot_general(
            chooser,
            correlation.astype(jnp.bfloat16),
            (((1,), (1,)), ((), ())),
            preferred_element_type=jnp.float32,
        )
        buckets = picked.astype(jnp.bfloat16).reshape(tile_count, capacity, lag_count)
        received = lax.all_to_all(buckets, "tile", split_axis=0, concat_axis=0, tiled=True)
        ordered = jnp.stack([received[d] for d in ring], axis=0)
        return ordered[None]

    return per_device


def solution(mesh):
    placed = (P("win", "tile", None), P("tile"), P("tile"), P("tile", None))
    return jax.shard_map(
        make_per_device(tile_ring(mesh)),
        mesh=mesh,
        in_specs=placed,
        out_specs=P("tile", None, None, "win"),
        check_vma=False,
    )
```

```python
import math

import jax
import jax.numpy as jnp
from jax import lax
from jax.sharding import PartitionSpec as P

BAND = 64


power_floor = 1e-06


def phase_table(rows, col_count, length):
    split = 64 if col_count % 64 == 0 else 1
    coarse = jnp.arange(col_count // split, dtype=jnp.int32) * split
    fine = jnp.arange(split, dtype=jnp.int32)
    scale = 2.0 * math.pi / length
    coarse_angle = ((rows[:, None] * coarse[None, :]) % length).astype(jnp.float32) * scale
    fine_angle = ((rows[:, None] * fine[None, :]) % length).astype(jnp.float32) * scale
    c_hi, s_hi = jnp.cos(coarse_angle)[:, :, None], jnp.sin(coarse_angle)[:, :, None]
    c_lo, s_lo = jnp.cos(fine_angle)[:, None, :], jnp.sin(fine_angle)[:, None, :]
    shape = (rows.shape[0], col_count)
    cosine = (c_hi * c_lo - s_hi * s_lo).reshape(shape)
    sine = (s_hi * c_lo + c_hi * s_lo).reshape(shape)
    return cosine, sine


def forward_matrix(length):
    cosine, sine = phase_table(jnp.arange(length // 2, dtype=jnp.int32), length, length)
    return jnp.concatenate([cosine, -sine], axis=0).astype(jnp.bfloat16)


def inverse_matrix(length, first_lag, lag_count, seg_total):
    half_bins = length // 2
    lags = jnp.arange(lag_count, dtype=jnp.int32) + first_lag
    cosine, sine = phase_table(lags, half_bins, length)
    bin_index = jnp.arange(half_bins)[None, :]
    weights = jnp.where(bin_index == 0, 1.0, 2.0).astype(jnp.float32) * (
        1.0 / math.sqrt(half_bins * seg_total)
    )
    return jnp.concatenate([weights * cosine, -weights * sine], axis=1)


def whiten(spectra, band_width):
    half_bins = spectra.shape[-2] // 2
    real_rows = spectra[..., :half_bins, :]
    imaginary = spectra[..., half_bins:, :]
    energy = real_rows * real_rows + imaginary * imaginary
    grouped = energy.shape[:-2] + (half_bins // band_width, band_width, energy.shape[-1])
    band_power = jnp.mean(energy.reshape(grouped), axis=-2, keepdims=True)
    inverse_rms = jnp.broadcast_to(lax.rsqrt(band_power + power_floor), grouped).reshape(
        energy.shape
    )
    return (spectra * jnp.concatenate([inverse_rms, inverse_rms], axis=-2)).astype(jnp.bfloat16)


def cross_terms(first_part, second_part):
    half_bins = first_part.shape[-2] // 2
    first_real = first_part[..., :half_bins, :].astype(jnp.float32)
    first_imag = first_part[..., half_bins:, :].astype(jnp.float32)
    second_real = second_part[..., :half_bins, :].astype(jnp.float32)
    second_imag = second_part[..., half_bins:, :].astype(jnp.float32)
    real_sum = first_real * second_real + first_imag * second_imag
    imag_sum = first_imag * second_real - first_real * second_imag
    return jnp.concatenate([real_sum, imag_sum], axis=-2)


def bucket_select(owner_ids, owner_count, capacity):
    onehot = (owner_ids[:, None] == jnp.arange(owner_count, dtype=jnp.int32)[None, :]).astype(
        jnp.int32
    )
    slot_rank = jnp.sum((jnp.cumsum(onehot, axis=0, dtype=jnp.int32) - 1) * onehot, axis=1)
    slot_id = owner_ids * capacity + slot_rank
    return (
        slot_id[None, :] == jnp.arange(owner_count * capacity, dtype=jnp.int32)[:, None]
    ).astype(jnp.bfloat16)


def tile_ring(mesh):
    count = mesh.shape["tile"]
    try:
        column = mesh.devices.reshape(count, -1)[:, 0]
        spots = [tuple(int(c) for c in d.coords) for d in column]
    except (AttributeError, TypeError):
        return list(range(count))
    near = [
        [j for j in range(count) if sum(abs(a - b) for a, b in zip(spots[i], spots[j])) == 1]
        for i in range(count)
    ]
    path, seen, budget = [0], {0}, [20000]

    def extend():
        budget[0] -= 1
        if budget[0] < 0:
            return False
        if len(path) == count:
            return count < 3 or 0 in near[path[-1]]
        options = [j for j in near[path[-1]] if j not in seen]
        options.sort(key=lambda j: sum(1 for k in near[j] if k not in seen))
        for j in options:
            path.append(j)
            seen.add(j)
            if extend():
                return True
            path.pop()
            seen.discard(j)
        return False

    return path if extend() else list(range(count))


def sum_and_invert(cross, length, lag_count, seg_total, win_count):
    win = lax.axis_index("win")
    if win_count % 2 or win_count & (win_count - 1):
        stacked = lax.psum(cross, "win")
        inverse = inverse_matrix(length, win * lag_count, lag_count, seg_total)
        return jnp.dot(inverse, stacked, precision=lax.Precision.HIGH).astype(jnp.bfloat16)
    core = win % 2
    half = cross.shape[1] // 2
    mine = lax.dynamic_slice_in_dim(cross, core * half, half, axis=1)
    other = lax.dynamic_slice_in_dim(cross, (1 - core) * half, half, axis=1)
    partner = [(w, w ^ 1) for w in range(win_count)]
    total = mine + lax.ppermute(other, "win", partner)
    step = 2
    while step < win_count:
        total = total + lax.ppermute(total, "win", [(w, w ^ step) for w in range(win_count)])
        step *= 2
    inverse = inverse_matrix(length, (win - core) * lag_count, 2 * lag_count, seg_total)
    both = jnp.dot(inverse, total, precision=lax.Precision.HIGH).astype(jnp.bfloat16)
    kept = lax.dynamic_slice_in_dim(both, core * lag_count, lag_count, axis=0)
    given = lax.dynamic_slice_in_dim(both, (1 - core) * lag_count, lag_count, axis=0)
    got = lax.ppermute(given, "win", partner)
    return jnp.where(core == 0, jnp.concatenate([kept, got], axis=1), jnp.concatenate([got, kept], axis=1))


def make_per_device(ring):
    count = len(ring)
    block_of = [0] * count
    for place, device in enumerate(ring):
        block_of[device] = place
    to_prev = [(ring[r], ring[(r - 1) % count]) for r in range(count)]
    to_next = [(ring[r], ring[(r + 1) % count]) for r in range(count)]
    to_owner = [(b, ring[b]) for b in range(count)]

    def per_device(records, pair_first, pair_offset, owners):
        pair_data = jnp.stack([pair_first, pair_offset, owners[:, 0]], axis=0)
        tile_count = lax.axis_size("tile")
        win_count = lax.axis_size("win")
        length = records.shape[1] * tile_count
        seg_total = records.shape[0] * win_count
        block = records.shape[2] // tile_count
        half = block // 2
        forward = forward_matrix(length).reshape(length, tile_count, records.shape[1])
        my_first, my_offset, my_owners = lax.ppermute(pair_data, "tile", to_owner)
        channel_ids = jnp.arange(2 * block, dtype=jnp.int32)[:, None]
        pick_first = (channel_ids == my_first[None, :]).astype(jnp.bfloat16)
        pick_second = (channel_ids == (my_first + my_offset)[None, :]).astype(jnp.bfloat16)
        cross = None
        for segment in range(records.shape[0]):
            pieces = []
            for b in block_of:
                low = b * block + half
                if low + block <= records.shape[2]:
                    pieces.append(records[segment, :, low:low + block])
                else:
                    pieces.append(
                        jnp.concatenate(
                            [records[segment, :, low:], records[segment, :, : low + block - records.shape[2]]],
                            axis=1,
                        )
                    )
            outgoing = jnp.stack(pieces, axis=0)
            received = lax.all_to_all(outgoing, "tile", split_axis=0, concat_axis=0, tiled=True)
            spectra = jnp.einsum("fjm,jmc->fc", forward, received, preferred_element_type=jnp.float32)
            whitened = whiten(spectra, BAND)
            from_prev = lax.ppermute(whitened[:, half:], "tile", to_next)
            from_next = lax.ppermute(whitened[:, :half], "tile", to_prev)
            joined = jnp.concatenate([from_prev, whitened, from_next], axis=1)
            first_part = jnp.dot(joined, pick_first, preferred_element_type=jnp.float32)
            second_part = jnp.dot(joined, pick_second, preferred_element_type=jnp.float32)
            term = cross_terms(first_part, second_part)
            cross = term if cross is None else cross + term
        lag_count = length // win_count
        correlation = sum_and_invert(cross, length, lag_count, seg_total, win_count)
        capacity = 5 * pair_first.shape[0] // (2 * tile_count)
        chooser = bucket_select(my_owners, tile_count, capacity)
        picked = lax.dot_general(
            chooser,
            correlation,
            (((1,), (1,)), ((), ())),
            preferred_element_type=jnp.float32,
        )
        buckets = picked.astype(jnp.bfloat16).reshape(tile_count, capacity, lag_count)
        received = lax.all_to_all(buckets, "tile", split_axis=0, concat_axis=0, tiled=True)
        ordered = jnp.stack([received[d] for d in ring], axis=0)
        return ordered[None]

    return per_device


def solution(mesh):
    placed = (P("win", "tile", None), P("tile"), P("tile"), P("tile", None))
    return jax.shard_map(
        make_per_device(tile_ring(mesh)),
        mesh=mesh,
        in_specs=placed,
        out_specs=P("tile", None, None, "win"),
        check_vma=False,
    )
```

```python
import math

import jax
import jax.numpy as jnp
from jax import lax
from jax.sharding import PartitionSpec as P

BAND = 64


power_floor = 1e-06


def phase_table(rows, col_count, length):
    split = 64 if col_count % 64 == 0 else 1
    coarse = jnp.arange(col_count // split, dtype=jnp.int32) * split
    fine = jnp.arange(split, dtype=jnp.int32)
    scale = 2.0 * math.pi / length
    coarse_angle = ((rows[:, None] * coarse[None, :]) % length).astype(jnp.float32) * scale
    fine_angle = ((rows[:, None] * fine[None, :]) % length).astype(jnp.float32) * scale
    c_hi, s_hi = jnp.cos(coarse_angle)[:, :, None], jnp.sin(coarse_angle)[:, :, None]
    c_lo, s_lo = jnp.cos(fine_angle)[:, None, :], jnp.sin(fine_angle)[:, None, :]
    shape = (rows.shape[0], col_count)
    cosine = (c_hi * c_lo - s_hi * s_lo).reshape(shape)
    sine = (s_hi * c_lo + c_hi * s_lo).reshape(shape)
    return cosine, sine


def forward_matrix(length):
    cosine, sine = phase_table(jnp.arange(length // 2, dtype=jnp.int32), length, length)
    return jnp.concatenate([cosine, -sine], axis=0).astype(jnp.bfloat16)


def inverse_matrix(length, first_lag, lag_count, seg_total):
    half_bins = length // 2
    lags = jnp.arange(lag_count, dtype=jnp.int32) + first_lag
    cosine, sine = phase_table(lags, half_bins, length)
    bin_index = jnp.arange(half_bins)[None, :]
    weights = jnp.where(bin_index == 0, 1.0, 2.0).astype(jnp.float32) * (
        1.0 / math.sqrt(half_bins * seg_total)
    )
    return jnp.concatenate([weights * cosine, -weights * sine], axis=1)


def whiten(spectra, band_width):
    half_bins = spectra.shape[-2] // 2
    real_rows = spectra[..., :half_bins, :]
    imaginary = spectra[..., half_bins:, :]
    energy = real_rows * real_rows + imaginary * imaginary
    grouped = energy.shape[:-2] + (half_bins // band_width, band_width, energy.shape[-1])
    band_power = jnp.mean(energy.reshape(grouped), axis=-2, keepdims=True)
    inverse_rms = jnp.broadcast_to(lax.rsqrt(band_power + power_floor), grouped).reshape(
        energy.shape
    )
    return (spectra * jnp.concatenate([inverse_rms, inverse_rms], axis=-2)).astype(jnp.bfloat16)


def cross_terms(first_part, second_part):
    half_bins = first_part.shape[-2] // 2
    first_real = first_part[..., :half_bins, :].astype(jnp.float32)
    first_imag = first_part[..., half_bins:, :].astype(jnp.float32)
    second_real = second_part[..., :half_bins, :].astype(jnp.float32)
    second_imag = second_part[..., half_bins:, :].astype(jnp.float32)
    real_sum = first_real * second_real + first_imag * second_imag
    imag_sum = first_imag * second_real - first_real * second_imag
    return jnp.concatenate([real_sum, imag_sum], axis=-2)


def bucket_select(owner_ids, owner_count, capacity):
    onehot = (owner_ids[:, None] == jnp.arange(owner_count, dtype=jnp.int32)[None, :]).astype(
        jnp.int32
    )
    slot_rank = jnp.sum((jnp.cumsum(onehot, axis=0, dtype=jnp.int32) - 1) * onehot, axis=1)
    slot_id = owner_ids * capacity + slot_rank
    return (
        slot_id[None, :] == jnp.arange(owner_count * capacity, dtype=jnp.int32)[:, None]
    ).astype(jnp.bfloat16)


def tile_ring(mesh):
    count = mesh.shape["tile"]
    try:
        column = mesh.devices.reshape(count, -1)[:, 0]
        spots = [tuple(int(c) for c in d.coords) for d in column]
    except (AttributeError, TypeError):
        return list(range(count))
    near = [
        [j for j in range(count) if sum(abs(a - b) for a, b in zip(spots[i], spots[j])) == 1]
        for i in range(count)
    ]
    path, seen, budget = [0], {0}, [20000]

    def extend():
        budget[0] -= 1
        if budget[0] < 0:
            return False
        if len(path) == count:
            return count < 3 or 0 in near[path[-1]]
        options = [j for j in near[path[-1]] if j not in seen]
        options.sort(key=lambda j: sum(1 for k in near[j] if k not in seen))
        for j in options:
            path.append(j)
            seen.add(j)
            if extend():
                return True
            path.pop()
            seen.discard(j)
        return False

    return path if extend() else list(range(count))


def sum_and_invert(cross, length, lag_count, seg_total, win_count):
    win = lax.axis_index("win")
    if win_count % 2 or win_count & (win_count - 1):
        stacked = lax.psum(cross, "win")
        inverse = inverse_matrix(length, win * lag_count, lag_count, seg_total)
        return jnp.dot(inverse, stacked, precision=lax.Precision.HIGH).astype(jnp.bfloat16)
    core = win % 2
    half = cross.shape[1] // 2
    mine = lax.dynamic_slice_in_dim(cross, core * half, half, axis=1)
    other = lax.dynamic_slice_in_dim(cross, (1 - core) * half, half, axis=1)
    partner = [(w, w ^ 1) for w in range(win_count)]
    total = mine + lax.ppermute(other, "win", partner)
    step = 2
    while step < win_count:
        total = total + lax.ppermute(total, "win", [(w, w ^ step) for w in range(win_count)])
        step *= 2
    inverse = inverse_matrix(length, (win - core) * lag_count, 2 * lag_count, seg_total)
    both = jnp.dot(inverse, total, precision=lax.Precision.HIGH).astype(jnp.bfloat16)
    kept = lax.dynamic_slice_in_dim(both, core * lag_count, lag_count, axis=0)
    given = lax.dynamic_slice_in_dim(both, (1 - core) * lag_count, lag_count, axis=0)
    got = lax.ppermute(given, "win", partner)
    return jnp.where(core == 0, jnp.concatenate([kept, got], axis=1), jnp.concatenate([got, kept], axis=1))


def make_per_device(ring):
    count = len(ring)
    block_of = [0] * count
    for place, device in enumerate(ring):
        block_of[device] = place
    to_prev = [(ring[r], ring[(r - 1) % count]) for r in range(count)]
    to_next = [(ring[r], ring[(r + 1) % count]) for r in range(count)]
    to_owner = [(b, ring[b]) for b in range(count)]

    def per_device(records, pair_first, pair_offset, owners):
        pair_data = jnp.stack([pair_first, pair_offset, owners[:, 0]], axis=0)
        tile_count = lax.axis_size("tile")
        win_count = lax.axis_size("win")
        length = records.shape[1] * tile_count
        seg_total = records.shape[0] * win_count
        block = records.shape[2] // tile_count
        half = block // 2
        forward = forward_matrix(length).reshape(length, tile_count, records.shape[1])
        my_first, my_offset, my_owners = lax.ppermute(pair_data, "tile", to_owner)
        channel_ids = jnp.arange(2 * block, dtype=jnp.int32)[:, None]
        pick_first = (channel_ids == my_first[None, :]).astype(jnp.bfloat16)
        pick_second = (channel_ids == (my_first + my_offset)[None, :]).astype(jnp.bfloat16)
        cross = None
        arrived = []
        for segment in range(records.shape[0]):
            pieces = []
            for b in block_of:
                low = b * block + half
                if low + block <= records.shape[2]:
                    pieces.append(records[segment, :, low:low + block])
                else:
                    pieces.append(
                        jnp.concatenate(
                            [records[segment, :, low:], records[segment, :, : low + block - records.shape[2]]],
                            axis=1,
                        )
                    )
            outgoing = jnp.stack(pieces, axis=0)
            received = lax.all_to_all(outgoing, "tile", split_axis=0, concat_axis=0, tiled=True)
            if arrived:
                received, _ = lax.optimization_barrier((received, arrived[-1]))
            spectra = jnp.einsum("fjm,jmc->fc", forward, received, preferred_element_type=jnp.float32)
            whitened = whiten(spectra, BAND)
            from_prev = lax.ppermute(whitened[:, half:], "tile", to_next)
            from_next = lax.ppermute(whitened[:, :half], "tile", to_prev)
            arrived.append((from_prev, from_next))
            joined = jnp.concatenate([from_prev, whitened, from_next], axis=1)
            first_part = jnp.dot(joined, pick_first, preferred_element_type=jnp.float32)
            second_part = jnp.dot(joined, pick_second, preferred_element_type=jnp.float32)
            term = cross_terms(first_part, second_part)
            cross = term if cross is None else cross + term
        lag_count = length // win_count
        correlation = sum_and_invert(cross, length, lag_count, seg_total, win_count)
        capacity = 5 * pair_first.shape[0] // (2 * tile_count)
        chooser = bucket_select(my_owners, tile_count, capacity)
        picked = lax.dot_general(
            chooser,
            correlation,
            (((1,), (1,)), ((), ())),
            preferred_element_type=jnp.float32,
        )
        buckets = picked.astype(jnp.bfloat16).reshape(tile_count, capacity, lag_count)
        received = lax.all_to_all(buckets, "tile", split_axis=0, concat_axis=0, tiled=True)
        ordered = jnp.stack([received[d] for d in ring], axis=0)
        return ordered[None]

    return per_device


def solution(mesh):
    placed = (P("win", "tile", None), P("tile"), P("tile"), P("tile", None))
    return jax.shard_map(
        make_per_device(tile_ring(mesh)),
        mesh=mesh,
        in_specs=placed,
        out_specs=P("tile", None, None, "win"),
        check_vma=False,
    )
```

```python
import math

import jax
import jax.numpy as jnp
from jax import lax
from jax.sharding import PartitionSpec as P

BAND = 64


power_floor = 1e-06


def phase_table(rows, col_count, length):
    split = 64 if col_count % 64 == 0 else 1
    coarse = jnp.arange(col_count // split, dtype=jnp.int32) * split
    fine = jnp.arange(split, dtype=jnp.int32)
    scale = 2.0 * math.pi / length
    coarse_angle = ((rows[:, None] * coarse[None, :]) % length).astype(jnp.float32) * scale
    fine_angle = ((rows[:, None] * fine[None, :]) % length).astype(jnp.float32) * scale
    c_hi, s_hi = jnp.cos(coarse_angle)[:, :, None], jnp.sin(coarse_angle)[:, :, None]
    c_lo, s_lo = jnp.cos(fine_angle)[:, None, :], jnp.sin(fine_angle)[:, None, :]
    shape = (rows.shape[0], col_count)
    cosine = (c_hi * c_lo - s_hi * s_lo).reshape(shape)
    sine = (s_hi * c_lo + c_hi * s_lo).reshape(shape)
    return cosine, sine


def forward_matrix(length):
    cosine, sine = phase_table(jnp.arange(length // 2, dtype=jnp.int32), length, length)
    return jnp.concatenate([cosine, -sine], axis=0).astype(jnp.bfloat16)


def inverse_matrix(length, first_lag, lag_count, seg_total):
    half_bins = length // 2
    lags = jnp.arange(lag_count, dtype=jnp.int32) + first_lag
    cosine, sine = phase_table(lags, half_bins, length)
    bin_index = jnp.arange(half_bins)[None, :]
    weights = jnp.where(bin_index == 0, 1.0, 2.0).astype(jnp.float32) * (
        1.0 / math.sqrt(half_bins * seg_total)
    )
    return jnp.concatenate([weights * cosine, -weights * sine], axis=1)


def whiten(spectra, band_width):
    half_bins = spectra.shape[-2] // 2
    real_rows = spectra[..., :half_bins, :]
    imaginary = spectra[..., half_bins:, :]
    energy = real_rows * real_rows + imaginary * imaginary
    grouped = energy.shape[:-2] + (half_bins // band_width, band_width, energy.shape[-1])
    band_power = jnp.mean(energy.reshape(grouped), axis=-2, keepdims=True)
    inverse_rms = jnp.broadcast_to(lax.rsqrt(band_power + power_floor), grouped).reshape(
        energy.shape
    )
    return (spectra * jnp.concatenate([inverse_rms, inverse_rms], axis=-2)).astype(jnp.bfloat16)


def cross_terms(first_part, second_part):
    half_bins = first_part.shape[-2] // 2
    first_real = first_part[..., :half_bins, :].astype(jnp.float32)
    first_imag = first_part[..., half_bins:, :].astype(jnp.float32)
    second_real = second_part[..., :half_bins, :].astype(jnp.float32)
    second_imag = second_part[..., half_bins:, :].astype(jnp.float32)
    real_sum = first_real * second_real + first_imag * second_imag
    imag_sum = first_imag * second_real - first_real * second_imag
    return jnp.concatenate([real_sum, imag_sum], axis=-2)


def bucket_select(owner_ids, owner_count, capacity):
    onehot = (owner_ids[:, None] == jnp.arange(owner_count, dtype=jnp.int32)[None, :]).astype(
        jnp.int32
    )
    slot_rank = jnp.sum((jnp.cumsum(onehot, axis=0, dtype=jnp.int32) - 1) * onehot, axis=1)
    slot_id = owner_ids * capacity + slot_rank
    return (
        slot_id[None, :] == jnp.arange(owner_count * capacity, dtype=jnp.int32)[:, None]
    ).astype(jnp.bfloat16)


def tile_ring(mesh):
    count = mesh.shape["tile"]
    try:
        column = mesh.devices.reshape(count, -1)[:, 0]
        spots = [tuple(int(c) for c in d.coords) for d in column]
    except (AttributeError, TypeError):
        return list(range(count))
    near = [
        [j for j in range(count) if sum(abs(a - b) for a, b in zip(spots[i], spots[j])) == 1]
        for i in range(count)
    ]
    path, seen, budget = [0], {0}, [20000]

    def extend():
        budget[0] -= 1
        if budget[0] < 0:
            return False
        if len(path) == count:
            return count < 3 or 0 in near[path[-1]]
        options = [j for j in near[path[-1]] if j not in seen]
        options.sort(key=lambda j: sum(1 for k in near[j] if k not in seen))
        for j in options:
            path.append(j)
            seen.add(j)
            if extend():
                return True
            path.pop()
            seen.discard(j)
        return False

    return path if extend() else list(range(count))


def sum_and_invert(cross, length, lag_count, seg_total, win_count):
    win = lax.axis_index("win")
    if win_count % 2 or win_count & (win_count - 1):
        stacked = lax.psum(cross, "win")
        inverse = inverse_matrix(length, win * lag_count, lag_count, seg_total)
        return jnp.dot(inverse, stacked, precision=lax.Precision.HIGH).astype(jnp.bfloat16)
    core = win % 2
    chip = win // 2
    half = cross.shape[1] // 2
    mine = lax.dynamic_slice_in_dim(cross, core * half, half, axis=1)
    other = lax.dynamic_slice_in_dim(cross, (1 - core) * half, half, axis=1)
    partner = [(w, w ^ 1) for w in range(win_count)]
    total = mine + lax.ppermute(other, "win", partner)
    inverse = inverse_matrix(length, 0, length, seg_total)
    lags = jnp.dot(inverse, total, precision=lax.Precision.HIGH)
    bit = win_count // 4
    while bit >= 1:
        rows = lags.shape[0] // 2
        upper = (chip // bit) % 2
        keep = lax.dynamic_slice_in_dim(lags, upper * rows, rows, axis=0)
        send = lax.dynamic_slice_in_dim(lags, (1 - upper) * rows, rows, axis=0)
        lags = keep + lax.ppermute(send, "win", [(w, w ^ (2 * bit)) for w in range(win_count)])
        bit //= 2
    both = lags.astype(jnp.bfloat16)
    kept = lax.dynamic_slice_in_dim(both, core * lag_count, lag_count, axis=0)
    given = lax.dynamic_slice_in_dim(both, (1 - core) * lag_count, lag_count, axis=0)
    got = lax.ppermute(given, "win", partner)
    return jnp.where(core == 0, jnp.concatenate([kept, got], axis=1), jnp.concatenate([got, kept], axis=1))


def make_per_device(ring):
    count = len(ring)
    block_of = [0] * count
    for place, device in enumerate(ring):
        block_of[device] = place
    to_prev = [(ring[r], ring[(r - 1) % count]) for r in range(count)]
    to_next = [(ring[r], ring[(r + 1) % count]) for r in range(count)]
    to_owner = [(b, ring[b]) for b in range(count)]

    def per_device(records, pair_first, pair_offset, owners):
        pair_data = jnp.stack([pair_first, pair_offset, owners[:, 0]], axis=0)
        tile_count = lax.axis_size("tile")
        win_count = lax.axis_size("win")
        length = records.shape[1] * tile_count
        seg_total = records.shape[0] * win_count
        block = records.shape[2] // tile_count
        half = block // 2
        forward = forward_matrix(length).reshape(length, tile_count, records.shape[1])
        my_first, my_offset, my_owners = lax.ppermute(pair_data, "tile", to_owner)
        channel_ids = jnp.arange(2 * block, dtype=jnp.int32)[:, None]
        pick_first = (channel_ids == my_first[None, :]).astype(jnp.bfloat16)
        pick_second = (channel_ids == (my_first + my_offset)[None, :]).astype(jnp.bfloat16)
        cross = None
        arrived = []
        for segment in range(records.shape[0]):
            pieces = []
            for b in block_of:
                low = b * block + half
                if low + block <= records.shape[2]:
                    pieces.append(records[segment, :, low:low + block])
                else:
                    pieces.append(
                        jnp.concatenate(
                            [records[segment, :, low:], records[segment, :, : low + block - records.shape[2]]],
                            axis=1,
                        )
                    )
            outgoing = jnp.stack(pieces, axis=0)
            received = lax.all_to_all(outgoing, "tile", split_axis=0, concat_axis=0, tiled=True)
            if arrived:
                received, _ = lax.optimization_barrier((received, arrived[-1]))
            spectra = jnp.einsum("fjm,jmc->fc", forward, received, preferred_element_type=jnp.float32)
            whitened = whiten(spectra, BAND)
            from_prev = lax.ppermute(whitened[:, half:], "tile", to_next)
            from_next = lax.ppermute(whitened[:, :half], "tile", to_prev)
            arrived.append((from_prev, from_next))
            joined = jnp.concatenate([from_prev, whitened, from_next], axis=1)
            first_part = jnp.dot(joined, pick_first, preferred_element_type=jnp.float32)
            second_part = jnp.dot(joined, pick_second, preferred_element_type=jnp.float32)
            term = cross_terms(first_part, second_part)
            cross = term if cross is None else cross + term
        lag_count = length // win_count
        correlation = sum_and_invert(cross, length, lag_count, seg_total, win_count)
        capacity = 5 * pair_first.shape[0] // (2 * tile_count)
        chooser = bucket_select(my_owners, tile_count, capacity)
        picked = lax.dot_general(
            chooser,
            correlation,
            (((1,), (1,)), ((), ())),
            preferred_element_type=jnp.float32,
        )
        buckets = picked.astype(jnp.bfloat16).reshape(tile_count, capacity, lag_count)
        received = lax.all_to_all(buckets, "tile", split_axis=0, concat_axis=0, tiled=True)
        ordered = jnp.stack([received[d] for d in ring], axis=0)
        return ordered[None]

    return per_device


def solution(mesh):
    placed = (P("win", "tile", None), P("tile"), P("tile"), P("tile", None))
    return jax.shard_map(
        make_per_device(tile_ring(mesh)),
        mesh=mesh,
        in_specs=placed,
        out_specs=P("tile", None, None, "win"),
        check_vma=False,
    )
```

```python
import math

import jax
import jax.numpy as jnp
from jax import lax
from jax.sharding import PartitionSpec as P

BAND = 64


power_floor = 1e-06


def phase_table(rows, col_count, length):
    split = 64 if col_count % 64 == 0 else 1
    coarse = jnp.arange(col_count // split, dtype=jnp.int32) * split
    fine = jnp.arange(split, dtype=jnp.int32)
    scale = 2.0 * math.pi / length
    coarse_angle = ((rows[:, None] * coarse[None, :]) % length).astype(jnp.float32) * scale
    fine_angle = ((rows[:, None] * fine[None, :]) % length).astype(jnp.float32) * scale
    c_hi, s_hi = jnp.cos(coarse_angle)[:, :, None], jnp.sin(coarse_angle)[:, :, None]
    c_lo, s_lo = jnp.cos(fine_angle)[:, None, :], jnp.sin(fine_angle)[:, None, :]
    shape = (rows.shape[0], col_count)
    cosine = (c_hi * c_lo - s_hi * s_lo).reshape(shape)
    sine = (s_hi * c_lo + c_hi * s_lo).reshape(shape)
    return cosine, sine


def forward_matrix(length):
    cosine, sine = phase_table(jnp.arange(length // 2, dtype=jnp.int32), length, length)
    return jnp.concatenate([cosine, -sine], axis=0).astype(jnp.bfloat16)


def inverse_matrix(length, first_lag, lag_count, seg_total):
    half_bins = length // 2
    lags = jnp.arange(lag_count, dtype=jnp.int32) + first_lag
    cosine, sine = phase_table(lags, half_bins, length)
    bin_index = jnp.arange(half_bins)[None, :]
    weights = jnp.where(bin_index == 0, 1.0, 2.0).astype(jnp.float32) * (
        1.0 / math.sqrt(half_bins * seg_total)
    )
    return jnp.concatenate([weights * cosine, -weights * sine], axis=1)


def whiten(spectra, band_width):
    half_bins = spectra.shape[-2] // 2
    real_rows = spectra[..., :half_bins, :]
    imaginary = spectra[..., half_bins:, :]
    energy = real_rows * real_rows + imaginary * imaginary
    grouped = energy.shape[:-2] + (half_bins // band_width, band_width, energy.shape[-1])
    band_power = jnp.mean(energy.reshape(grouped), axis=-2, keepdims=True)
    inverse_rms = jnp.broadcast_to(lax.rsqrt(band_power + power_floor), grouped).reshape(
        energy.shape
    )
    return (spectra * jnp.concatenate([inverse_rms, inverse_rms], axis=-2)).astype(jnp.bfloat16)


def cross_terms(first_part, second_part):
    half_bins = first_part.shape[-2] // 2
    first_real = first_part[..., :half_bins, :].astype(jnp.float32)
    first_imag = first_part[..., half_bins:, :].astype(jnp.float32)
    second_real = second_part[..., :half_bins, :].astype(jnp.float32)
    second_imag = second_part[..., half_bins:, :].astype(jnp.float32)
    real_sum = first_real * second_real + first_imag * second_imag
    imag_sum = first_imag * second_real - first_real * second_imag
    return jnp.concatenate([real_sum, imag_sum], axis=-2)


def bucket_select(owner_ids, owner_count, capacity):
    onehot = (owner_ids[:, None] == jnp.arange(owner_count, dtype=jnp.int32)[None, :]).astype(
        jnp.int32
    )
    slot_rank = jnp.sum((jnp.cumsum(onehot, axis=0, dtype=jnp.int32) - 1) * onehot, axis=1)
    slot_id = owner_ids * capacity + slot_rank
    return (
        slot_id[None, :] == jnp.arange(owner_count * capacity, dtype=jnp.int32)[:, None]
    ).astype(jnp.bfloat16)


def tile_ring(mesh):
    count = mesh.shape["tile"]
    try:
        column = mesh.devices.reshape(count, -1)[:, 0]
        spots = [tuple(int(c) for c in d.coords) for d in column]
    except (AttributeError, TypeError):
        return list(range(count))
    near = [
        [j for j in range(count) if sum(abs(a - b) for a, b in zip(spots[i], spots[j])) == 1]
        for i in range(count)
    ]
    path, seen, budget = [0], {0}, [20000]

    def extend():
        budget[0] -= 1
        if budget[0] < 0:
            return False
        if len(path) == count:
            return count < 3 or 0 in near[path[-1]]
        options = [j for j in near[path[-1]] if j not in seen]
        options.sort(key=lambda j: sum(1 for k in near[j] if k not in seen))
        for j in options:
            path.append(j)
            seen.add(j)
            if extend():
                return True
            path.pop()
            seen.discard(j)
        return False

    return path if extend() else list(range(count))


def sum_and_invert(cross, length, lag_count, seg_total, win_count, lag_start):
    win = lax.axis_index("win")
    if win_count % 2 or win_count & (win_count - 1):
        stacked = lax.psum(cross, "win")
        inverse = inverse_matrix(length, win * lag_count, lag_count, seg_total)
        return jnp.dot(inverse, stacked, precision=lax.Precision.HIGH).astype(jnp.bfloat16)
    core = win % 2
    chip = win // 2
    half = cross.shape[1] // 2
    mine = lax.dynamic_slice_in_dim(cross, core * half, half, axis=1)
    other = lax.dynamic_slice_in_dim(cross, (1 - core) * half, half, axis=1)
    partner = [(w, w ^ 1) for w in range(win_count)]
    total = mine + lax.ppermute(other, "win", partner)
    inverse = inverse_matrix(length, lag_start, length, seg_total)
    lags = jnp.dot(inverse, total, precision=lax.Precision.HIGH)
    bit = win_count // 4
    while bit >= 1:
        rows = lags.shape[0] // 2
        upper = (chip // bit) % 2
        keep = lax.dynamic_slice_in_dim(lags, upper * rows, rows, axis=0)
        send = lax.dynamic_slice_in_dim(lags, (1 - upper) * rows, rows, axis=0)
        lags = keep + lax.ppermute(send, "win", [(w, w ^ (2 * bit)) for w in range(win_count)])
        bit //= 2
    both = lags.astype(jnp.bfloat16)
    kept = lax.dynamic_slice_in_dim(both, core * lag_count, lag_count, axis=0)
    given = lax.dynamic_slice_in_dim(both, (1 - core) * lag_count, lag_count, axis=0)
    got = lax.ppermute(given, "win", partner)
    return jnp.where(core == 0, jnp.concatenate([kept, got], axis=1), jnp.concatenate([got, kept], axis=1))


def make_per_device(ring):
    count = len(ring)
    block_of = [0] * count
    for place, device in enumerate(ring):
        block_of[device] = place
    to_prev = [(ring[r], ring[(r - 1) % count]) for r in range(count)]
    to_next = [(ring[r], ring[(r + 1) % count]) for r in range(count)]
    to_owner = [(b, ring[b]) for b in range(count)]

    def per_device(records, pair_first, pair_offset, owners):
        pair_data = jnp.stack([pair_first, pair_offset, owners[:, 0]], axis=0)
        tile_count = lax.axis_size("tile")
        win_count = lax.axis_size("win")
        length = records.shape[1] * tile_count
        seg_total = records.shape[0] * win_count
        block = records.shape[2] // tile_count
        half = block // 2
        forward = forward_matrix(length).reshape(length, tile_count, records.shape[1])
        my_first, my_offset, my_owners = lax.ppermute(pair_data, "tile", to_owner)
        channel_ids = jnp.arange(2 * block, dtype=jnp.int32)[:, None]
        pick_first = (channel_ids == my_first[None, :]).astype(jnp.bfloat16)
        pick_second = (channel_ids == (my_first + my_offset)[None, :]).astype(jnp.bfloat16)
        cross = None
        arrived = []
        for segment in range(records.shape[0]):
            pieces = []
            for b in block_of:
                low = b * block + half
                if low + block <= records.shape[2]:
                    pieces.append(records[segment, :, low:low + block])
                else:
                    pieces.append(
                        jnp.concatenate(
                            [records[segment, :, low:], records[segment, :, : low + block - records.shape[2]]],
                            axis=1,
                        )
                    )
            outgoing = jnp.stack(pieces, axis=0)
            received = lax.all_to_all(outgoing, "tile", split_axis=0, concat_axis=0, tiled=True)
            if arrived:
                received, _ = lax.optimization_barrier((received, arrived[-1]))
            spectra = jnp.einsum("fjm,jmc->fc", forward, received, preferred_element_type=jnp.float32)
            whitened = whiten(spectra, BAND)
            from_prev = lax.ppermute(whitened[:, half:], "tile", to_next)
            from_next = lax.ppermute(whitened[:, :half], "tile", to_prev)
            if segment == 0:
                lag_start, _ = lax.optimization_barrier((jnp.int32(0), whitened))
            arrived.append((from_prev, from_next))
            joined = jnp.concatenate([from_prev, whitened, from_next], axis=1)
            first_part = jnp.dot(joined, pick_first, preferred_element_type=jnp.float32)
            second_part = jnp.dot(joined, pick_second, preferred_element_type=jnp.float32)
            term = cross_terms(first_part, second_part)
            cross = term if cross is None else cross + term
        lag_count = length // win_count
        correlation = sum_and_invert(cross, length, lag_count, seg_total, win_count, lag_start)
        capacity = 5 * pair_first.shape[0] // (2 * tile_count)
        chooser = bucket_select(my_owners, tile_count, capacity)
        picked = lax.dot_general(
            chooser,
            correlation,
            (((1,), (1,)), ((), ())),
            preferred_element_type=jnp.float32,
        )
        buckets = picked.astype(jnp.bfloat16).reshape(tile_count, capacity, lag_count)
        received = lax.all_to_all(buckets, "tile", split_axis=0, concat_axis=0, tiled=True)
        ordered = jnp.stack([received[d] for d in ring], axis=0)
        return ordered[None]

    return per_device


def solution(mesh):
    placed = (P("win", "tile", None), P("tile"), P("tile"), P("tile", None))
    return jax.shard_map(
        make_per_device(tile_ring(mesh)),
        mesh=mesh,
        in_specs=placed,
        out_specs=P("tile", None, None, "win"),
        check_vma=False,
    )
```

```python
import math

import jax
import jax.numpy as jnp
from jax import lax
from jax.experimental import pallas as pl
from jax.sharding import PartitionSpec as P

BAND = 64


power_floor = 1e-06


def phase_table(rows, col_count, length):
    split = 64 if col_count % 64 == 0 else 1
    coarse = jnp.arange(col_count // split, dtype=jnp.int32) * split
    fine = jnp.arange(split, dtype=jnp.int32)
    scale = 2.0 * math.pi / length
    coarse_angle = ((rows[:, None] * coarse[None, :]) % length).astype(jnp.float32) * scale
    fine_angle = ((rows[:, None] * fine[None, :]) % length).astype(jnp.float32) * scale
    c_hi, s_hi = jnp.cos(coarse_angle)[:, :, None], jnp.sin(coarse_angle)[:, :, None]
    c_lo, s_lo = jnp.cos(fine_angle)[:, None, :], jnp.sin(fine_angle)[:, None, :]
    shape = (rows.shape[0], col_count)
    cosine = (c_hi * c_lo - s_hi * s_lo).reshape(shape)
    sine = (s_hi * c_lo + c_hi * s_lo).reshape(shape)
    return cosine, sine


def forward_matrix(length):
    cosine, sine = phase_table(jnp.arange(length // 2, dtype=jnp.int32), length, length)
    return jnp.concatenate([cosine, -sine], axis=0).astype(jnp.bfloat16)


def inverse_matrix(length, first_lag, lag_count, seg_total):
    half_bins = length // 2
    lags = jnp.arange(lag_count, dtype=jnp.int32) + first_lag
    cosine, sine = phase_table(lags, half_bins, length)
    bin_index = jnp.arange(half_bins)[None, :]
    weights = jnp.where(bin_index == 0, 1.0, 2.0).astype(jnp.float32) * (
        1.0 / math.sqrt(half_bins * seg_total)
    )
    return jnp.concatenate([weights * cosine, -weights * sine], axis=1)


def whiten(spectra, band_width):
    half_bins = spectra.shape[-2] // 2
    real_rows = spectra[..., :half_bins, :]
    imaginary = spectra[..., half_bins:, :]
    energy = real_rows * real_rows + imaginary * imaginary
    grouped = energy.shape[:-2] + (half_bins // band_width, band_width, energy.shape[-1])
    band_power = jnp.mean(energy.reshape(grouped), axis=-2, keepdims=True)
    inverse_rms = jnp.broadcast_to(lax.rsqrt(band_power + power_floor), grouped).reshape(
        energy.shape
    )
    return (spectra * jnp.concatenate([inverse_rms, inverse_rms], axis=-2)).astype(jnp.bfloat16)


def cross_terms(first_part, second_part):
    half_bins = first_part.shape[-2] // 2
    first_real = first_part[..., :half_bins, :].astype(jnp.float32)
    first_imag = first_part[..., half_bins:, :].astype(jnp.float32)
    second_real = second_part[..., :half_bins, :].astype(jnp.float32)
    second_imag = second_part[..., half_bins:, :].astype(jnp.float32)
    real_sum = first_real * second_real + first_imag * second_imag
    imag_sum = first_imag * second_real - first_real * second_imag
    return jnp.concatenate([real_sum, imag_sum], axis=-2)


def bucket_select(owner_ids, owner_count, capacity):
    onehot = (owner_ids[:, None] == jnp.arange(owner_count, dtype=jnp.int32)[None, :]).astype(
        jnp.int32
    )
    slot_rank = jnp.sum((jnp.cumsum(onehot, axis=0, dtype=jnp.int32) - 1) * onehot, axis=1)
    slot_id = owner_ids * capacity + slot_rank
    return (
        slot_id[None, :] == jnp.arange(owner_count * capacity, dtype=jnp.int32)[:, None]
    ).astype(jnp.bfloat16)


def tile_ring(mesh):
    count = mesh.shape["tile"]
    try:
        column = mesh.devices.reshape(count, -1)[:, 0]
        spots = [tuple(int(c) for c in d.coords) for d in column]
    except (AttributeError, TypeError):
        return list(range(count))
    near = [
        [j for j in range(count) if sum(abs(a - b) for a, b in zip(spots[i], spots[j])) == 1]
        for i in range(count)
    ]
    path, seen, budget = [0], {0}, [20000]

    def extend():
        budget[0] -= 1
        if budget[0] < 0:
            return False
        if len(path) == count:
            return count < 3 or 0 in near[path[-1]]
        options = [j for j in near[path[-1]] if j not in seen]
        options.sort(key=lambda j: sum(1 for k in near[j] if k not in seen))
        for j in options:
            path.append(j)
            seen.add(j)
            if extend():
                return True
            path.pop()
            seen.discard(j)
        return False

    return path if extend() else list(range(count))


def sum_and_invert(cross, length, lag_count, seg_total, win_count, lag_start):
    win = lax.axis_index("win")
    if win_count % 2 or win_count & (win_count - 1):
        stacked = lax.psum(cross, "win")
        inverse = inverse_matrix(length, win * lag_count, lag_count, seg_total)
        return jnp.dot(inverse, stacked, precision=lax.Precision.HIGH).astype(jnp.bfloat16)
    core = win % 2
    chip = win // 2
    half = cross.shape[1] // 2
    mine = lax.dynamic_slice_in_dim(cross, core * half, half, axis=1)
    other = lax.dynamic_slice_in_dim(cross, (1 - core) * half, half, axis=1)
    partner = [(w, w ^ 1) for w in range(win_count)]
    total = mine + lax.ppermute(other, "win", partner)
    inverse = inverse_matrix(length, lag_start, length, seg_total)
    lags = jnp.dot(inverse, total, precision=lax.Precision.HIGH)
    bit = win_count // 4
    while bit >= 1:
        rows = lags.shape[0] // 2
        upper = (chip // bit) % 2
        keep = lax.dynamic_slice_in_dim(lags, upper * rows, rows, axis=0)
        send = lax.dynamic_slice_in_dim(lags, (1 - upper) * rows, rows, axis=0)
        lags = keep + lax.ppermute(send, "win", [(w, w ^ (2 * bit)) for w in range(win_count)])
        bit //= 2
    both = lags.astype(jnp.bfloat16)
    kept = lax.dynamic_slice_in_dim(both, core * lag_count, lag_count, axis=0)
    given = lax.dynamic_slice_in_dim(both, (1 - core) * lag_count, lag_count, axis=0)
    got = lax.ppermute(given, "win", partner)
    return jnp.where(core == 0, jnp.concatenate([kept, got], axis=1), jnp.concatenate([got, kept], axis=1))


def lay_out_blocks(records, block_of, block, half):
    segs, rows, width = records.shape
    parts = len(block_of)

    def kernel(src, dst):
        for place, b in enumerate(block_of):
            low = b * block + half
            if low + block <= width:
                dst[0, place] = src[0, :, low:low + block]
            else:
                dst[0, place, :, : width - low] = src[0, :, low:]
                dst[0, place, :, width - low:] = src[0, :, : low + block - width]

    return pl.pallas_call(
        kernel,
        out_shape=jax.ShapeDtypeStruct((segs, parts, rows, block), records.dtype),
        grid=(segs,),
        in_specs=[pl.BlockSpec((1, rows, width), lambda s: (s, 0, 0))],
        out_specs=pl.BlockSpec((1, parts, rows, block), lambda s: (s, 0, 0, 0)),
    )(records)


def make_per_device(ring):
    count = len(ring)
    block_of = [0] * count
    for place, device in enumerate(ring):
        block_of[device] = place
    to_prev = [(ring[r], ring[(r - 1) % count]) for r in range(count)]
    to_next = [(ring[r], ring[(r + 1) % count]) for r in range(count)]
    to_owner = [(b, ring[b]) for b in range(count)]

    def per_device(records, pair_first, pair_offset, owners):
        pair_data = jnp.stack([pair_first, pair_offset, owners[:, 0]], axis=0)
        tile_count = lax.axis_size("tile")
        win_count = lax.axis_size("win")
        length = records.shape[1] * tile_count
        seg_total = records.shape[0] * win_count
        block = records.shape[2] // tile_count
        half = block // 2
        forward = forward_matrix(length).reshape(length, tile_count, records.shape[1])
        my_first, my_offset, my_owners = lax.ppermute(pair_data, "tile", to_owner)
        channel_ids = jnp.arange(2 * block, dtype=jnp.int32)[:, None]
        pick_first = (channel_ids == my_first[None, :]).astype(jnp.bfloat16)
        pick_second = (channel_ids == (my_first + my_offset)[None, :]).astype(jnp.bfloat16)
        cross = None
        arrived = []
        laid_out = lay_out_blocks(records, block_of, block, half)
        for segment in range(records.shape[0]):
            outgoing = laid_out[segment]
            received = lax.all_to_all(outgoing, "tile", split_axis=0, concat_axis=0, tiled=True)
            if arrived:
                received, _ = lax.optimization_barrier((received, arrived[-1]))
            spectra = jnp.einsum("fjm,jmc->fc", forward, received, preferred_element_type=jnp.float32)
            whitened = whiten(spectra, BAND)
            from_prev = lax.ppermute(whitened[:, half:], "tile", to_next)
            from_next = lax.ppermute(whitened[:, :half], "tile", to_prev)
            if segment == 0:
                lag_start, _ = lax.optimization_barrier((jnp.int32(0), whitened))
            arrived.append((from_prev, from_next))
            joined = jnp.concatenate([from_prev, whitened, from_next], axis=1)
            first_part = jnp.dot(joined, pick_first, preferred_element_type=jnp.float32)
            second_part = jnp.dot(joined, pick_second, preferred_element_type=jnp.float32)
            term = cross_terms(first_part, second_part)
            cross = term if cross is None else cross + term
        lag_count = length // win_count
        correlation = sum_and_invert(cross, length, lag_count, seg_total, win_count, lag_start)
        capacity = 5 * pair_first.shape[0] // (2 * tile_count)
        chooser = bucket_select(my_owners, tile_count, capacity)
        picked = lax.dot_general(
            chooser,
            correlation,
            (((1,), (1,)), ((), ())),
            preferred_element_type=jnp.float32,
        )
        buckets = picked.astype(jnp.bfloat16).reshape(tile_count, capacity, lag_count)
        received = lax.all_to_all(buckets, "tile", split_axis=0, concat_axis=0, tiled=True)
        ordered = jnp.stack([received[d] for d in ring], axis=0)
        return ordered[None]

    return per_device


def solution(mesh):
    placed = (P("win", "tile", None), P("tile"), P("tile"), P("tile", None))
    return jax.shard_map(
        make_per_device(tile_ring(mesh)),
        mesh=mesh,
        in_specs=placed,
        out_specs=P("tile", None, None, "win"),
        check_vma=False,
    )
```

```python
import math

import jax
import jax.numpy as jnp
from jax import lax
from jax.experimental import pallas as pl
from jax.sharding import PartitionSpec as P

BAND = 64


power_floor = 1e-06


def phase_table(rows, col_count, length):
    split = 64 if col_count % 64 == 0 else 1
    coarse = jnp.arange(col_count // split, dtype=jnp.int32) * split
    fine = jnp.arange(split, dtype=jnp.int32)
    scale = 2.0 * math.pi / length
    coarse_angle = ((rows[:, None] * coarse[None, :]) % length).astype(jnp.float32) * scale
    fine_angle = ((rows[:, None] * fine[None, :]) % length).astype(jnp.float32) * scale
    c_hi, s_hi = jnp.cos(coarse_angle)[:, :, None], jnp.sin(coarse_angle)[:, :, None]
    c_lo, s_lo = jnp.cos(fine_angle)[:, None, :], jnp.sin(fine_angle)[:, None, :]
    shape = (rows.shape[0], col_count)
    cosine = (c_hi * c_lo - s_hi * s_lo).reshape(shape)
    sine = (s_hi * c_lo + c_hi * s_lo).reshape(shape)
    return cosine, sine


def forward_matrix(length):
    cosine, sine = phase_table(jnp.arange(length // 2, dtype=jnp.int32), length, length)
    return jnp.concatenate([cosine, -sine], axis=0).astype(jnp.bfloat16)


def inverse_matrix(length, first_lag, lag_count, seg_total):
    half_bins = length // 2
    lags = jnp.arange(lag_count, dtype=jnp.int32) + first_lag
    cosine, sine = phase_table(lags, half_bins, length)
    bin_index = jnp.arange(half_bins)[None, :]
    weights = jnp.where(bin_index == 0, 1.0, 2.0).astype(jnp.float32) * (
        1.0 / math.sqrt(half_bins * seg_total)
    )
    return jnp.concatenate([weights * cosine, -weights * sine], axis=1)


def whiten(spectra, band_width):
    half_bins = spectra.shape[-2] // 2
    real_rows = spectra[..., :half_bins, :]
    imaginary = spectra[..., half_bins:, :]
    energy = real_rows * real_rows + imaginary * imaginary
    grouped = energy.shape[:-2] + (half_bins // band_width, band_width, energy.shape[-1])
    band_power = jnp.mean(energy.reshape(grouped), axis=-2, keepdims=True)
    inverse_rms = jnp.broadcast_to(lax.rsqrt(band_power + power_floor), grouped).reshape(
        energy.shape
    )
    return (spectra * jnp.concatenate([inverse_rms, inverse_rms], axis=-2)).astype(jnp.bfloat16)


def cross_terms(first_part, second_part):
    half_bins = first_part.shape[-2] // 2
    first_real = first_part[..., :half_bins, :].astype(jnp.float32)
    first_imag = first_part[..., half_bins:, :].astype(jnp.float32)
    second_real = second_part[..., :half_bins, :].astype(jnp.float32)
    second_imag = second_part[..., half_bins:, :].astype(jnp.float32)
    real_sum = first_real * second_real + first_imag * second_imag
    imag_sum = first_imag * second_real - first_real * second_imag
    return jnp.concatenate([real_sum, imag_sum], axis=-2)


def bucket_select(owner_ids, owner_count, capacity):
    onehot = (owner_ids[:, None] == jnp.arange(owner_count, dtype=jnp.int32)[None, :]).astype(
        jnp.int32
    )
    slot_rank = jnp.sum((jnp.cumsum(onehot, axis=0, dtype=jnp.int32) - 1) * onehot, axis=1)
    slot_id = owner_ids * capacity + slot_rank
    return (
        slot_id[None, :] == jnp.arange(owner_count * capacity, dtype=jnp.int32)[:, None]
    ).astype(jnp.bfloat16)


def tile_ring(mesh):
    count = mesh.shape["tile"]
    try:
        column = mesh.devices.reshape(count, -1)[:, 0]
        spots = [tuple(int(c) for c in d.coords) for d in column]
    except (AttributeError, TypeError):
        return list(range(count))
    near = [
        [j for j in range(count) if sum(abs(a - b) for a, b in zip(spots[i], spots[j])) == 1]
        for i in range(count)
    ]
    path, seen, budget = [0], {0}, [20000]

    def extend():
        budget[0] -= 1
        if budget[0] < 0:
            return False
        if len(path) == count:
            return count < 3 or 0 in near[path[-1]]
        options = [j for j in near[path[-1]] if j not in seen]
        options.sort(key=lambda j: sum(1 for k in near[j] if k not in seen))
        for j in options:
            path.append(j)
            seen.add(j)
            if extend():
                return True
            path.pop()
            seen.discard(j)
        return False

    return path if extend() else list(range(count))


def sum_and_invert(cross, length, lag_count, seg_total, win_count, lag_start):
    win = lax.axis_index("win")
    if win_count % 2 or win_count & (win_count - 1):
        stacked = lax.psum(cross, "win")
        inverse = inverse_matrix(length, win * lag_count, lag_count, seg_total)
        return jnp.dot(inverse, stacked, precision=lax.Precision.HIGH).astype(jnp.bfloat16)
    core = win % 2
    chip = win // 2
    half = cross.shape[1] // 2
    mine = lax.dynamic_slice_in_dim(cross, core * half, half, axis=1)
    other = lax.dynamic_slice_in_dim(cross, (1 - core) * half, half, axis=1)
    partner = [(w, w ^ 1) for w in range(win_count)]
    total = mine + lax.ppermute(other, "win", partner)
    inverse = inverse_matrix(length, lag_start, length, seg_total)
    lags = jnp.dot(inverse, total, precision=lax.Precision.HIGH)
    bit = win_count // 4
    while bit >= 1:
        rows = lags.shape[0] // 2
        upper = (chip // bit) % 2
        keep = lax.dynamic_slice_in_dim(lags, upper * rows, rows, axis=0)
        send = lax.dynamic_slice_in_dim(lags, (1 - upper) * rows, rows, axis=0)
        lags = keep + lax.ppermute(send, "win", [(w, w ^ (2 * bit)) for w in range(win_count)])
        bit //= 2
    both = lags.astype(jnp.bfloat16)
    kept = lax.dynamic_slice_in_dim(both, core * lag_count, lag_count, axis=0)
    given = lax.dynamic_slice_in_dim(both, (1 - core) * lag_count, lag_count, axis=0)
    got = lax.ppermute(given, "win", partner)
    return jnp.where(core == 0, jnp.concatenate([kept, got], axis=1), jnp.concatenate([got, kept], axis=1))


def lay_out_blocks(records, segment, block_of, block, half):
    segs, rows, width = records.shape
    parts = len(block_of)

    def kernel(src, dst):
        for place, b in enumerate(block_of):
            low = b * block + half
            if low + block <= width:
                dst[place] = src[0, :, low:low + block]
            else:
                dst[place, :, : width - low] = src[0, :, low:]
                dst[place, :, width - low:] = src[0, :, : low + block - width]

    return pl.pallas_call(
        kernel,
        out_shape=jax.ShapeDtypeStruct((parts, rows, block), records.dtype),
        grid=(1,),
        in_specs=[pl.BlockSpec((1, rows, width), lambda i: (segment, 0, 0))],
        out_specs=pl.BlockSpec((parts, rows, block), lambda i: (0, 0, 0)),
    )(records)


def make_per_device(ring):
    count = len(ring)
    block_of = [0] * count
    for place, device in enumerate(ring):
        block_of[device] = place
    to_prev = [(ring[r], ring[(r - 1) % count]) for r in range(count)]
    to_next = [(ring[r], ring[(r + 1) % count]) for r in range(count)]
    to_owner = [(b, ring[b]) for b in range(count)]

    def per_device(records, pair_first, pair_offset, owners):
        pair_data = jnp.stack([pair_first, pair_offset, owners[:, 0]], axis=0)
        tile_count = lax.axis_size("tile")
        win_count = lax.axis_size("win")
        length = records.shape[1] * tile_count
        seg_total = records.shape[0] * win_count
        block = records.shape[2] // tile_count
        half = block // 2
        forward = forward_matrix(length).reshape(length, tile_count, records.shape[1])
        my_first, my_offset, my_owners = lax.ppermute(pair_data, "tile", to_owner)
        channel_ids = jnp.arange(2 * block, dtype=jnp.int32)[:, None]
        pick_first = (channel_ids == my_first[None, :]).astype(jnp.bfloat16)
        pick_second = (channel_ids == (my_first + my_offset)[None, :]).astype(jnp.bfloat16)
        cross = None
        arrived = []
        for segment in range(records.shape[0]):
            outgoing = lay_out_blocks(records, segment, block_of, block, half)
            received = lax.all_to_all(outgoing, "tile", split_axis=0, concat_axis=0, tiled=True)
            if arrived:
                received, _ = lax.optimization_barrier((received, arrived[-1]))
            spectra = jnp.einsum("fjm,jmc->fc", forward, received, preferred_element_type=jnp.float32)
            whitened = whiten(spectra, BAND)
            from_prev = lax.ppermute(whitened[:, half:], "tile", to_next)
            from_next = lax.ppermute(whitened[:, :half], "tile", to_prev)
            if segment == 0:
                lag_start, _ = lax.optimization_barrier((jnp.int32(0), whitened))
            arrived.append((from_prev, from_next))
            joined = jnp.concatenate([from_prev, whitened, from_next], axis=1)
            first_part = jnp.dot(joined, pick_first, preferred_element_type=jnp.float32)
            second_part = jnp.dot(joined, pick_second, preferred_element_type=jnp.float32)
            term = cross_terms(first_part, second_part)
            cross = term if cross is None else cross + term
        lag_count = length // win_count
        correlation = sum_and_invert(cross, length, lag_count, seg_total, win_count, lag_start)
        capacity = 5 * pair_first.shape[0] // (2 * tile_count)
        chooser = bucket_select(my_owners, tile_count, capacity)
        picked = lax.dot_general(
            chooser,
            correlation,
            (((1,), (1,)), ((), ())),
            preferred_element_type=jnp.float32,
        )
        buckets = picked.astype(jnp.bfloat16).reshape(tile_count, capacity, lag_count)
        received = lax.all_to_all(buckets, "tile", split_axis=0, concat_axis=0, tiled=True)
        ordered = jnp.stack([received[d] for d in ring], axis=0)
        return ordered[None]

    return per_device


def solution(mesh):
    placed = (P("win", "tile", None), P("tile"), P("tile"), P("tile", None))
    return jax.shard_map(
        make_per_device(tile_ring(mesh)),
        mesh=mesh,
        in_specs=placed,
        out_specs=P("tile", None, None, "win"),
        check_vma=False,
    )
```

```python
import math

import jax
import jax.numpy as jnp
from jax import lax
from jax.experimental import pallas as pl
from jax.sharding import PartitionSpec as P

BAND = 64


power_floor = 1e-06


def phase_table(rows, col_count, length):
    split = 64 if col_count % 64 == 0 else 1
    coarse = jnp.arange(col_count // split, dtype=jnp.int32) * split
    fine = jnp.arange(split, dtype=jnp.int32)
    scale = 2.0 * math.pi / length
    coarse_angle = ((rows[:, None] * coarse[None, :]) % length).astype(jnp.float32) * scale
    fine_angle = ((rows[:, None] * fine[None, :]) % length).astype(jnp.float32) * scale
    c_hi, s_hi = jnp.cos(coarse_angle)[:, :, None], jnp.sin(coarse_angle)[:, :, None]
    c_lo, s_lo = jnp.cos(fine_angle)[:, None, :], jnp.sin(fine_angle)[:, None, :]
    shape = (rows.shape[0], col_count)
    cosine = (c_hi * c_lo - s_hi * s_lo).reshape(shape)
    sine = (s_hi * c_lo + c_hi * s_lo).reshape(shape)
    return cosine, sine


def forward_matrix(length):
    cosine, sine = phase_table(jnp.arange(length // 2, dtype=jnp.int32), length, length)
    return jnp.concatenate([cosine, -sine], axis=0).astype(jnp.bfloat16)


def inverse_matrix(length, first_lag, lag_count, seg_total):
    half_bins = length // 2
    lags = jnp.arange(lag_count, dtype=jnp.int32) + first_lag
    cosine, sine = phase_table(lags, half_bins, length)
    bin_index = jnp.arange(half_bins)[None, :]
    weights = jnp.where(bin_index == 0, 1.0, 2.0).astype(jnp.float32) * (
        1.0 / math.sqrt(half_bins * seg_total)
    )
    return jnp.concatenate([weights * cosine, -weights * sine], axis=1)


def whiten(spectra, band_width):
    half_bins = spectra.shape[-2] // 2
    real_rows = spectra[..., :half_bins, :]
    imaginary = spectra[..., half_bins:, :]
    energy = real_rows * real_rows + imaginary * imaginary
    grouped = energy.shape[:-2] + (half_bins // band_width, band_width, energy.shape[-1])
    band_power = jnp.mean(energy.reshape(grouped), axis=-2, keepdims=True)
    inverse_rms = jnp.broadcast_to(lax.rsqrt(band_power + power_floor), grouped).reshape(
        energy.shape
    )
    return (spectra * jnp.concatenate([inverse_rms, inverse_rms], axis=-2)).astype(jnp.bfloat16)


def cross_terms(first_part, second_part):
    half_bins = first_part.shape[-2] // 2
    first_real = first_part[..., :half_bins, :].astype(jnp.float32)
    first_imag = first_part[..., half_bins:, :].astype(jnp.float32)
    second_real = second_part[..., :half_bins, :].astype(jnp.float32)
    second_imag = second_part[..., half_bins:, :].astype(jnp.float32)
    real_sum = first_real * second_real + first_imag * second_imag
    imag_sum = first_imag * second_real - first_real * second_imag
    return jnp.concatenate([real_sum, imag_sum], axis=-2)


def bucket_select(owner_ids, owner_count, capacity):
    onehot = (owner_ids[:, None] == jnp.arange(owner_count, dtype=jnp.int32)[None, :]).astype(
        jnp.int32
    )
    slot_rank = jnp.sum((jnp.cumsum(onehot, axis=0, dtype=jnp.int32) - 1) * onehot, axis=1)
    slot_id = owner_ids * capacity + slot_rank
    return (
        slot_id[None, :] == jnp.arange(owner_count * capacity, dtype=jnp.int32)[:, None]
    ).astype(jnp.bfloat16)


def tile_ring(mesh):
    count = mesh.shape["tile"]
    try:
        column = mesh.devices.reshape(count, -1)[:, 0]
        spots = [tuple(int(c) for c in d.coords) for d in column]
    except (AttributeError, TypeError):
        return list(range(count))
    near = [
        [j for j in range(count) if sum(abs(a - b) for a, b in zip(spots[i], spots[j])) == 1]
        for i in range(count)
    ]
    path, seen, budget = [0], {0}, [20000]

    def extend():
        budget[0] -= 1
        if budget[0] < 0:
            return False
        if len(path) == count:
            return count < 3 or 0 in near[path[-1]]
        options = [j for j in near[path[-1]] if j not in seen]
        options.sort(key=lambda j: sum(1 for k in near[j] if k not in seen))
        for j in options:
            path.append(j)
            seen.add(j)
            if extend():
                return True
            path.pop()
            seen.discard(j)
        return False

    return path if extend() else list(range(count))


def inverse_table(length, lag_start):
    cosine, sine = phase_table(jnp.arange(length, dtype=jnp.int32) + lag_start, length // 2, length)
    return jnp.concatenate([cosine, -sine], axis=1)


def sum_and_invert(cross, length, lag_count, seg_total, win_count, table):
    win = lax.axis_index("win")
    if win_count % 2 or win_count & (win_count - 1):
        stacked = lax.psum(cross, "win")
        inverse = inverse_matrix(length, win * lag_count, lag_count, seg_total)
        return jnp.dot(inverse, stacked, precision=lax.Precision.HIGH).astype(jnp.bfloat16)
    core = win % 2
    chip = win // 2
    half = cross.shape[1] // 2
    mine = lax.dynamic_slice_in_dim(cross, core * half, half, axis=1)
    other = lax.dynamic_slice_in_dim(cross, (1 - core) * half, half, axis=1)
    partner = [(w, w ^ 1) for w in range(win_count)]
    total = mine + lax.ppermute(other, "win", partner)
    half_bins = length // 2
    weights = jnp.where(jnp.arange(half_bins) == 0, 1.0, 2.0).astype(jnp.float32) * (
        1.0 / math.sqrt(half_bins * seg_total)
    )
    scaled = total * jnp.concatenate([weights, weights])[:, None]
    lags = jnp.dot(table, scaled, precision=lax.Precision.HIGH)
    bit = win_count // 4
    while bit >= 1:
        rows = lags.shape[0] // 2
        upper = (chip // bit) % 2
        keep = lax.dynamic_slice_in_dim(lags, upper * rows, rows, axis=0)
        send = lax.dynamic_slice_in_dim(lags, (1 - upper) * rows, rows, axis=0)
        lags = keep + lax.ppermute(send, "win", [(w, w ^ (2 * bit)) for w in range(win_count)])
        bit //= 2
    both = lags.astype(jnp.bfloat16)
    kept = lax.dynamic_slice_in_dim(both, core * lag_count, lag_count, axis=0)
    given = lax.dynamic_slice_in_dim(both, (1 - core) * lag_count, lag_count, axis=0)
    got = lax.ppermute(given, "win", partner)
    return jnp.where(core == 0, jnp.concatenate([kept, got], axis=1), jnp.concatenate([got, kept], axis=1))


def lay_out_blocks(records, segment, block_of, block, half):
    segs, rows, width = records.shape
    parts = len(block_of)

    def kernel(src, dst):
        for place, b in enumerate(block_of):
            low = b * block + half
            if low + block <= width:
                dst[place] = src[0, :, low:low + block]
            else:
                dst[place, :, : width - low] = src[0, :, low:]
                dst[place, :, width - low:] = src[0, :, : low + block - width]

    return pl.pallas_call(
        kernel,
        out_shape=jax.ShapeDtypeStruct((parts, rows, block), records.dtype),
        grid=(1,),
        in_specs=[pl.BlockSpec((1, rows, width), lambda i: (segment, 0, 0))],
        out_specs=pl.BlockSpec((parts, rows, block), lambda i: (0, 0, 0)),
    )(records)


def make_per_device(ring):
    count = len(ring)
    block_of = [0] * count
    for place, device in enumerate(ring):
        block_of[device] = place
    to_prev = [(ring[r], ring[(r - 1) % count]) for r in range(count)]
    to_next = [(ring[r], ring[(r + 1) % count]) for r in range(count)]
    to_owner = [(b, ring[b]) for b in range(count)]

    def per_device(records, pair_first, pair_offset, owners):
        pair_data = jnp.stack([pair_first, pair_offset, owners[:, 0]], axis=0)
        tile_count = lax.axis_size("tile")
        win_count = lax.axis_size("win")
        length = records.shape[1] * tile_count
        seg_total = records.shape[0] * win_count
        block = records.shape[2] // tile_count
        half = block // 2
        forward = forward_matrix(length).reshape(length, tile_count, records.shape[1])
        my_first, my_offset, my_owners = lax.ppermute(pair_data, "tile", to_owner)
        channel_ids = jnp.arange(2 * block, dtype=jnp.int32)[:, None]
        pick_first = (channel_ids == my_first[None, :]).astype(jnp.bfloat16)
        pick_second = (channel_ids == (my_first + my_offset)[None, :]).astype(jnp.bfloat16)
        cross = None
        arrived = []
        for segment in range(records.shape[0]):
            outgoing = lay_out_blocks(records, segment, block_of, block, half)
            received = lax.all_to_all(outgoing, "tile", split_axis=0, concat_axis=0, tiled=True)
            if arrived:
                received, _ = lax.optimization_barrier((received, arrived[-1]))
            if segment == min(2, records.shape[0] - 1):
                received, table = lax.optimization_barrier((received, inverse_table(length, lag_start)))
            spectra = jnp.einsum("fjm,jmc->fc", forward, received, preferred_element_type=jnp.float32)
            whitened = whiten(spectra, BAND)
            from_prev = lax.ppermute(whitened[:, half:], "tile", to_next)
            from_next = lax.ppermute(whitened[:, :half], "tile", to_prev)
            if segment == 0:
                lag_start, _ = lax.optimization_barrier((jnp.int32(0), whitened))
            arrived.append((from_prev, from_next))
            joined = jnp.concatenate([from_prev, whitened, from_next], axis=1)
            first_part = jnp.dot(joined, pick_first, preferred_element_type=jnp.float32)
            second_part = jnp.dot(joined, pick_second, preferred_element_type=jnp.float32)
            term = cross_terms(first_part, second_part)
            cross = term if cross is None else cross + term
        lag_count = length // win_count
        correlation = sum_and_invert(cross, length, lag_count, seg_total, win_count, table)
        capacity = 5 * pair_first.shape[0] // (2 * tile_count)
        chooser = bucket_select(my_owners, tile_count, capacity)
        picked = lax.dot_general(
            chooser,
            correlation,
            (((1,), (1,)), ((), ())),
            preferred_element_type=jnp.float32,
        )
        buckets = picked.astype(jnp.bfloat16).reshape(tile_count, capacity, lag_count)
        received = lax.all_to_all(buckets, "tile", split_axis=0, concat_axis=0, tiled=True)
        ordered = jnp.stack([received[d] for d in ring], axis=0)
        return ordered[None]

    return per_device


def solution(mesh):
    placed = (P("win", "tile", None), P("tile"), P("tile"), P("tile", None))
    return jax.shard_map(
        make_per_device(tile_ring(mesh)),
        mesh=mesh,
        in_specs=placed,
        out_specs=P("tile", None, None, "win"),
        check_vma=False,
    )
```

```python
import math

import jax
import jax.numpy as jnp
from jax import lax
from jax.experimental import pallas as pl
from jax.sharding import PartitionSpec as P

BAND = 64


power_floor = 1e-06


def phase_table(rows, col_count, length):
    split = 64 if col_count % 64 == 0 else 1
    coarse = jnp.arange(col_count // split, dtype=jnp.int32) * split
    fine = jnp.arange(split, dtype=jnp.int32)
    scale = 2.0 * math.pi / length
    coarse_angle = ((rows[:, None] * coarse[None, :]) % length).astype(jnp.float32) * scale
    fine_angle = ((rows[:, None] * fine[None, :]) % length).astype(jnp.float32) * scale
    c_hi, s_hi = jnp.cos(coarse_angle)[:, :, None], jnp.sin(coarse_angle)[:, :, None]
    c_lo, s_lo = jnp.cos(fine_angle)[:, None, :], jnp.sin(fine_angle)[:, None, :]
    shape = (rows.shape[0], col_count)
    cosine = (c_hi * c_lo - s_hi * s_lo).reshape(shape)
    sine = (s_hi * c_lo + c_hi * s_lo).reshape(shape)
    return cosine, sine


def forward_matrix(length):
    cosine, sine = phase_table(jnp.arange(length // 2, dtype=jnp.int32), length, length)
    return jnp.concatenate([cosine, -sine], axis=0).astype(jnp.bfloat16)


def inverse_matrix(length, first_lag, lag_count, seg_total):
    half_bins = length // 2
    lags = jnp.arange(lag_count, dtype=jnp.int32) + first_lag
    cosine, sine = phase_table(lags, half_bins, length)
    bin_index = jnp.arange(half_bins)[None, :]
    weights = jnp.where(bin_index == 0, 1.0, 2.0).astype(jnp.float32) * (
        1.0 / math.sqrt(half_bins * seg_total)
    )
    return jnp.concatenate([weights * cosine, -weights * sine], axis=1)


def whiten(spectra, band_width):
    half_bins = spectra.shape[-2] // 2
    real_rows = spectra[..., :half_bins, :]
    imaginary = spectra[..., half_bins:, :]
    energy = real_rows * real_rows + imaginary * imaginary
    grouped = energy.shape[:-2] + (half_bins // band_width, band_width, energy.shape[-1])
    band_power = jnp.mean(energy.reshape(grouped), axis=-2, keepdims=True)
    inverse_rms = jnp.broadcast_to(lax.rsqrt(band_power + power_floor), grouped).reshape(
        energy.shape
    )
    return (spectra * jnp.concatenate([inverse_rms, inverse_rms], axis=-2)).astype(jnp.bfloat16)


def cross_terms(first_part, second_part):
    half_bins = first_part.shape[-2] // 2
    first_real = first_part[..., :half_bins, :].astype(jnp.float32)
    first_imag = first_part[..., half_bins:, :].astype(jnp.float32)
    second_real = second_part[..., :half_bins, :].astype(jnp.float32)
    second_imag = second_part[..., half_bins:, :].astype(jnp.float32)
    real_sum = first_real * second_real + first_imag * second_imag
    imag_sum = first_imag * second_real - first_real * second_imag
    return jnp.concatenate([real_sum, imag_sum], axis=-2)


def bucket_select(owner_ids, owner_count, capacity):
    onehot = (owner_ids[:, None] == jnp.arange(owner_count, dtype=jnp.int32)[None, :]).astype(
        jnp.int32
    )
    slot_rank = jnp.sum((jnp.cumsum(onehot, axis=0, dtype=jnp.int32) - 1) * onehot, axis=1)
    slot_id = owner_ids * capacity + slot_rank
    return (
        slot_id[None, :] == jnp.arange(owner_count * capacity, dtype=jnp.int32)[:, None]
    ).astype(jnp.bfloat16)


def tile_ring(mesh):
    count = mesh.shape["tile"]
    try:
        column = mesh.devices.reshape(count, -1)[:, 0]
        spots = [tuple(int(c) for c in d.coords) for d in column]
    except (AttributeError, TypeError):
        return list(range(count))
    near = [
        [j for j in range(count) if sum(abs(a - b) for a, b in zip(spots[i], spots[j])) == 1]
        for i in range(count)
    ]
    path, seen, budget = [0], {0}, [20000]

    def extend():
        budget[0] -= 1
        if budget[0] < 0:
            return False
        if len(path) == count:
            return count < 3 or 0 in near[path[-1]]
        options = [j for j in near[path[-1]] if j not in seen]
        options.sort(key=lambda j: sum(1 for k in near[j] if k not in seen))
        for j in options:
            path.append(j)
            seen.add(j)
            if extend():
                return True
            path.pop()
            seen.discard(j)
        return False

    return path if extend() else list(range(count))


def inverse_table(length, lag_start):
    return phase_table(jnp.arange(length // 2 + 8, dtype=jnp.int32) + lag_start, length // 2, length)


def sum_and_invert(cross, length, lag_count, seg_total, win_count, table):
    win = lax.axis_index("win")
    if win_count % 2 or win_count & (win_count - 1):
        stacked = lax.psum(cross, "win")
        inverse = inverse_matrix(length, win * lag_count, lag_count, seg_total)
        return jnp.dot(inverse, stacked, precision=lax.Precision.HIGH).astype(jnp.bfloat16)
    core = win % 2
    chip = win // 2
    half = cross.shape[1] // 2
    mine = lax.dynamic_slice_in_dim(cross, core * half, half, axis=1)
    other = lax.dynamic_slice_in_dim(cross, (1 - core) * half, half, axis=1)
    partner = [(w, w ^ 1) for w in range(win_count)]
    total = mine + lax.ppermute(other, "win", partner)
    half_bins = length // 2
    weights = jnp.where(jnp.arange(half_bins) == 0, 1.0, 2.0).astype(jnp.float32) * (
        1.0 / math.sqrt(half_bins * seg_total)
    )
    cos_table, sin_table = table
    scaled = total * jnp.concatenate([weights, weights])[:, None]
    even = jnp.dot(cos_table, scaled[:half_bins], precision=lax.Precision.HIGH)
    odd = jnp.dot(sin_table, scaled[half_bins:], precision=lax.Precision.HIGH)
    lags = jnp.concatenate(
        [
            even[:half_bins] - odd[:half_bins],
            even[half_bins:half_bins + 1] - odd[half_bins:half_bins + 1],
            jnp.flip(even[1:half_bins] + odd[1:half_bins], axis=0),
        ],
        axis=0,
    )
    bit = win_count // 4
    while bit >= 1:
        rows = lags.shape[0] // 2
        upper = (chip // bit) % 2
        keep = lax.dynamic_slice_in_dim(lags, upper * rows, rows, axis=0)
        send = lax.dynamic_slice_in_dim(lags, (1 - upper) * rows, rows, axis=0)
        lags = keep + lax.ppermute(send, "win", [(w, w ^ (2 * bit)) for w in range(win_count)])
        bit //= 2
    both = lags.astype(jnp.bfloat16)
    kept = lax.dynamic_slice_in_dim(both, core * lag_count, lag_count, axis=0)
    given = lax.dynamic_slice_in_dim(both, (1 - core) * lag_count, lag_count, axis=0)
    got = lax.ppermute(given, "win", partner)
    return jnp.where(core == 0, jnp.concatenate([kept, got], axis=1), jnp.concatenate([got, kept], axis=1))


def lay_out_blocks(records, segment, block_of, block, half):
    segs, rows, width = records.shape
    parts = len(block_of)

    def kernel(src, dst):
        for place, b in enumerate(block_of):
            low = b * block + half
            if low + block <= width:
                dst[place] = src[0, :, low:low + block]
            else:
                dst[place, :, : width - low] = src[0, :, low:]
                dst[place, :, width - low:] = src[0, :, : low + block - width]

    return pl.pallas_call(
        kernel,
        out_shape=jax.ShapeDtypeStruct((parts, rows, block), records.dtype),
        grid=(1,),
        in_specs=[pl.BlockSpec((1, rows, width), lambda i: (segment, 0, 0))],
        out_specs=pl.BlockSpec((parts, rows, block), lambda i: (0, 0, 0)),
    )(records)


def make_per_device(ring):
    count = len(ring)
    block_of = [0] * count
    for place, device in enumerate(ring):
        block_of[device] = place
    to_prev = [(ring[r], ring[(r - 1) % count]) for r in range(count)]
    to_next = [(ring[r], ring[(r + 1) % count]) for r in range(count)]
    to_owner = [(b, ring[b]) for b in range(count)]

    def per_device(records, pair_first, pair_offset, owners):
        pair_data = jnp.stack([pair_first, pair_offset, owners[:, 0]], axis=0)
        tile_count = lax.axis_size("tile")
        win_count = lax.axis_size("win")
        length = records.shape[1] * tile_count
        seg_total = records.shape[0] * win_count
        block = records.shape[2] // tile_count
        half = block // 2
        forward = forward_matrix(length).reshape(length, tile_count, records.shape[1])
        my_first, my_offset, my_owners = lax.ppermute(pair_data, "tile", to_owner)
        channel_ids = jnp.arange(2 * block, dtype=jnp.int32)[:, None]
        pick_first = (channel_ids == my_first[None, :]).astype(jnp.bfloat16)
        pick_second = (channel_ids == (my_first + my_offset)[None, :]).astype(jnp.bfloat16)
        cross = None
        arrived = []
        for segment in range(records.shape[0]):
            outgoing = lay_out_blocks(records, segment, block_of, block, half)
            received = lax.all_to_all(outgoing, "tile", split_axis=0, concat_axis=0, tiled=True)
            if arrived:
                received, _ = lax.optimization_barrier((received, arrived[-1]))
            if segment == min(2, records.shape[0] - 1):
                received, table = lax.optimization_barrier((received, inverse_table(length, lag_start)))
            spectra = jnp.einsum("fjm,jmc->fc", forward, received, preferred_element_type=jnp.float32)
            whitened = whiten(spectra, BAND)
            from_prev = lax.ppermute(whitened[:, half:], "tile", to_next)
            from_next = lax.ppermute(whitened[:, :half], "tile", to_prev)
            if segment == 0:
                lag_start, _ = lax.optimization_barrier((jnp.int32(0), whitened))
            arrived.append((from_prev, from_next))
            joined = jnp.concatenate([from_prev, whitened, from_next], axis=1)
            first_part = jnp.dot(joined, pick_first, preferred_element_type=jnp.float32)
            second_part = jnp.dot(joined, pick_second, preferred_element_type=jnp.float32)
            term = cross_terms(first_part, second_part)
            cross = term if cross is None else cross + term
        lag_count = length // win_count
        correlation = sum_and_invert(cross, length, lag_count, seg_total, win_count, table)
        capacity = 5 * pair_first.shape[0] // (2 * tile_count)
        chooser = bucket_select(my_owners, tile_count, capacity)
        picked = lax.dot_general(
            chooser,
            correlation,
            (((1,), (1,)), ((), ())),
            preferred_element_type=jnp.float32,
        )
        buckets = picked.astype(jnp.bfloat16).reshape(tile_count, capacity, lag_count)
        received = lax.all_to_all(buckets, "tile", split_axis=0, concat_axis=0, tiled=True)
        ordered = jnp.stack([received[d] for d in ring], axis=0)
        return ordered[None]

    return per_device


def solution(mesh):
    placed = (P("win", "tile", None), P("tile"), P("tile"), P("tile", None))
    return jax.shard_map(
        make_per_device(tile_ring(mesh)),
        mesh=mesh,
        in_specs=placed,
        out_specs=P("tile", None, None, "win"),
        check_vma=False,
    )
```

```python
import math

import jax
import jax.numpy as jnp
from jax import lax
from jax.experimental import pallas as pl
from jax.sharding import PartitionSpec as P

BAND = 64


power_floor = 1e-06


def phase_table(rows, col_count, length):
    split = 64 if col_count % 64 == 0 else 1
    coarse = jnp.arange(col_count // split, dtype=jnp.int32) * split
    fine = jnp.arange(split, dtype=jnp.int32)
    scale = 2.0 * math.pi / length
    coarse_angle = ((rows[:, None] * coarse[None, :]) % length).astype(jnp.float32) * scale
    fine_angle = ((rows[:, None] * fine[None, :]) % length).astype(jnp.float32) * scale
    c_hi, s_hi = jnp.cos(coarse_angle)[:, :, None], jnp.sin(coarse_angle)[:, :, None]
    c_lo, s_lo = jnp.cos(fine_angle)[:, None, :], jnp.sin(fine_angle)[:, None, :]
    shape = (rows.shape[0], col_count)
    cosine = (c_hi * c_lo - s_hi * s_lo).reshape(shape)
    sine = (s_hi * c_lo + c_hi * s_lo).reshape(shape)
    return cosine, sine


def forward_matrix(length):
    cosine, sine = phase_table(jnp.arange(length // 2, dtype=jnp.int32), length, length)
    return jnp.concatenate([cosine, -sine], axis=0).astype(jnp.bfloat16)


def inverse_matrix(length, first_lag, lag_count, seg_total):
    half_bins = length // 2
    lags = jnp.arange(lag_count, dtype=jnp.int32) + first_lag
    cosine, sine = phase_table(lags, half_bins, length)
    bin_index = jnp.arange(half_bins)[None, :]
    weights = jnp.where(bin_index == 0, 1.0, 2.0).astype(jnp.float32) * (
        1.0 / math.sqrt(half_bins * seg_total)
    )
    return jnp.concatenate([weights * cosine, -weights * sine], axis=1)


def whiten(spectra, band_width):
    half_bins = spectra.shape[-2] // 2
    real_rows = spectra[..., :half_bins, :]
    imaginary = spectra[..., half_bins:, :]
    energy = real_rows * real_rows + imaginary * imaginary
    grouped = energy.shape[:-2] + (half_bins // band_width, band_width, energy.shape[-1])
    band_power = jnp.mean(energy.reshape(grouped), axis=-2, keepdims=True)
    inverse_rms = jnp.broadcast_to(lax.rsqrt(band_power + power_floor), grouped).reshape(
        energy.shape
    )
    return (spectra * jnp.concatenate([inverse_rms, inverse_rms], axis=-2)).astype(jnp.bfloat16)


def cross_terms(first_part, second_part):
    half_bins = first_part.shape[-2] // 2
    first_real = first_part[..., :half_bins, :].astype(jnp.float32)
    first_imag = first_part[..., half_bins:, :].astype(jnp.float32)
    second_real = second_part[..., :half_bins, :].astype(jnp.float32)
    second_imag = second_part[..., half_bins:, :].astype(jnp.float32)
    real_sum = first_real * second_real + first_imag * second_imag
    imag_sum = first_imag * second_real - first_real * second_imag
    return jnp.concatenate([real_sum, imag_sum], axis=-2)


def bucket_select(owner_ids, owner_count, capacity):
    onehot = (owner_ids[:, None] == jnp.arange(owner_count, dtype=jnp.int32)[None, :]).astype(
        jnp.int32
    )
    slot_rank = jnp.sum((jnp.cumsum(onehot, axis=0, dtype=jnp.int32) - 1) * onehot, axis=1)
    slot_id = owner_ids * capacity + slot_rank
    return (
        slot_id[None, :] == jnp.arange(owner_count * capacity, dtype=jnp.int32)[:, None]
    ).astype(jnp.bfloat16)


def tile_ring(mesh):
    count = mesh.shape["tile"]
    try:
        column = mesh.devices.reshape(count, -1)[:, 0]
        spots = [tuple(int(c) for c in d.coords) for d in column]
    except (AttributeError, TypeError):
        return list(range(count))
    near = [
        [j for j in range(count) if sum(abs(a - b) for a, b in zip(spots[i], spots[j])) == 1]
        for i in range(count)
    ]
    path, seen, budget = [0], {0}, [20000]

    def extend():
        budget[0] -= 1
        if budget[0] < 0:
            return False
        if len(path) == count:
            return count < 3 or 0 in near[path[-1]]
        options = [j for j in near[path[-1]] if j not in seen]
        options.sort(key=lambda j: sum(1 for k in near[j] if k not in seen))
        for j in options:
            path.append(j)
            seen.add(j)
            if extend():
                return True
            path.pop()
            seen.discard(j)
        return False

    return path if extend() else list(range(count))


def inverse_table(length, lag_start):
    cosine, sine = phase_table(jnp.arange(length, dtype=jnp.int32) + lag_start, length // 2, length)
    return jnp.concatenate([cosine, -sine], axis=1)


def sum_and_invert(cross, length, lag_count, seg_total, win_count, table):
    win = lax.axis_index("win")
    if win_count % 2 or win_count & (win_count - 1):
        stacked = lax.psum(cross, "win")
        inverse = inverse_matrix(length, win * lag_count, lag_count, seg_total)
        return jnp.dot(inverse, stacked, precision=lax.Precision.HIGH).astype(jnp.bfloat16)
    core = win % 2
    chip = win // 2
    half = cross.shape[1] // 2
    mine = lax.dynamic_slice_in_dim(cross, core * half, half, axis=1)
    other = lax.dynamic_slice_in_dim(cross, (1 - core) * half, half, axis=1)
    partner = [(w, w ^ 1) for w in range(win_count)]
    total = mine + lax.ppermute(other, "win", partner)
    half_bins = length // 2
    weights = jnp.where(jnp.arange(half_bins) == 0, 1.0, 2.0).astype(jnp.float32) * (
        1.0 / math.sqrt(half_bins * seg_total)
    )
    scaled = total * jnp.concatenate([weights, weights])[:, None]
    lags = jnp.dot(table, scaled, preferred_element_type=jnp.float32)
    bit = win_count // 4
    while bit >= 1:
        rows = lags.shape[0] // 2
        upper = (chip // bit) % 2
        keep = lax.dynamic_slice_in_dim(lags, upper * rows, rows, axis=0)
        send = lax.dynamic_slice_in_dim(lags, (1 - upper) * rows, rows, axis=0)
        lags = keep + lax.ppermute(send, "win", [(w, w ^ (2 * bit)) for w in range(win_count)])
        bit //= 2
    both = lags.astype(jnp.bfloat16)
    kept = lax.dynamic_slice_in_dim(both, core * lag_count, lag_count, axis=0)
    given = lax.dynamic_slice_in_dim(both, (1 - core) * lag_count, lag_count, axis=0)
    got = lax.ppermute(given, "win", partner)
    return jnp.where(core == 0, jnp.concatenate([kept, got], axis=1), jnp.concatenate([got, kept], axis=1))


def lay_out_blocks(records, segment, block_of, block, half):
    segs, rows, width = records.shape
    parts = len(block_of)

    def kernel(src, dst):
        for place, b in enumerate(block_of):
            low = b * block + half
            if low + block <= width:
                dst[place] = src[0, :, low:low + block]
            else:
                dst[place, :, : width - low] = src[0, :, low:]
                dst[place, :, width - low:] = src[0, :, : low + block - width]

    return pl.pallas_call(
        kernel,
        out_shape=jax.ShapeDtypeStruct((parts, rows, block), records.dtype),
        grid=(1,),
        in_specs=[pl.BlockSpec((1, rows, width), lambda i: (segment, 0, 0))],
        out_specs=pl.BlockSpec((parts, rows, block), lambda i: (0, 0, 0)),
    )(records)


def make_per_device(ring):
    count = len(ring)
    block_of = [0] * count
    for place, device in enumerate(ring):
        block_of[device] = place
    to_prev = [(ring[r], ring[(r - 1) % count]) for r in range(count)]
    to_next = [(ring[r], ring[(r + 1) % count]) for r in range(count)]
    to_owner = [(b, ring[b]) for b in range(count)]

    def per_device(records, pair_first, pair_offset, owners):
        pair_data = jnp.stack([pair_first, pair_offset, owners[:, 0]], axis=0)
        tile_count = lax.axis_size("tile")
        win_count = lax.axis_size("win")
        length = records.shape[1] * tile_count
        seg_total = records.shape[0] * win_count
        block = records.shape[2] // tile_count
        half = block // 2
        forward = forward_matrix(length).reshape(length, tile_count, records.shape[1])
        my_first, my_offset, my_owners = lax.ppermute(pair_data, "tile", to_owner)
        channel_ids = jnp.arange(2 * block, dtype=jnp.int32)[:, None]
        pick_first = (channel_ids == my_first[None, :]).astype(jnp.bfloat16)
        pick_second = (channel_ids == (my_first + my_offset)[None, :]).astype(jnp.bfloat16)
        cross = None
        arrived = []
        for segment in range(records.shape[0]):
            outgoing = lay_out_blocks(records, segment, block_of, block, half)
            received = lax.all_to_all(outgoing, "tile", split_axis=0, concat_axis=0, tiled=True)
            if arrived:
                received, _ = lax.optimization_barrier((received, arrived[-1]))
            if segment == min(2, records.shape[0] - 1):
                received, table = lax.optimization_barrier((received, inverse_table(length, lag_start)))
            spectra = jnp.einsum("fjm,jmc->fc", forward, received, preferred_element_type=jnp.float32)
            whitened = whiten(spectra, BAND)
            from_prev = lax.ppermute(whitened[:, half:], "tile", to_next)
            from_next = lax.ppermute(whitened[:, :half], "tile", to_prev)
            if segment == 0:
                lag_start, _ = lax.optimization_barrier((jnp.int32(0), whitened))
            arrived.append((from_prev, from_next))
            joined = jnp.concatenate([from_prev, whitened, from_next], axis=1)
            first_part = jnp.dot(joined, pick_first, preferred_element_type=jnp.float32)
            second_part = jnp.dot(joined, pick_second, preferred_element_type=jnp.float32)
            term = cross_terms(first_part, second_part)
            cross = term if cross is None else cross + term
        lag_count = length // win_count
        correlation = sum_and_invert(cross, length, lag_count, seg_total, win_count, table)
        capacity = 5 * pair_first.shape[0] // (2 * tile_count)
        chooser = bucket_select(my_owners, tile_count, capacity)
        picked = lax.dot_general(
            chooser,
            correlation,
            (((1,), (1,)), ((), ())),
            preferred_element_type=jnp.float32,
        )
        buckets = picked.astype(jnp.bfloat16).reshape(tile_count, capacity, lag_count)
        received = lax.all_to_all(buckets, "tile", split_axis=0, concat_axis=0, tiled=True)
        ordered = jnp.stack([received[d] for d in ring], axis=0)
        return ordered[None]

    return per_device


def solution(mesh):
    placed = (P("win", "tile", None), P("tile"), P("tile"), P("tile", None))
    return jax.shard_map(
        make_per_device(tile_ring(mesh)),
        mesh=mesh,
        in_specs=placed,
        out_specs=P("tile", None, None, "win"),
        check_vma=False,
    )
```

```python
import math

import jax
import jax.numpy as jnp
from jax import lax
from jax.experimental import pallas as pl
from jax.sharding import PartitionSpec as P

BAND = 64


power_floor = 1e-06


def phase_table(rows, col_count, length):
    split = 64 if col_count % 64 == 0 else 1
    coarse = jnp.arange(col_count // split, dtype=jnp.int32) * split
    fine = jnp.arange(split, dtype=jnp.int32)
    scale = 2.0 * math.pi / length
    coarse_angle = ((rows[:, None] * coarse[None, :]) % length).astype(jnp.float32) * scale
    fine_angle = ((rows[:, None] * fine[None, :]) % length).astype(jnp.float32) * scale
    c_hi, s_hi = jnp.cos(coarse_angle)[:, :, None], jnp.sin(coarse_angle)[:, :, None]
    c_lo, s_lo = jnp.cos(fine_angle)[:, None, :], jnp.sin(fine_angle)[:, None, :]
    shape = (rows.shape[0], col_count)
    cosine = (c_hi * c_lo - s_hi * s_lo).reshape(shape)
    sine = (s_hi * c_lo + c_hi * s_lo).reshape(shape)
    return cosine, sine


def forward_matrix(length):
    cosine, sine = phase_table(jnp.arange(length // 2, dtype=jnp.int32), length, length)
    return jnp.concatenate([cosine, -sine], axis=0).astype(jnp.bfloat16)


def inverse_matrix(length, first_lag, lag_count, seg_total):
    half_bins = length // 2
    lags = jnp.arange(lag_count, dtype=jnp.int32) + first_lag
    cosine, sine = phase_table(lags, half_bins, length)
    bin_index = jnp.arange(half_bins)[None, :]
    weights = jnp.where(bin_index == 0, 1.0, 2.0).astype(jnp.float32) * (
        1.0 / math.sqrt(half_bins * seg_total)
    )
    return jnp.concatenate([weights * cosine, -weights * sine], axis=1)


def whiten(spectra, band_width):
    half_bins = spectra.shape[-2] // 2
    real_rows = spectra[..., :half_bins, :]
    imaginary = spectra[..., half_bins:, :]
    energy = real_rows * real_rows + imaginary * imaginary
    grouped = energy.shape[:-2] + (half_bins // band_width, band_width, energy.shape[-1])
    band_power = jnp.mean(energy.reshape(grouped), axis=-2, keepdims=True)
    inverse_rms = jnp.broadcast_to(lax.rsqrt(band_power + power_floor), grouped).reshape(
        energy.shape
    )
    return (spectra * jnp.concatenate([inverse_rms, inverse_rms], axis=-2)).astype(jnp.bfloat16)


def cross_terms(first_part, second_part):
    half_bins = first_part.shape[-2] // 2
    first_real = first_part[..., :half_bins, :].astype(jnp.float32)
    first_imag = first_part[..., half_bins:, :].astype(jnp.float32)
    second_real = second_part[..., :half_bins, :].astype(jnp.float32)
    second_imag = second_part[..., half_bins:, :].astype(jnp.float32)
    real_sum = first_real * second_real + first_imag * second_imag
    imag_sum = first_imag * second_real - first_real * second_imag
    return jnp.concatenate([real_sum, imag_sum], axis=-2)


def bucket_select(owner_ids, owner_count, capacity):
    onehot = (owner_ids[:, None] == jnp.arange(owner_count, dtype=jnp.int32)[None, :]).astype(
        jnp.int32
    )
    slot_rank = jnp.sum((jnp.cumsum(onehot, axis=0, dtype=jnp.int32) - 1) * onehot, axis=1)
    slot_id = owner_ids * capacity + slot_rank
    return (
        slot_id[None, :] == jnp.arange(owner_count * capacity, dtype=jnp.int32)[:, None]
    ).astype(jnp.bfloat16)


def tile_ring(mesh):
    count = mesh.shape["tile"]
    try:
        column = mesh.devices.reshape(count, -1)[:, 0]
        spots = [tuple(int(c) for c in d.coords) for d in column]
    except (AttributeError, TypeError):
        return list(range(count))
    near = [
        [j for j in range(count) if sum(abs(a - b) for a, b in zip(spots[i], spots[j])) == 1]
        for i in range(count)
    ]
    path, seen, budget = [0], {0}, [20000]

    def extend():
        budget[0] -= 1
        if budget[0] < 0:
            return False
        if len(path) == count:
            return count < 3 or 0 in near[path[-1]]
        options = [j for j in near[path[-1]] if j not in seen]
        options.sort(key=lambda j: sum(1 for k in near[j] if k not in seen))
        for j in options:
            path.append(j)
            seen.add(j)
            if extend():
                return True
            path.pop()
            seen.discard(j)
        return False

    return path if extend() else list(range(count))


def inverse_table(length, lag_start):
    cosine, sine = phase_table(jnp.arange(length, dtype=jnp.int32) + lag_start, length // 2, length)
    return jnp.concatenate([cosine, -sine], axis=1)


def sum_and_invert(cross, length, lag_count, seg_total, win_count, table):
    win = lax.axis_index("win")
    if win_count % 2 or win_count & (win_count - 1):
        stacked = lax.psum(cross, "win")
        inverse = inverse_matrix(length, win * lag_count, lag_count, seg_total)
        return jnp.dot(inverse, stacked, precision=lax.Precision.HIGH).astype(jnp.bfloat16)
    core = win % 2
    chip = win // 2
    half = cross.shape[1] // 2
    mine = lax.dynamic_slice_in_dim(cross, core * half, half, axis=1)
    other = lax.dynamic_slice_in_dim(cross, (1 - core) * half, half, axis=1)
    partner = [(w, w ^ 1) for w in range(win_count)]
    total = mine + lax.ppermute(other, "win", partner)
    half_bins = length // 2
    weights = jnp.where(jnp.arange(half_bins) == 0, 1.0, 2.0).astype(jnp.float32) * (
        1.0 / math.sqrt(half_bins * seg_total)
    )
    scaled = total * jnp.concatenate([weights, weights])[:, None]
    lags = jnp.dot(table, scaled, preferred_element_type=jnp.float32)
    bit = win_count // 4
    while bit >= 1:
        rows = lags.shape[0] // 2
        upper = (chip // bit) % 2
        keep = lax.dynamic_slice_in_dim(lags, upper * rows, rows, axis=0)
        send = lax.dynamic_slice_in_dim(lags, (1 - upper) * rows, rows, axis=0)
        lags = keep + lax.ppermute(send, "win", [(w, w ^ (2 * bit)) for w in range(win_count)])
        bit //= 2
    both = lags.astype(jnp.bfloat16)
    kept = lax.dynamic_slice_in_dim(both, core * lag_count, lag_count, axis=0)
    given = lax.dynamic_slice_in_dim(both, (1 - core) * lag_count, lag_count, axis=0)
    got = lax.ppermute(given, "win", partner)
    return jnp.where(core == 0, jnp.concatenate([kept, got], axis=1), jnp.concatenate([got, kept], axis=1))


def lay_out_blocks(records, segment, block_of, block, half):
    segs, rows, width = records.shape
    parts = len(block_of)

    def kernel(src, dst):
        for place, b in enumerate(block_of):
            low = b * block + half
            if low + block <= width:
                dst[place] = src[0, :, low:low + block]
            else:
                dst[place, :, : width - low] = src[0, :, low:]
                dst[place, :, width - low:] = src[0, :, : low + block - width]

    return pl.pallas_call(
        kernel,
        out_shape=jax.ShapeDtypeStruct((parts, rows, block), records.dtype),
        grid=(1,),
        in_specs=[pl.BlockSpec((1, rows, width), lambda i: (segment, 0, 0))],
        out_specs=pl.BlockSpec((parts, rows, block), lambda i: (0, 0, 0)),
    )(records)


def make_per_device(ring):
    count = len(ring)
    block_of = [0] * count
    for place, device in enumerate(ring):
        block_of[device] = place
    to_prev = [(ring[r], ring[(r - 1) % count]) for r in range(count)]
    to_next = [(ring[r], ring[(r + 1) % count]) for r in range(count)]
    to_owner = [(b, ring[b]) for b in range(count)]

    def per_device(records, pair_first, pair_offset, owners):
        pair_data = jnp.stack([pair_first, pair_offset, owners[:, 0]], axis=0)
        tile_count = lax.axis_size("tile")
        win_count = lax.axis_size("win")
        length = records.shape[1] * tile_count
        seg_total = records.shape[0] * win_count
        block = records.shape[2] // tile_count
        half = block // 2
        forward = forward_matrix(length)
        my_first, my_offset, my_owners = lax.ppermute(pair_data, "tile", to_owner)
        channel_ids = jnp.arange(2 * block, dtype=jnp.int32)[:, None]
        pick_first = (channel_ids == my_first[None, :]).astype(jnp.bfloat16)
        pick_second = (channel_ids == (my_first + my_offset)[None, :]).astype(jnp.bfloat16)
        cross = None
        arrived = []
        for segment in range(records.shape[0]):
            outgoing = lay_out_blocks(records, segment, block_of, block, half)
            received = lax.all_to_all(outgoing, "tile", split_axis=0, concat_axis=0, tiled=True)
            if arrived:
                received, _ = lax.optimization_barrier((received, arrived[-1]))
            if segment == min(2, records.shape[0] - 1):
                received, table = lax.optimization_barrier((received, inverse_table(length, lag_start)))
            spectra = jnp.dot(forward, received.reshape(length, block), preferred_element_type=jnp.float32)
            whitened = whiten(spectra, BAND)
            from_prev = lax.ppermute(whitened[:, half:], "tile", to_next)
            from_next = lax.ppermute(whitened[:, :half], "tile", to_prev)
            if segment == 0:
                lag_start, _ = lax.optimization_barrier((jnp.int32(0), whitened))
            arrived.append((from_prev, from_next))
            joined = jnp.concatenate([from_prev, whitened, from_next], axis=1)
            first_part = jnp.dot(joined, pick_first, preferred_element_type=jnp.float32)
            second_part = jnp.dot(joined, pick_second, preferred_element_type=jnp.float32)
            term = cross_terms(first_part, second_part)
            cross = term if cross is None else cross + term
        lag_count = length // win_count
        correlation = sum_and_invert(cross, length, lag_count, seg_total, win_count, table)
        capacity = 5 * pair_first.shape[0] // (2 * tile_count)
        chooser = bucket_select(my_owners, tile_count, capacity)
        picked = lax.dot_general(
            chooser,
            correlation,
            (((1,), (1,)), ((), ())),
            preferred_element_type=jnp.float32,
        )
        buckets = picked.astype(jnp.bfloat16).reshape(tile_count, capacity, lag_count)
        received = lax.all_to_all(buckets, "tile", split_axis=0, concat_axis=0, tiled=True)
        ordered = jnp.stack([received[d] for d in ring], axis=0)
        return ordered[None]

    return per_device


def solution(mesh):
    placed = (P("win", "tile", None), P("tile"), P("tile"), P("tile", None))
    return jax.shard_map(
        make_per_device(tile_ring(mesh)),
        mesh=mesh,
        in_specs=placed,
        out_specs=P("tile", None, None, "win"),
        check_vma=False,
    )
```

```python
import math

import jax
import jax.numpy as jnp
from jax import lax
from jax.experimental import pallas as pl
from jax.sharding import PartitionSpec as P

BAND = 64


power_floor = 1e-06


def phase_table(rows, col_count, length):
    split = 64 if col_count % 64 == 0 else 1
    coarse = jnp.arange(col_count // split, dtype=jnp.int32) * split
    fine = jnp.arange(split, dtype=jnp.int32)
    scale = 2.0 * math.pi / length
    coarse_angle = ((rows[:, None] * coarse[None, :]) % length).astype(jnp.float32) * scale
    fine_angle = ((rows[:, None] * fine[None, :]) % length).astype(jnp.float32) * scale
    c_hi, s_hi = jnp.cos(coarse_angle)[:, :, None], jnp.sin(coarse_angle)[:, :, None]
    c_lo, s_lo = jnp.cos(fine_angle)[:, None, :], jnp.sin(fine_angle)[:, None, :]
    shape = (rows.shape[0], col_count)
    cosine = (c_hi * c_lo - s_hi * s_lo).reshape(shape)
    sine = (s_hi * c_lo + c_hi * s_lo).reshape(shape)
    return cosine, sine


def forward_matrix(length):
    cosine, sine = phase_table(jnp.arange(length // 2, dtype=jnp.int32), length, length)
    return jnp.concatenate([cosine, -sine], axis=0).astype(jnp.bfloat16)


def inverse_matrix(length, first_lag, lag_count, seg_total):
    half_bins = length // 2
    lags = jnp.arange(lag_count, dtype=jnp.int32) + first_lag
    cosine, sine = phase_table(lags, half_bins, length)
    bin_index = jnp.arange(half_bins)[None, :]
    weights = jnp.where(bin_index == 0, 1.0, 2.0).astype(jnp.float32) * (
        1.0 / math.sqrt(half_bins * seg_total)
    )
    return jnp.concatenate([weights * cosine, -weights * sine], axis=1)


def whiten(spectra, band_width):
    half_bins = spectra.shape[-2] // 2
    real_rows = spectra[..., :half_bins, :]
    imaginary = spectra[..., half_bins:, :]
    energy = real_rows * real_rows + imaginary * imaginary
    grouped = energy.shape[:-2] + (half_bins // band_width, band_width, energy.shape[-1])
    band_power = jnp.mean(energy.reshape(grouped), axis=-2, keepdims=True)
    inverse_rms = jnp.broadcast_to(lax.rsqrt(band_power + power_floor), grouped).reshape(
        energy.shape
    )
    return (spectra * jnp.concatenate([inverse_rms, inverse_rms], axis=-2)).astype(jnp.bfloat16)


def cross_terms(first_part, second_part):
    half_bins = first_part.shape[-2] // 2
    first_real = first_part[..., :half_bins, :].astype(jnp.float32)
    first_imag = first_part[..., half_bins:, :].astype(jnp.float32)
    second_real = second_part[..., :half_bins, :].astype(jnp.float32)
    second_imag = second_part[..., half_bins:, :].astype(jnp.float32)
    real_sum = first_real * second_real + first_imag * second_imag
    imag_sum = first_imag * second_real - first_real * second_imag
    return jnp.concatenate([real_sum, imag_sum], axis=-2)


def bucket_select(owner_ids, owner_count, capacity):
    onehot = (owner_ids[:, None] == jnp.arange(owner_count, dtype=jnp.int32)[None, :]).astype(
        jnp.int32
    )
    slot_rank = jnp.sum((jnp.cumsum(onehot, axis=0, dtype=jnp.int32) - 1) * onehot, axis=1)
    slot_id = owner_ids * capacity + slot_rank
    return (
        slot_id[None, :] == jnp.arange(owner_count * capacity, dtype=jnp.int32)[:, None]
    ).astype(jnp.bfloat16)


def tile_ring(mesh):
    count = mesh.shape["tile"]
    try:
        column = mesh.devices.reshape(count, -1)[:, 0]
        spots = [tuple(int(c) for c in d.coords) for d in column]
    except (AttributeError, TypeError):
        return list(range(count))
    near = [
        [j for j in range(count) if sum(abs(a - b) for a, b in zip(spots[i], spots[j])) == 1]
        for i in range(count)
    ]
    path, seen, budget = [0], {0}, [20000]

    def extend():
        budget[0] -= 1
        if budget[0] < 0:
            return False
        if len(path) == count:
            return count < 3 or 0 in near[path[-1]]
        options = [j for j in near[path[-1]] if j not in seen]
        options.sort(key=lambda j: sum(1 for k in near[j] if k not in seen))
        for j in options:
            path.append(j)
            seen.add(j)
            if extend():
                return True
            path.pop()
            seen.discard(j)
        return False

    return path if extend() else list(range(count))


def inverse_table(length, lag_start):
    cosine, sine = phase_table(jnp.arange(length, dtype=jnp.int32) + lag_start, length // 2, length)
    return jnp.concatenate([cosine, -sine], axis=1)


def sum_and_invert(cross, length, lag_count, seg_total, win_count, table):
    win = lax.axis_index("win")
    if win_count % 2 or win_count & (win_count - 1):
        stacked = lax.psum(cross, "win")
        inverse = inverse_matrix(length, win * lag_count, lag_count, seg_total)
        return jnp.dot(inverse, stacked, precision=lax.Precision.HIGH).astype(jnp.bfloat16)
    core = win % 2
    chip = win // 2
    half = cross.shape[1] // 2
    mine = lax.dynamic_slice_in_dim(cross, core * half, half, axis=1)
    other = lax.dynamic_slice_in_dim(cross, (1 - core) * half, half, axis=1)
    partner = [(w, w ^ 1) for w in range(win_count)]
    total = mine + lax.ppermute(other, "win", partner)
    half_bins = length // 2
    weights = jnp.where(jnp.arange(half_bins) == 0, 1.0, 2.0).astype(jnp.float32) * (
        1.0 / math.sqrt(half_bins * seg_total)
    )
    scaled = total * jnp.concatenate([weights, weights])[:, None]
    lags = jnp.dot(table, scaled, precision=lax.Precision.HIGH)
    bit = win_count // 4
    while bit >= 1:
        rows = lags.shape[0] // 2
        upper = (chip // bit) % 2
        keep = lax.dynamic_slice_in_dim(lags, upper * rows, rows, axis=0)
        send = lax.dynamic_slice_in_dim(lags, (1 - upper) * rows, rows, axis=0)
        lags = keep + lax.ppermute(send, "win", [(w, w ^ (2 * bit)) for w in range(win_count)])
        bit //= 2
    both = lags.astype(jnp.bfloat16)
    kept = lax.dynamic_slice_in_dim(both, core * lag_count, lag_count, axis=0)
    given = lax.dynamic_slice_in_dim(both, (1 - core) * lag_count, lag_count, axis=0)
    got = lax.ppermute(given, "win", partner)
    return jnp.where(core == 0, jnp.concatenate([kept, got], axis=1), jnp.concatenate([got, kept], axis=1))


def lay_out_blocks(records, segment, block_of, block, half):
    segs, rows, width = records.shape
    parts = len(block_of)

    def kernel(src, dst):
        for place, b in enumerate(block_of):
            low = b * block + half
            if low + block <= width:
                dst[place] = src[0, :, low:low + block]
            else:
                dst[place, :, : width - low] = src[0, :, low:]
                dst[place, :, width - low:] = src[0, :, : low + block - width]

    return pl.pallas_call(
        kernel,
        out_shape=jax.ShapeDtypeStruct((parts, rows, block), records.dtype),
        grid=(1,),
        in_specs=[pl.BlockSpec((1, rows, width), lambda i: (segment, 0, 0))],
        out_specs=pl.BlockSpec((parts, rows, block), lambda i: (0, 0, 0)),
    )(records)


def make_per_device(ring):
    count = len(ring)
    block_of = [0] * count
    for place, device in enumerate(ring):
        block_of[device] = place
    to_prev = [(ring[r], ring[(r - 1) % count]) for r in range(count)]
    to_next = [(ring[r], ring[(r + 1) % count]) for r in range(count)]
    to_owner = [(b, ring[b]) for b in range(count)]

    def per_device(records, pair_first, pair_offset, owners):
        pair_data = jnp.stack([pair_first, pair_offset, owners[:, 0]], axis=0)
        tile_count = lax.axis_size("tile")
        win_count = lax.axis_size("win")
        length = records.shape[1] * tile_count
        seg_total = records.shape[0] * win_count
        block = records.shape[2] // tile_count
        half = block // 2
        forward = forward_matrix(length)
        my_first, my_offset, my_owners = lax.ppermute(pair_data, "tile", to_owner)
        channel_ids = jnp.arange(2 * block, dtype=jnp.int32)[:, None]
        pick_first = (channel_ids == my_first[None, :]).astype(jnp.bfloat16)
        pick_second = (channel_ids == (my_first + my_offset)[None, :]).astype(jnp.bfloat16)
        cross = None
        arrived = []
        for segment in range(records.shape[0]):
            outgoing = lay_out_blocks(records, segment, block_of, block, half)
            received = lax.all_to_all(outgoing, "tile", split_axis=0, concat_axis=0, tiled=True)
            if arrived:
                received, _ = lax.optimization_barrier((received, arrived[-1]))
            if segment == min(2, records.shape[0] - 1):
                received, table = lax.optimization_barrier((received, inverse_table(length, lag_start)))
            spectra = jnp.dot(forward, received.reshape(length, block), preferred_element_type=jnp.float32)
            whitened = whiten(spectra, BAND)
            from_prev = lax.ppermute(whitened[:, half:], "tile", to_next)
            from_next = lax.ppermute(whitened[:, :half], "tile", to_prev)
            if segment == 0:
                lag_start, _ = lax.optimization_barrier((jnp.int32(0), whitened))
            arrived.append((from_prev, from_next))
            joined = jnp.concatenate([from_prev, whitened, from_next], axis=1)
            first_part = jnp.dot(joined, pick_first, preferred_element_type=jnp.float32)
            second_part = jnp.dot(joined, pick_second, preferred_element_type=jnp.float32)
            term = cross_terms(first_part, second_part)
            cross = term if cross is None else cross + term
        lag_count = length // win_count
        correlation = sum_and_invert(cross, length, lag_count, seg_total, win_count, table)
        capacity = 5 * pair_first.shape[0] // (2 * tile_count)
        chooser = bucket_select(my_owners, tile_count, capacity)
        picked = lax.dot_general(
            chooser,
            correlation,
            (((1,), (1,)), ((), ())),
            preferred_element_type=jnp.float32,
        )
        buckets = picked.astype(jnp.bfloat16).reshape(tile_count, capacity, lag_count)
        received = lax.all_to_all(buckets, "tile", split_axis=0, concat_axis=0, tiled=True)
        ordered = jnp.stack([received[d] for d in ring], axis=0)
        return ordered[None]

    return per_device


def solution(mesh):
    placed = (P("win", "tile", None), P("tile"), P("tile"), P("tile", None))
    return jax.shard_map(
        make_per_device(tile_ring(mesh)),
        mesh=mesh,
        in_specs=placed,
        out_specs=P("tile", None, None, "win"),
        check_vma=False,
    )
```

```python
import math

import jax
import jax.numpy as jnp
from jax import lax
from jax.experimental import pallas as pl
from jax.sharding import PartitionSpec as P

BAND = 64


power_floor = 1e-06


def phase_table(rows, col_count, length):
    split = 64 if col_count % 64 == 0 else 1
    coarse = jnp.arange(col_count // split, dtype=jnp.int32) * split
    fine = jnp.arange(split, dtype=jnp.int32)
    scale = 2.0 * math.pi / length
    coarse_angle = ((rows[:, None] * coarse[None, :]) % length).astype(jnp.float32) * scale
    fine_angle = ((rows[:, None] * fine[None, :]) % length).astype(jnp.float32) * scale
    c_hi, s_hi = jnp.cos(coarse_angle)[:, :, None], jnp.sin(coarse_angle)[:, :, None]
    c_lo, s_lo = jnp.cos(fine_angle)[:, None, :], jnp.sin(fine_angle)[:, None, :]
    shape = (rows.shape[0], col_count)
    cosine = (c_hi * c_lo - s_hi * s_lo).reshape(shape)
    sine = (s_hi * c_lo + c_hi * s_lo).reshape(shape)
    return cosine, sine


def forward_matrix(length):
    cosine, sine = phase_table(jnp.arange(length // 2, dtype=jnp.int32), length, length)
    return jnp.concatenate([cosine, -sine], axis=0).astype(jnp.bfloat16)


def inverse_matrix(length, first_lag, lag_count, seg_total):
    half_bins = length // 2
    lags = jnp.arange(lag_count, dtype=jnp.int32) + first_lag
    cosine, sine = phase_table(lags, half_bins, length)
    bin_index = jnp.arange(half_bins)[None, :]
    weights = jnp.where(bin_index == 0, 1.0, 2.0).astype(jnp.float32) * (
        1.0 / math.sqrt(half_bins * seg_total)
    )
    return jnp.concatenate([weights * cosine, -weights * sine], axis=1)


def whiten(spectra, band_width):
    half_bins = spectra.shape[-2] // 2
    real_rows = spectra[..., :half_bins, :]
    imaginary = spectra[..., half_bins:, :]
    energy = real_rows * real_rows + imaginary * imaginary
    grouped = energy.shape[:-2] + (half_bins // band_width, band_width, energy.shape[-1])
    band_power = jnp.mean(energy.reshape(grouped), axis=-2, keepdims=True)
    inverse_rms = jnp.broadcast_to(lax.rsqrt(band_power + power_floor), grouped).reshape(
        energy.shape
    )
    return (spectra * jnp.concatenate([inverse_rms, inverse_rms], axis=-2)).astype(jnp.bfloat16)


def cross_terms(first_part, second_part):
    half_bins = first_part.shape[-2] // 2
    first_real = first_part[..., :half_bins, :].astype(jnp.float32)
    first_imag = first_part[..., half_bins:, :].astype(jnp.float32)
    second_real = second_part[..., :half_bins, :].astype(jnp.float32)
    second_imag = second_part[..., half_bins:, :].astype(jnp.float32)
    real_sum = first_real * second_real + first_imag * second_imag
    imag_sum = first_imag * second_real - first_real * second_imag
    return jnp.concatenate([real_sum, imag_sum], axis=-2)


def bucket_select(owner_ids, owner_count, capacity):
    onehot = (owner_ids[:, None] == jnp.arange(owner_count, dtype=jnp.int32)[None, :]).astype(
        jnp.int32
    )
    slot_rank = jnp.sum((jnp.cumsum(onehot, axis=0, dtype=jnp.int32) - 1) * onehot, axis=1)
    slot_id = owner_ids * capacity + slot_rank
    return (
        slot_id[None, :] == jnp.arange(owner_count * capacity, dtype=jnp.int32)[:, None]
    ).astype(jnp.bfloat16)


def tile_ring(mesh):
    count = mesh.shape["tile"]
    try:
        column = mesh.devices.reshape(count, -1)[:, 0]
        spots = [tuple(int(c) for c in d.coords) for d in column]
    except (AttributeError, TypeError):
        return list(range(count))
    near = [
        [j for j in range(count) if sum(abs(a - b) for a, b in zip(spots[i], spots[j])) == 1]
        for i in range(count)
    ]
    path, seen, budget = [0], {0}, [20000]

    def extend():
        budget[0] -= 1
        if budget[0] < 0:
            return False
        if len(path) == count:
            return count < 3 or 0 in near[path[-1]]
        options = [j for j in near[path[-1]] if j not in seen]
        options.sort(key=lambda j: sum(1 for k in near[j] if k not in seen))
        for j in options:
            path.append(j)
            seen.add(j)
            if extend():
                return True
            path.pop()
            seen.discard(j)
        return False

    return path if extend() else list(range(count))


def inverse_table(length, lag_start):
    cosine, sine = phase_table(jnp.arange(length, dtype=jnp.int32) + lag_start, length // 2, length)
    return jnp.concatenate([cosine, -sine], axis=1)


def sum_and_invert(cross, length, lag_count, seg_total, win_count, table):
    win = lax.axis_index("win")
    if win_count % 2 or win_count & (win_count - 1):
        stacked = lax.psum(cross, "win")
        inverse = inverse_matrix(length, win * lag_count, lag_count, seg_total)
        return jnp.dot(inverse, stacked, precision=lax.Precision.HIGH).astype(jnp.bfloat16)
    core = win % 2
    chip = win // 2
    half = cross.shape[1] // 2
    mine = lax.dynamic_slice_in_dim(cross, core * half, half, axis=1)
    other = lax.dynamic_slice_in_dim(cross, (1 - core) * half, half, axis=1)
    partner = [(w, w ^ 1) for w in range(win_count)]
    total = mine + lax.ppermute(other, "win", partner)
    half_bins = length // 2
    weights = jnp.where(jnp.arange(half_bins) == 0, 1.0, 2.0).astype(jnp.float32) * (
        1.0 / math.sqrt(half_bins * seg_total)
    )
    scaled = total * jnp.concatenate([weights, weights])[:, None]
    lags = jnp.dot(table, scaled, preferred_element_type=jnp.float32)
    bit = win_count // 4
    while bit >= 1:
        rows = lags.shape[0] // 2
        upper = (chip // bit) % 2
        keep = lax.dynamic_slice_in_dim(lags, upper * rows, rows, axis=0)
        send = lax.dynamic_slice_in_dim(lags, (1 - upper) * rows, rows, axis=0)
        lags = keep + lax.ppermute(send, "win", [(w, w ^ (2 * bit)) for w in range(win_count)])
        bit //= 2
    both = lags.astype(jnp.bfloat16)
    kept = lax.dynamic_slice_in_dim(both, core * lag_count, lag_count, axis=0)
    given = lax.dynamic_slice_in_dim(both, (1 - core) * lag_count, lag_count, axis=0)
    got = lax.ppermute(given, "win", partner)
    return jnp.where(core == 0, jnp.concatenate([kept, got], axis=1), jnp.concatenate([got, kept], axis=1))


def lay_out_blocks(records, segment, block_of, block, half):
    segs, rows, width = records.shape
    parts = len(block_of)

    def kernel(src, dst):
        for place, b in enumerate(block_of):
            low = b * block + half
            if low + block <= width:
                dst[place] = src[0, :, low:low + block]
            else:
                dst[place, :, : width - low] = src[0, :, low:]
                dst[place, :, width - low:] = src[0, :, : low + block - width]

    return pl.pallas_call(
        kernel,
        out_shape=jax.ShapeDtypeStruct((parts, rows, block), records.dtype),
        grid=(1,),
        in_specs=[pl.BlockSpec((1, rows, width), lambda i: (segment, 0, 0))],
        out_specs=pl.BlockSpec((parts, rows, block), lambda i: (0, 0, 0)),
    )(records)


def make_per_device(ring):
    count = len(ring)
    block_of = [0] * count
    for place, device in enumerate(ring):
        block_of[device] = place
    to_prev = [(ring[r], ring[(r - 1) % count]) for r in range(count)]
    to_next = [(ring[r], ring[(r + 1) % count]) for r in range(count)]
    to_owner = [(b, ring[b]) for b in range(count)]

    def per_device(records, pair_first, pair_offset, owners):
        pair_data = jnp.stack([pair_first, pair_offset, owners[:, 0]], axis=0)
        tile_count = lax.axis_size("tile")
        win_count = lax.axis_size("win")
        length = records.shape[1] * tile_count
        seg_total = records.shape[0] * win_count
        block = records.shape[2] // tile_count
        half = block // 2
        forward = forward_matrix(length)
        my_first, my_offset, my_owners = lax.ppermute(pair_data, "tile", to_owner)
        channel_ids = jnp.arange(2 * block, dtype=jnp.int32)[:, None]
        pick_first = (channel_ids == my_first[None, :]).astype(jnp.bfloat16)
        pick_second = (channel_ids == (my_first + my_offset)[None, :]).astype(jnp.bfloat16)
        cross = None
        arrived = []
        for segment in range(records.shape[0]):
            outgoing = lay_out_blocks(records, segment, block_of, block, half)
            received = lax.all_to_all(outgoing, "tile", split_axis=0, concat_axis=0, tiled=True)
            if arrived:
                received, _ = lax.optimization_barrier((received, arrived[-1]))
            if segment == min(2, records.shape[0] - 1):
                received, table = lax.optimization_barrier((received, inverse_table(length, lag_start)))
            samples = received.reshape(length, block)
            if segment == records.shape[0] - 1 and segment > 0:
                lower = whiten(jnp.dot(forward, samples[:, :half], preferred_element_type=jnp.float32), BAND)
                from_next = lax.ppermute(lower, "tile", to_prev)
                upper = whiten(jnp.dot(forward, samples[:, half:], preferred_element_type=jnp.float32), BAND)
                from_prev = lax.ppermute(upper, "tile", to_next)
                whitened = jnp.concatenate([lower, upper], axis=1)
            else:
                spectra = jnp.dot(forward, samples, preferred_element_type=jnp.float32)
                whitened = whiten(spectra, BAND)
                from_prev = lax.ppermute(whitened[:, half:], "tile", to_next)
                from_next = lax.ppermute(whitened[:, :half], "tile", to_prev)
            if segment == 0:
                lag_start, _ = lax.optimization_barrier((jnp.int32(0), whitened))
            arrived.append((from_prev, from_next))
            joined = jnp.concatenate([from_prev, whitened, from_next], axis=1)
            first_part = jnp.dot(joined, pick_first, preferred_element_type=jnp.float32)
            second_part = jnp.dot(joined, pick_second, preferred_element_type=jnp.float32)
            term = cross_terms(first_part, second_part)
            cross = term if cross is None else cross + term
        lag_count = length // win_count
        correlation = sum_and_invert(cross, length, lag_count, seg_total, win_count, table)
        capacity = 5 * pair_first.shape[0] // (2 * tile_count)
        chooser = bucket_select(my_owners, tile_count, capacity)
        picked = lax.dot_general(
            chooser,
            correlation,
            (((1,), (1,)), ((), ())),
            preferred_element_type=jnp.float32,
        )
        buckets = picked.astype(jnp.bfloat16).reshape(tile_count, capacity, lag_count)
        received = lax.all_to_all(buckets, "tile", split_axis=0, concat_axis=0, tiled=True)
        ordered = jnp.stack([received[d] for d in ring], axis=0)
        return ordered[None]

    return per_device


def solution(mesh):
    placed = (P("win", "tile", None), P("tile"), P("tile"), P("tile", None))
    return jax.shard_map(
        make_per_device(tile_ring(mesh)),
        mesh=mesh,
        in_specs=placed,
        out_specs=P("tile", None, None, "win"),
        check_vma=False,
    )
```

```python
import math

import jax
import jax.numpy as jnp
from jax import lax
from jax.experimental import pallas as pl
from jax.sharding import PartitionSpec as P

BAND = 64


power_floor = 1e-06


def phase_table(rows, col_count, length):
    split = 64 if col_count % 64 == 0 else 1
    coarse = jnp.arange(col_count // split, dtype=jnp.int32) * split
    fine = jnp.arange(split, dtype=jnp.int32)
    scale = 2.0 * math.pi / length
    coarse_angle = ((rows[:, None] * coarse[None, :]) % length).astype(jnp.float32) * scale
    fine_angle = ((rows[:, None] * fine[None, :]) % length).astype(jnp.float32) * scale
    c_hi, s_hi = jnp.cos(coarse_angle)[:, :, None], jnp.sin(coarse_angle)[:, :, None]
    c_lo, s_lo = jnp.cos(fine_angle)[:, None, :], jnp.sin(fine_angle)[:, None, :]
    shape = (rows.shape[0], col_count)
    cosine = (c_hi * c_lo - s_hi * s_lo).reshape(shape)
    sine = (s_hi * c_lo + c_hi * s_lo).reshape(shape)
    return cosine, sine


def forward_matrix(length):
    cosine, sine = phase_table(jnp.arange(length // 2, dtype=jnp.int32), length, length)
    return jnp.concatenate([cosine, -sine], axis=0).astype(jnp.bfloat16)


def inverse_matrix(length, first_lag, lag_count, seg_total):
    half_bins = length // 2
    lags = jnp.arange(lag_count, dtype=jnp.int32) + first_lag
    cosine, sine = phase_table(lags, half_bins, length)
    bin_index = jnp.arange(half_bins)[None, :]
    weights = jnp.where(bin_index == 0, 1.0, 2.0).astype(jnp.float32) * (
        1.0 / math.sqrt(half_bins * seg_total)
    )
    return jnp.concatenate([weights * cosine, -weights * sine], axis=1)


def whiten(spectra, band_width):
    half_bins = spectra.shape[-2] // 2
    real_rows = spectra[..., :half_bins, :]
    imaginary = spectra[..., half_bins:, :]
    energy = real_rows * real_rows + imaginary * imaginary
    grouped = energy.shape[:-2] + (half_bins // band_width, band_width, energy.shape[-1])
    band_power = jnp.mean(energy.reshape(grouped), axis=-2, keepdims=True)
    inverse_rms = jnp.broadcast_to(lax.rsqrt(band_power + power_floor), grouped).reshape(
        energy.shape
    )
    return (spectra * jnp.concatenate([inverse_rms, inverse_rms], axis=-2)).astype(jnp.bfloat16)


def cross_terms(first_part, second_part):
    half_bins = first_part.shape[-2] // 2
    first_real = first_part[..., :half_bins, :].astype(jnp.float32)
    first_imag = first_part[..., half_bins:, :].astype(jnp.float32)
    second_real = second_part[..., :half_bins, :].astype(jnp.float32)
    second_imag = second_part[..., half_bins:, :].astype(jnp.float32)
    real_sum = first_real * second_real + first_imag * second_imag
    imag_sum = first_imag * second_real - first_real * second_imag
    return jnp.concatenate([real_sum, imag_sum], axis=-2)


def bucket_select(owner_ids, owner_count, capacity, order=lambda v: v):
    onehot = (owner_ids[:, None] == jnp.arange(owner_count, dtype=jnp.int32)[None, :]).astype(
        jnp.int32
    )
    slot_rank = jnp.sum((jnp.cumsum(onehot, axis=0, dtype=jnp.int32) - 1) * onehot, axis=1)
    slot_id = order(owner_ids * capacity + slot_rank)
    return (
        slot_id[None, :] == jnp.arange(owner_count * capacity, dtype=jnp.int32)[:, None]
    ).astype(jnp.bfloat16)


def tile_ring(mesh):
    count = mesh.shape["tile"]
    try:
        column = mesh.devices.reshape(count, -1)[:, 0]
        spots = [tuple(int(c) for c in d.coords) for d in column]
    except (AttributeError, TypeError):
        return list(range(count))
    near = [
        [j for j in range(count) if sum(abs(a - b) for a, b in zip(spots[i], spots[j])) == 1]
        for i in range(count)
    ]
    path, seen, budget = [0], {0}, [20000]

    def extend():
        budget[0] -= 1
        if budget[0] < 0:
            return False
        if len(path) == count:
            return count < 3 or 0 in near[path[-1]]
        options = [j for j in near[path[-1]] if j not in seen]
        options.sort(key=lambda j: sum(1 for k in near[j] if k not in seen))
        for j in options:
            path.append(j)
            seen.add(j)
            if extend():
                return True
            path.pop()
            seen.discard(j)
        return False

    return path if extend() else list(range(count))


def inverse_table(length, lag_start):
    cosine, sine = phase_table(jnp.arange(length, dtype=jnp.int32) + lag_start, length // 2, length)
    return jnp.concatenate([cosine, -sine], axis=1)


def sum_and_invert(cross, length, lag_count, seg_total, win_count, table):
    win = lax.axis_index("win")
    if win_count % 2 or win_count & (win_count - 1):
        stacked = lax.psum(cross, "win")
        inverse = inverse_matrix(length, win * lag_count, lag_count, seg_total)
        return jnp.dot(inverse, stacked, precision=lax.Precision.HIGH).astype(jnp.bfloat16)
    core = win % 2
    chip = win // 2
    half = cross.shape[1] // 2
    mine = cross[:, :half]
    other = cross[:, half:]
    partner = [(w, w ^ 1) for w in range(win_count)]
    total = mine + lax.ppermute(other, "win", partner)
    half_bins = length // 2
    weights = jnp.where(jnp.arange(half_bins) == 0, 1.0, 2.0).astype(jnp.float32) * (
        1.0 / math.sqrt(half_bins * seg_total)
    )
    scaled = total * jnp.concatenate([weights, weights])[:, None]
    lags = jnp.dot(table, scaled, preferred_element_type=jnp.float32)
    bit = win_count // 4
    while bit >= 1:
        rows = lags.shape[0] // 2
        upper = (chip // bit) % 2
        keep = lax.dynamic_slice_in_dim(lags, upper * rows, rows, axis=0)
        send = lax.dynamic_slice_in_dim(lags, (1 - upper) * rows, rows, axis=0)
        lags = keep + lax.ppermute(send, "win", [(w, w ^ (2 * bit)) for w in range(win_count)])
        bit //= 2
    both = lags.astype(jnp.bfloat16)
    kept = lax.dynamic_slice_in_dim(both, core * lag_count, lag_count, axis=0)
    given = lax.dynamic_slice_in_dim(both, (1 - core) * lag_count, lag_count, axis=0)
    got = lax.ppermute(given, "win", partner)
    return jnp.concatenate([kept, got], axis=1)


def lay_out_blocks(records, segment, block_of, block, half):
    segs, rows, width = records.shape
    parts = len(block_of)

    def kernel(src, dst):
        for place, b in enumerate(block_of):
            low = b * block + half
            if low + block <= width:
                dst[place] = src[0, :, low:low + block]
            else:
                dst[place, :, : width - low] = src[0, :, low:]
                dst[place, :, width - low:] = src[0, :, : low + block - width]

    return pl.pallas_call(
        kernel,
        out_shape=jax.ShapeDtypeStruct((parts, rows, block), records.dtype),
        grid=(1,),
        in_specs=[pl.BlockSpec((1, rows, width), lambda i: (segment, 0, 0))],
        out_specs=pl.BlockSpec((parts, rows, block), lambda i: (0, 0, 0)),
    )(records)


def make_per_device(ring):
    count = len(ring)
    block_of = [0] * count
    for place, device in enumerate(ring):
        block_of[device] = place
    to_prev = [(ring[r], ring[(r - 1) % count]) for r in range(count)]
    to_next = [(ring[r], ring[(r + 1) % count]) for r in range(count)]
    to_owner = [(b, ring[b]) for b in range(count)]

    def per_device(records, pair_first, pair_offset, owners):
        pair_data = jnp.stack([pair_first, pair_offset, owners[:, 0]], axis=0)
        tile_count = lax.axis_size("tile")
        win_count = lax.axis_size("win")
        length = records.shape[1] * tile_count
        seg_total = records.shape[0] * win_count
        block = records.shape[2] // tile_count
        half = block // 2
        forward = forward_matrix(length)
        my_first, my_offset, my_owners = lax.ppermute(pair_data, "tile", to_owner)
        order = lambda v: v
        if win_count % 2 == 0 and not win_count & (win_count - 1):
            core = lax.axis_index("win") % 2
            order = lambda v: jnp.where(core == 0, v, jnp.roll(v, -(v.shape[0] // 2)))
        my_first, my_offset = order(my_first), order(my_offset)
        channel_ids = jnp.arange(2 * block, dtype=jnp.int32)[:, None]
        pick_first = (channel_ids == my_first[None, :]).astype(jnp.bfloat16)
        pick_second = (channel_ids == (my_first + my_offset)[None, :]).astype(jnp.bfloat16)
        cross = None
        arrived = []
        for segment in range(records.shape[0]):
            outgoing = lay_out_blocks(records, segment, block_of, block, half)
            received = lax.all_to_all(outgoing, "tile", split_axis=0, concat_axis=0, tiled=True)
            if arrived:
                received, _ = lax.optimization_barrier((received, arrived[-1]))
            if segment == min(2, records.shape[0] - 1):
                received, table = lax.optimization_barrier((received, inverse_table(length, lag_start)))
            spectra = jnp.dot(forward, received.reshape(length, block), preferred_element_type=jnp.float32)
            whitened = whiten(spectra, BAND)
            from_prev = lax.ppermute(whitened[:, half:], "tile", to_next)
            from_next = lax.ppermute(whitened[:, :half], "tile", to_prev)
            if segment == 0:
                lag_start, _ = lax.optimization_barrier((jnp.int32(0), whitened))
            arrived.append((from_prev, from_next))
            joined = jnp.concatenate([from_prev, whitened, from_next], axis=1)
            first_part = jnp.dot(joined, pick_first, preferred_element_type=jnp.float32)
            second_part = jnp.dot(joined, pick_second, preferred_element_type=jnp.float32)
            term = cross_terms(first_part, second_part)
            cross = term if cross is None else cross + term
        lag_count = length // win_count
        correlation = sum_and_invert(cross, length, lag_count, seg_total, win_count, table)
        capacity = 5 * pair_first.shape[0] // (2 * tile_count)
        chooser = bucket_select(my_owners, tile_count, capacity, order)
        picked = lax.dot_general(
            chooser,
            correlation,
            (((1,), (1,)), ((), ())),
            preferred_element_type=jnp.float32,
        )
        buckets = picked.astype(jnp.bfloat16).reshape(tile_count, capacity, lag_count)
        received = lax.all_to_all(buckets, "tile", split_axis=0, concat_axis=0, tiled=True)
        ordered = jnp.stack([received[d] for d in ring], axis=0)
        return ordered[None]

    return per_device


def solution(mesh):
    placed = (P("win", "tile", None), P("tile"), P("tile"), P("tile", None))
    return jax.shard_map(
        make_per_device(tile_ring(mesh)),
        mesh=mesh,
        in_specs=placed,
        out_specs=P("tile", None, None, "win"),
        check_vma=False,
    )
```

```python
import math

import jax
import jax.numpy as jnp
from jax import lax
from jax.experimental import pallas as pl
from jax.sharding import PartitionSpec as P

BAND = 64


power_floor = 1e-06


def phase_table(rows, col_count, length):
    split = 64 if col_count % 64 == 0 else 1
    coarse = jnp.arange(col_count // split, dtype=jnp.int32) * split
    fine = jnp.arange(split, dtype=jnp.int32)
    scale = 2.0 * math.pi / length
    coarse_angle = ((rows[:, None] * coarse[None, :]) % length).astype(jnp.float32) * scale
    fine_angle = ((rows[:, None] * fine[None, :]) % length).astype(jnp.float32) * scale
    c_hi, s_hi = jnp.cos(coarse_angle)[:, :, None], jnp.sin(coarse_angle)[:, :, None]
    c_lo, s_lo = jnp.cos(fine_angle)[:, None, :], jnp.sin(fine_angle)[:, None, :]
    shape = (rows.shape[0], col_count)
    cosine = (c_hi * c_lo - s_hi * s_lo).reshape(shape)
    sine = (s_hi * c_lo + c_hi * s_lo).reshape(shape)
    return cosine, sine


def forward_matrix(length):
    cosine, sine = phase_table(jnp.arange(length // 2, dtype=jnp.int32), length, length)
    return jnp.concatenate([cosine, -sine], axis=0).astype(jnp.bfloat16)


def inverse_matrix(length, first_lag, lag_count, seg_total):
    half_bins = length // 2
    lags = jnp.arange(lag_count, dtype=jnp.int32) + first_lag
    cosine, sine = phase_table(lags, half_bins, length)
    bin_index = jnp.arange(half_bins)[None, :]
    weights = jnp.where(bin_index == 0, 1.0, 2.0).astype(jnp.float32) * (
        1.0 / math.sqrt(half_bins * seg_total)
    )
    return jnp.concatenate([weights * cosine, -weights * sine], axis=1)


def whiten(spectra, band_width):
    half_bins = spectra.shape[-2] // 2
    real_rows = spectra[..., :half_bins, :]
    imaginary = spectra[..., half_bins:, :]
    energy = real_rows * real_rows + imaginary * imaginary
    grouped = energy.shape[:-2] + (half_bins // band_width, band_width, energy.shape[-1])
    band_power = jnp.mean(energy.reshape(grouped), axis=-2, keepdims=True)
    inverse_rms = jnp.broadcast_to(lax.rsqrt(band_power + power_floor), grouped).reshape(
        energy.shape
    )
    return (spectra * jnp.concatenate([inverse_rms, inverse_rms], axis=-2)).astype(jnp.bfloat16)


def cross_terms(first_part, second_part):
    half_bins = first_part.shape[-2] // 2
    first_real = first_part[..., :half_bins, :].astype(jnp.float32)
    first_imag = first_part[..., half_bins:, :].astype(jnp.float32)
    second_real = second_part[..., :half_bins, :].astype(jnp.float32)
    second_imag = second_part[..., half_bins:, :].astype(jnp.float32)
    real_sum = first_real * second_real + first_imag * second_imag
    imag_sum = first_imag * second_real - first_real * second_imag
    return jnp.concatenate([real_sum, imag_sum], axis=-2)


def bucket_select(owner_ids, owner_count, capacity, order=lambda v: v):
    onehot = (owner_ids[:, None] == jnp.arange(owner_count, dtype=jnp.int32)[None, :]).astype(
        jnp.int32
    )
    slot_rank = jnp.sum((jnp.cumsum(onehot, axis=0, dtype=jnp.int32) - 1) * onehot, axis=1)
    slot_id = order(owner_ids * capacity + slot_rank)
    return (
        slot_id[None, :] == jnp.arange(owner_count * capacity, dtype=jnp.int32)[:, None]
    ).astype(jnp.bfloat16)


def tile_ring(mesh):
    count = mesh.shape["tile"]
    try:
        column = mesh.devices.reshape(count, -1)[:, 0]
        spots = [tuple(int(c) for c in d.coords) for d in column]
    except (AttributeError, TypeError):
        return list(range(count))
    near = [
        [j for j in range(count) if sum(abs(a - b) for a, b in zip(spots[i], spots[j])) == 1]
        for i in range(count)
    ]
    path, seen, budget = [0], {0}, [20000]

    def extend():
        budget[0] -= 1
        if budget[0] < 0:
            return False
        if len(path) == count:
            return count < 3 or 0 in near[path[-1]]
        options = [j for j in near[path[-1]] if j not in seen]
        options.sort(key=lambda j: sum(1 for k in near[j] if k not in seen))
        for j in options:
            path.append(j)
            seen.add(j)
            if extend():
                return True
            path.pop()
            seen.discard(j)
        return False

    return path if extend() else list(range(count))


def inverse_table(length, lag_start):
    cosine, sine = phase_table(jnp.arange(length, dtype=jnp.int32) + lag_start, length // 2, length)
    return jnp.concatenate([cosine, -sine], axis=1)


def sum_and_invert(cross, length, lag_count, seg_total, win_count, table):
    win = lax.axis_index("win")
    if win_count % 2 or win_count & (win_count - 1):
        stacked = lax.psum(cross, "win")
        inverse = inverse_matrix(length, win * lag_count, lag_count, seg_total)
        return jnp.dot(inverse, stacked, precision=lax.Precision.HIGH).astype(jnp.bfloat16)
    core = win % 2
    chip = win // 2
    half = cross.shape[1] // 2
    mine = cross[:, :half]
    other = cross[:, half:]
    partner = [(w, w ^ 1) for w in range(win_count)]
    total = mine + lax.ppermute(other, "win", partner)
    half_bins = length // 2
    weights = jnp.where(jnp.arange(half_bins) == 0, 1.0, 2.0).astype(jnp.float32) * (
        1.0 / math.sqrt(half_bins * seg_total)
    )
    scaled = total * jnp.concatenate([weights, weights])[:, None]
    lags = jnp.dot(table, scaled, preferred_element_type=jnp.float32)
    bit = win_count // 4
    while bit >= 1:
        rows = lags.shape[0] // 2
        upper = (chip // bit) % 2
        keep = lax.dynamic_slice_in_dim(lags, upper * rows, rows, axis=0)
        send = lax.dynamic_slice_in_dim(lags, (1 - upper) * rows, rows, axis=0)
        lags = keep + lax.ppermute(send, "win", [(w, w ^ (2 * bit)) for w in range(win_count)])
        bit //= 2
    both = lags.astype(jnp.bfloat16)
    kept = lax.dynamic_slice_in_dim(both, core * lag_count, lag_count, axis=0)
    given = lax.dynamic_slice_in_dim(both, (1 - core) * lag_count, lag_count, axis=0)
    got = lax.ppermute(given, "win", partner)
    return jnp.concatenate([kept, got], axis=1)


def lay_out_blocks(records, segment, block_of, block, half):
    segs, rows, width = records.shape
    parts = len(block_of)

    def kernel(src, dst):
        for place, b in enumerate(block_of):
            low = b * block + half
            if low + block <= width:
                dst[place] = src[0, :, low:low + block]
            else:
                dst[place, :, : width - low] = src[0, :, low:]
                dst[place, :, width - low:] = src[0, :, : low + block - width]

    return pl.pallas_call(
        kernel,
        out_shape=jax.ShapeDtypeStruct((parts, rows, block), records.dtype),
        grid=(1,),
        in_specs=[pl.BlockSpec((1, rows, width), lambda i: (segment, 0, 0))],
        out_specs=pl.BlockSpec((parts, rows, block), lambda i: (0, 0, 0)),
    )(records)


def make_per_device(ring):
    count = len(ring)
    block_of = [0] * count
    for place, device in enumerate(ring):
        block_of[device] = place
    to_prev = [(ring[r], ring[(r - 1) % count]) for r in range(count)]
    to_next = [(ring[r], ring[(r + 1) % count]) for r in range(count)]
    to_owner = [(b, ring[b]) for b in range(count)]

    def per_device(records, pair_first, pair_offset, owners):
        pair_data = jnp.stack([pair_first, pair_offset, owners[:, 0]], axis=0)
        tile_count = lax.axis_size("tile")
        win_count = lax.axis_size("win")
        length = records.shape[1] * tile_count
        seg_total = records.shape[0] * win_count
        block = records.shape[2] // tile_count
        half = block // 2
        forward = forward_matrix(length)
        my_first, my_offset, my_owners = lax.ppermute(pair_data, "tile", to_owner)
        order = lambda v: v
        if win_count % 2 == 0 and not win_count & (win_count - 1):
            core = lax.axis_index("win") % 2
            order = lambda v: jnp.where(core == 0, v, jnp.roll(v, -(v.shape[0] // 2)))
        my_first, my_offset = order(my_first), order(my_offset)
        channel_ids = jnp.arange(2 * block, dtype=jnp.int32)[:, None]
        pick_first = (channel_ids == my_first[None, :]).astype(jnp.bfloat16)
        pick_second = (channel_ids == (my_first + my_offset)[None, :]).astype(jnp.bfloat16)
        cross = None
        arrived = []
        for segment in range(records.shape[0]):
            outgoing = lay_out_blocks(records, segment, block_of, block, half)
            received = lax.all_to_all(outgoing, "tile", split_axis=0, concat_axis=0, tiled=True)
            if arrived:
                received, _ = lax.optimization_barrier((received, arrived[-1]))
            if segment == min(2, records.shape[0] - 1):
                received, table = lax.optimization_barrier((received, inverse_table(length, lag_start)))
            spectra = jnp.dot(forward, received.reshape(length, block), preferred_element_type=jnp.float32)
            lower = whiten(spectra[:, :half], BAND)
            upper = whiten(spectra[:, half:], BAND)
            from_prev = lax.ppermute(upper, "tile", to_next)
            from_next = lax.ppermute(lower, "tile", to_prev)
            whitened = jnp.concatenate([lower, upper], axis=1)
            if segment == 0:
                lag_start, _ = lax.optimization_barrier((jnp.int32(0), whitened))
            arrived.append((from_prev, from_next))
            joined = jnp.concatenate([from_prev, whitened, from_next], axis=1)
            first_part = jnp.dot(joined, pick_first, preferred_element_type=jnp.float32)
            second_part = jnp.dot(joined, pick_second, preferred_element_type=jnp.float32)
            term = cross_terms(first_part, second_part)
            cross = term if cross is None else cross + term
        lag_count = length // win_count
        correlation = sum_and_invert(cross, length, lag_count, seg_total, win_count, table)
        capacity = 5 * pair_first.shape[0] // (2 * tile_count)
        chooser = bucket_select(my_owners, tile_count, capacity, order)
        picked = lax.dot_general(
            chooser,
            correlation,
            (((1,), (1,)), ((), ())),
            preferred_element_type=jnp.float32,
        )
        buckets = picked.astype(jnp.bfloat16).reshape(tile_count, capacity, lag_count)
        received = lax.all_to_all(buckets, "tile", split_axis=0, concat_axis=0, tiled=True)
        ordered = jnp.stack([received[d] for d in ring], axis=0)
        return ordered[None]

    return per_device


def solution(mesh):
    placed = (P("win", "tile", None), P("tile"), P("tile"), P("tile", None))
    return jax.shard_map(
        make_per_device(tile_ring(mesh)),
        mesh=mesh,
        in_specs=placed,
        out_specs=P("tile", None, None, "win"),
        check_vma=False,
    )
```
